32 devices in a mesh: sta: 8 (over z, x), tm: 4 (over y, core).
Axes of the slice: x: 2, y: 2, z: 4, core: 2. Of those that a mesh axis runs over, the one named last changes fastest.
Arguments:
- records: float32 [16, 1, 65536], P('sta', None, 'tm'), may hold values from -6 to 6
- pair_blocks: int32 [24, 2], P('sta'), may hold values from 0 to 7, as said below
- pair_count: int32 [8], P('sta'), may hold values from 0 to 3, as said below
Outputs:
- correlations: float32 [24, 2, 2, 2048], P('sta', None, None, 'tm')
The draws below stay inside these ranges and needn't reach their ends.
Inputs may be any that keep to these rules, and one draw needn't show every extreme that they name: `pair_blocks`: slot q belongs to owner o = q // 3. Every slot names blocks a <= b with o <= a and b <= o + 3, both below 8; the slots in use have a < b. `pair_count`: an owner with no higher block within 3 has no slot in use.
All inputs are finite; a program needn't handle non-finite values.
Results may differ from the reference program's by a relative error of at most 0.0003.
Values sent between devices are 32-bit elements; how exact they have to be, the bound alone decides.
No kernel may reach another device: no remote copies, remote signals or barrier semaphores. Data moves between devices by JAX's collectives and lax.ppermute only.
A program may use at most 64 MiB of HBM per device.

```python
import math
import jax
import jax.numpy as jnp
from jax import lax

STA_DEV = 2
HOURS = 1
SAMPLES = 65536
FACTOR_A = 256
BAND = 32
LAGS = 4
REACH = 3
SLOTS = 3
STATIONS = 16
N_STA = 8


def pair_table(key):
    base_key = jax.random.fold_in(key, 7)
    count_key, second_key, first_key = jax.random.split(base_key, 3)
    owner_ids = jnp.arange(N_STA, dtype=jnp.int32)
    slot_ids = jnp.arange(SLOTS, dtype=jnp.int32)
    room = jnp.minimum(REACH, N_STA - 1 - owner_ids)
    counts = jax.random.randint(count_key, (N_STA,), 1, SLOTS + 1)
    counts = jnp.where(owner_ids == 0, SLOTS, counts)
    counts = jnp.where(room > 0, counts, 0).astype(jnp.int32)
    safe_room = jnp.maximum(room, 1)
    raw_second = jax.random.randint(second_key, (N_STA, SLOTS), 0, REACH)
    second_off = 1 + raw_second % safe_room[:, None]
    raw_first = jax.random.randint(first_key, (N_STA, SLOTS), 0, REACH)
    first_off = raw_first % second_off
    first_off = jnp.where((owner_ids[:, None] == 0) & (slot_ids[None, :] == 0), 0, first_off)
    first_off = jnp.where(room[:, None] > 0, first_off, 0)
    second_off = jnp.where(room[:, None] > 0, second_off, 0)
    blocks = jnp.stack([owner_ids[:, None] + first_off, owner_ids[:, None] + second_off], -1)
    return (blocks.reshape(N_STA * SLOTS, 2).astype(jnp.int32), counts)


def draw_pair_blocks(key, part):
    return pair_table(key)[0]


def draw_pair_count(key, part):
    return pair_table(key)[1]


def block_levels(key, extent, shards, smallest, high):
    def one(position, shards_of):
        steps = jax.random.uniform(jax.random.fold_in(jax.random.fold_in(key, 6), position), (shards_of,), jnp.float32, smallest / len(shards), high / len(shards))
        return jnp.repeat(jnp.exp(steps), extent[position] // shards_of).reshape((-1,) + (1,) * (len(extent) - position - 1))

    factor_of = one(*shards[0])
    for cut in shards[1:]:
        factor_of = factor_of * one(*cut)
    return factor_of


def bell_draw(stream_key, dims, deviation, most, cuts=(), held_as=jnp.bfloat16):
    result = deviation * jax.random.normal(stream_key, dims, jnp.float32)
    if cuts:
        result = result * block_levels(stream_key, dims, cuts, -0.22, 0.18)
    return jnp.clip(result, -most, most).astype(held_as)


def setup_inputs(seed: int = 0) -> dict:
    keys = jax.random.split(jax.random.key(seed), 4)
    return {
        "records": bell_draw(keys[0], (STATIONS, HOURS, SAMPLES), 1.0, 6.0, ((0, 8), (2, 4)), jnp.float32),
        "pair_blocks": draw_pair_blocks(jax.random.fold_in(keys[3], 71), 0),
        "pair_count": draw_pair_count(jax.random.fold_in(keys[3], 71), 0),
    }


epsilon = 1e-06

def reference(records, pair_blocks, pair_count):
    length = SAMPLES
    spectra = jnp.fft.fft(records, axis=-1)
    banded = spectra.reshape(spectra.shape[0], spectra.shape[1], length // BAND, BAND)
    band_power = lax.optimization_barrier(jnp.mean(jnp.real(banded) ** 2 + jnp.imag(banded) ** 2, axis=-1, keepdims=True))
    whitened = (banded / jnp.sqrt(band_power + epsilon)).reshape(spectra.shape)
    factor_b = length // FACTOR_A
    lag_rows = jnp.concatenate([jnp.arange(LAGS, dtype=jnp.int32), FACTOR_A - LAGS + jnp.arange(LAGS, dtype=jnp.int32)])
    norm_factor = length / math.sqrt(length * HOURS)

    def one_slot(slot_id):
        owner_id = slot_id // SLOTS
        slot_rank = slot_id % SLOTS
        first_block = pair_blocks[slot_id, 0]
        second_block = pair_blocks[slot_id, 1]
        left_block = lax.dynamic_slice_in_dim(whitened, (first_block * STA_DEV).astype(jnp.int32), STA_DEV, 0)
        right_block = lax.dynamic_slice_in_dim(whitened, (second_block * STA_DEV).astype(jnp.int32), STA_DEV, 0)
        cross_spec = jnp.einsum('ihk,jhk->ijk', left_block, jnp.conj(right_block))
        correlated = jnp.real(jnp.fft.ifft(cross_spec, axis=-1)) * norm_factor
        correlated = correlated.reshape(STA_DEV, STA_DEV, FACTOR_A, factor_b)[:, :, lag_rows, :]
        live_mask = (slot_rank < pair_count[owner_id]).astype(correlated.dtype)
        return (correlated * live_mask).reshape(STA_DEV, STA_DEV, 2 * LAGS * factor_b)
    return lax.map(one_slot, jnp.arange(N_STA * SLOTS, dtype=jnp.int32))
```

```python
import math

import jax
import jax.numpy as jnp
from jax import lax
from jax.sharding import PartitionSpec as P

SAMPLES = 65536
FACTOR_A = 256
BAND = 32
LAGS = 4
REACH = 3


highest = lax.Precision.HIGHEST
epsilon = 1e-06


def passed_along(block, axis, distance):
    devices = range(lax.axis_size(axis))
    route = [(i - distance, i) for i in devices if i - distance in devices]
    return lax.ppermute(block, axis, route)


def angles(row_ids, col_ids, modulus):
    product = row_ids[:, None] * col_ids[None, :] % modulus
    radians = product.astype(jnp.float32) * (2.0 * math.pi / modulus)
    return (jnp.cos(radians), jnp.sin(radians))


def matmul(left_mat, right_mat):
    return jnp.dot(left_mat, right_mat, precision=highest, preferred_element_type=jnp.float32)


def local(records, pair_blocks, pair_count):
    stations, hour_count, time_cols = records.shape
    time_devices = lax.axis_size("tm")
    time_rank = lax.axis_index("tm")
    owner_id = lax.axis_index("sta")
    factor_a = FACTOR_A
    factor_b = SAMPLES // FACTOR_A
    rows_local = factor_a // time_devices
    cols_local = factor_b // time_devices
    series = stations * hour_count
    arranged = records.reshape(series, rows_local, factor_b).transpose(1, 0, 2)
    spread = lax.all_to_all(arranged, "tm", split_axis=2, concat_axis=0, tiled=True)
    index_a = jnp.arange(factor_a, dtype=jnp.int32)
    index_b = jnp.arange(factor_b, dtype=jnp.int32)
    cosine_a, sine_a = angles(index_a, index_a, factor_a)
    flat_rows = spread.reshape(factor_a, series * cols_local)
    both_a = jnp.concatenate([cosine_a, -sine_a], axis=0)
    section = matmul(both_a, flat_rows).reshape(2, factor_a, series, cols_local)
    section_real, section_imag = section[0], section[1]
    col_global = time_rank * cols_local + jnp.arange(cols_local, dtype=jnp.int32)
    cosine_t, sine_t = angles(index_a, col_global, SAMPLES)
    twisted_real = section_real * cosine_t[:, None, :] + section_imag * sine_t[:, None, :]
    twisted_imag = section_imag * cosine_t[:, None, :] - section_real * sine_t[:, None, :]
    twisted = jnp.stack([twisted_real, twisted_imag], axis=2)
    moved = lax.all_to_all(twisted, "tm", split_axis=0, concat_axis=3, tiled=True)
    cosine_b, sine_b = angles(index_b, index_b, factor_b)
    forward_b = jnp.concatenate(
        [jnp.concatenate([cosine_b, -sine_b], axis=1), jnp.concatenate([sine_b, cosine_b], axis=1)],
        axis=0,
    )
    spec = matmul(moved.reshape(rows_local * series, 2 * factor_b), forward_b)
    banded = spec.reshape(rows_local // BAND, BAND, series, 2, factor_b)
    band_power = jnp.mean(
        banded[:, :, :, 0] * banded[:, :, :, 0] + banded[:, :, :, 1] * banded[:, :, :, 1],
        axis=1,
        keepdims=True,
    )
    band_scale = lax.rsqrt(band_power + epsilon)
    whitened = (banded * band_scale[:, :, :, None]).reshape(
        rows_local, stations, hour_count, 2, factor_b
    )
    pieces = [whitened]
    for distance in range(1, REACH + 1):
        pieces.append(passed_along(whitened, "sta", -distance))
    nearby = jnp.stack(pieces)
    slot_total = pair_blocks.shape[0]
    first_off = pair_blocks[:, 0] - owner_id
    second_off = pair_blocks[:, 1] - owner_id
    left_spec = jnp.stack(
        [lax.dynamic_index_in_dim(nearby, first_off[s], 0, keepdims=False) for s in range(slot_total)]
    )
    right_spec = jnp.stack(
        [lax.dynamic_index_in_dim(nearby, second_off[s], 0, keepdims=False) for s in range(slot_total)]
    )
    left_real = left_spec[:, :, :, None, :, 0]
    left_imag = left_spec[:, :, :, None, :, 1]
    right_real = right_spec[:, :, None, :, :, 0]
    right_imag = right_spec[:, :, None, :, :, 1]
    cross_real = jnp.sum(left_real * right_real + left_imag * right_imag, axis=4)
    cross_imag = jnp.sum(left_imag * right_real - left_real * right_imag, axis=4)
    cross = jnp.concatenate([cross_real, cross_imag], axis=-1)
    inverse_b = jnp.concatenate(
        [jnp.concatenate([cosine_b, sine_b], axis=1), jnp.concatenate([-sine_b, cosine_b], axis=1)],
        axis=0,
    )
    lag = matmul(cross.reshape(-1, 2 * factor_b), inverse_b).reshape(
        slot_total, rows_local, stations, stations, 2, factor_b
    )
    lag_real, lag_imag = lag[:, :, :, :, 0], lag[:, :, :, :, 1]
    k1_ids = time_rank * rows_local + jnp.arange(rows_local, dtype=jnp.int32)
    cosine_u, sine_u = angles(k1_ids, index_b, SAMPLES)
    turn_real = lag_real * cosine_u[None, :, None, None, :] - lag_imag * sine_u[None, :, None, None, :]
    turn_imag = lag_real * sine_u[None, :, None, None, :] + lag_imag * cosine_u[None, :, None, None, :]
    lag_ids = jnp.concatenate(
        [jnp.arange(LAGS, dtype=jnp.int32), factor_a - LAGS + jnp.arange(LAGS, dtype=jnp.int32)]
    )
    cosine_l, sine_l = angles(lag_ids, k1_ids, factor_a)
    lag_weights = jnp.concatenate([cosine_l, -sine_l], axis=1).reshape(
        time_devices, 2 * LAGS // time_devices, 2 * rows_local
    )
    turned = jnp.concatenate([turn_real, turn_imag], axis=1)
    scale_out = 1.0 / math.sqrt(SAMPLES * hour_count)
    live_mask = (jnp.arange(slot_total) < pair_count[0]).astype(jnp.float32) * scale_out
    lag_block = jnp.einsum(
        "dwp,spijm->dsijwm",
        lag_weights,
        turned,
        precision=highest,
        preferred_element_type=jnp.float32,
    )
    lag_block = lag_block * live_mask[None, :, None, None, None, None]
    gathered = lax.all_to_all(lag_block, "tm", split_axis=0, concat_axis=0, tiled=True)
    total = jnp.sum(gathered, axis=0)
    return total.reshape(slot_total, stations, stations, 2 * LAGS * factor_b // time_devices)


def solution(mesh):
    placed = (P("sta", None, "tm"), P("sta", None), P("sta"))
    return jax.shard_map(
        local, mesh=mesh, in_specs=placed, out_specs=P("sta", None, None, "tm"), check_vma=False
    )
```

```python
import math

import jax
import numpy as np
import jax.numpy as jnp
from jax import lax
from jax.sharding import PartitionSpec as P

SAMPLES = 65536
FACTOR_A = 256
BAND = 32
LAGS = 4
REACH = 3


highest = lax.Precision.HIGHEST
epsilon = 1e-06


def passed_along(block, axis, distance):
    devices = range(lax.axis_size(axis))
    route = [(i - distance, i) for i in devices if i - distance in devices]
    return lax.ppermute(block, axis, route)


def angles(row_ids, col_ids, modulus):
    product = row_ids[:, None] * col_ids[None, :] % modulus
    radians = product.astype(jnp.float32) * (2.0 * math.pi / modulus)
    return (jnp.cos(radians), jnp.sin(radians))


def matmul(left_mat, right_mat):
    return jnp.dot(left_mat, right_mat, precision=highest, preferred_element_type=jnp.float32)


def local(records, pair_blocks, pair_count):
    stations, hour_count, time_cols = records.shape
    time_devices = lax.axis_size("tm")
    time_rank = lax.axis_index("tm")
    owner_id = lax.axis_index("sta")
    factor_a = FACTOR_A
    factor_b = SAMPLES // FACTOR_A
    rows_local = factor_a // time_devices
    cols_local = factor_b // time_devices
    series = stations * hour_count
    arranged = records.reshape(series, rows_local, factor_b).transpose(1, 0, 2)
    spread = lax.all_to_all(arranged, "tm", split_axis=2, concat_axis=0, tiled=True)
    index_a = jnp.arange(factor_a, dtype=jnp.int32)
    index_b = jnp.arange(factor_b, dtype=jnp.int32)
    paired = rows_local == 2 * BAND and factor_a == 2 * BAND * time_devices
    if paired:
        order = [
            piece
            for t in range(time_devices)
            for piece in (np.arange(BAND) + BAND * t, factor_a - BAND * (t + 1) + np.arange(BAND))
        ]
        k1_order = jnp.asarray(np.concatenate(order).astype(np.int32))
        k1_ids = jnp.concatenate(
            [
                BAND * time_rank + jnp.arange(BAND, dtype=jnp.int32),
                factor_a - BAND * (time_rank + 1) + jnp.arange(BAND, dtype=jnp.int32),
            ]
        )
    else:
        k1_order = index_a
        k1_ids = time_rank * rows_local + jnp.arange(rows_local, dtype=jnp.int32)
    cosine_a, sine_a = angles(k1_order, index_a, factor_a)
    flat_rows = spread.reshape(factor_a, series * cols_local)
    both_a = jnp.concatenate([cosine_a, -sine_a], axis=0)
    section = matmul(both_a, flat_rows).reshape(2, factor_a, series, cols_local)
    section_real, section_imag = section[0], section[1]
    col_global = time_rank * cols_local + jnp.arange(cols_local, dtype=jnp.int32)
    cosine_t, sine_t = angles(k1_order, col_global, SAMPLES)
    twisted_real = section_real * cosine_t[:, None, :] + section_imag * sine_t[:, None, :]
    twisted_imag = section_imag * cosine_t[:, None, :] - section_real * sine_t[:, None, :]
    twisted = jnp.stack([twisted_real, twisted_imag], axis=2)
    moved = lax.all_to_all(twisted, "tm", split_axis=0, concat_axis=3, tiled=True)
    cosine_b, sine_b = angles(index_b, index_b, factor_b)
    forward_b = jnp.concatenate(
        [jnp.concatenate([cosine_b, -sine_b], axis=1), jnp.concatenate([sine_b, cosine_b], axis=1)],
        axis=0,
    )
    spec = matmul(moved.reshape(rows_local * series, 2 * factor_b), forward_b)
    banded = spec.reshape(rows_local // BAND, BAND, series, 2, factor_b)
    band_power = jnp.mean(
        banded[:, :, :, 0] * banded[:, :, :, 0] + banded[:, :, :, 1] * banded[:, :, :, 1],
        axis=1,
        keepdims=True,
    )
    band_scale = lax.rsqrt(band_power + epsilon)
    whitened = (banded * band_scale[:, :, :, None]).reshape(rows_local, series, 2, factor_b)
    if paired:
        scale_row = band_scale[:, 0].transpose(1, 0, 2)[None]
        sent = jnp.concatenate([spec.reshape(rows_local, series, 2, factor_b)[: BAND + 1], scale_row])

        def rebuilt(piece):
            spec_part = piece[: BAND + 1]
            scale_low = piece[BAND + 1, :, 0][None, :, None, :]
            scale_high = piece[BAND + 1, :, 1][None, :, None, :]
            conj_sign = jnp.asarray([1.0, -1.0], jnp.float32)[None, None, :, None]
            mirrored = spec_part[1:BAND][::-1, :, :, ::-1] * conj_sign
            high = jnp.concatenate([spec_part[BAND:], mirrored])
            return jnp.concatenate([spec_part[:BAND] * scale_low, high * scale_high])

    else:
        sent = whitened

        def rebuilt(piece):
            return piece

    pieces = [whitened]
    for distance in range(1, REACH + 1):
        pieces.append(rebuilt(passed_along(sent, "sta", -distance)))
    nearby = jnp.stack(pieces).reshape(REACH + 1, rows_local, stations, hour_count, 2, factor_b)
    slot_total = pair_blocks.shape[0]
    first_off = pair_blocks[:, 0] - owner_id
    second_off = pair_blocks[:, 1] - owner_id
    left_spec = jnp.stack(
        [lax.dynamic_index_in_dim(nearby, first_off[s], 0, keepdims=False) for s in range(slot_total)]
    )
    right_spec = jnp.stack(
        [lax.dynamic_index_in_dim(nearby, second_off[s], 0, keepdims=False) for s in range(slot_total)]
    )
    left_real = left_spec[:, :, :, None, :, 0]
    left_imag = left_spec[:, :, :, None, :, 1]
    right_real = right_spec[:, :, None, :, :, 0]
    right_imag = right_spec[:, :, None, :, :, 1]
    cross_real = jnp.sum(left_real * right_real + left_imag * right_imag, axis=4)
    cross_imag = jnp.sum(left_imag * right_real - left_real * right_imag, axis=4)
    cross = jnp.concatenate([cross_real, cross_imag], axis=-1)
    inverse_b = jnp.concatenate(
        [jnp.concatenate([cosine_b, sine_b], axis=1), jnp.concatenate([-sine_b, cosine_b], axis=1)],
        axis=0,
    )
    lag = matmul(cross.reshape(-1, 2 * factor_b), inverse_b).reshape(
        slot_total, rows_local, stations, stations, 2, factor_b
    )
    lag_real, lag_imag = lag[:, :, :, :, 0], lag[:, :, :, :, 1]
    cosine_u, sine_u = angles(k1_ids, index_b, SAMPLES)
    turn_real = lag_real * cosine_u[None, :, None, None, :] - lag_imag * sine_u[None, :, None, None, :]
    turn_imag = lag_real * sine_u[None, :, None, None, :] + lag_imag * cosine_u[None, :, None, None, :]
    lag_ids = jnp.concatenate(
        [jnp.arange(LAGS, dtype=jnp.int32), factor_a - LAGS + jnp.arange(LAGS, dtype=jnp.int32)]
    )
    cosine_l, sine_l = angles(lag_ids, k1_ids, factor_a)
    lag_weights = jnp.concatenate([cosine_l, -sine_l], axis=1).reshape(
        time_devices, 2 * LAGS // time_devices, 2 * rows_local
    )
    turned = jnp.concatenate([turn_real, turn_imag], axis=1)
    scale_out = 1.0 / math.sqrt(SAMPLES * hour_count)
    live_mask = (jnp.arange(slot_total) < pair_count[0]).astype(jnp.float32) * scale_out
    lag_block = jnp.einsum(
        "dwp,spijm->dsijwm",
        lag_weights,
        turned,
        precision=highest,
        preferred_element_type=jnp.float32,
    )
    lag_block = lag_block * live_mask[None, :, None, None, None, None]
    gathered = lax.all_to_all(lag_block, "tm", split_axis=0, concat_axis=0, tiled=True)
    total = jnp.sum(gathered, axis=0)
    return total.reshape(slot_total, stations, stations, 2 * LAGS * factor_b // time_devices)


def solution(mesh):
    placed = (P("sta", None, "tm"), P("sta", None), P("sta"))
    return jax.shard_map(
        local, mesh=mesh, in_specs=placed, out_specs=P("sta", None, None, "tm"), check_vma=False
    )
```

```python
import math

import jax
import jax.numpy as jnp
from jax import lax
from jax.sharding import PartitionSpec as P

SAMPLES = 65536
FACTOR_A = 256
BAND = 32
LAGS = 4
REACH = 3


highest = lax.Precision.HIGHEST
epsilon = 1e-06


def passed_along(block, axis, distance):
    devices = range(lax.axis_size(axis))
    route = [(i - distance, i) for i in devices if i - distance in devices]
    return lax.ppermute(block, axis, route)


def angles(row_ids, col_ids, modulus):
    product = row_ids[:, None] * col_ids[None, :] % modulus
    radians = product.astype(jnp.float32) * (2.0 * math.pi / modulus)
    return (jnp.cos(radians), jnp.sin(radians))


def matmul(left_mat, right_mat):
    return jnp.dot(left_mat, right_mat, precision=highest, preferred_element_type=jnp.float32)


def local(records, pair_blocks, pair_count):
    stations, hour_count, time_cols = records.shape
    time_devices = lax.axis_size("tm")
    time_rank = lax.axis_index("tm")
    owner_id = lax.axis_index("sta")
    factor_a = FACTOR_A
    factor_b = SAMPLES // FACTOR_A
    rows_local = factor_a // time_devices
    cols_local = factor_b // time_devices
    series = stations * hour_count
    arranged = records.reshape(series, rows_local, factor_b).transpose(1, 0, 2)
    spread = lax.all_to_all(arranged, "tm", split_axis=2, concat_axis=0, tiled=True)
    index_a = jnp.arange(factor_a, dtype=jnp.int32)
    index_b = jnp.arange(factor_b, dtype=jnp.int32)
    paired = rows_local == 2 * BAND and factor_a == 2 * BAND * time_devices
    if paired:
        owner_of_row = index_a // rows_local
        place_in_row = index_a % rows_local
        k1_order = jnp.where(
            place_in_row < BAND,
            BAND * owner_of_row + place_in_row,
            factor_a - BAND * (owner_of_row + 2) + place_in_row,
        )
        k1_ids = jnp.concatenate(
            [
                BAND * time_rank + jnp.arange(BAND, dtype=jnp.int32),
                factor_a - BAND * (time_rank + 1) + jnp.arange(BAND, dtype=jnp.int32),
            ]
        )
    else:
        k1_order = index_a
        k1_ids = time_rank * rows_local + jnp.arange(rows_local, dtype=jnp.int32)
    cosine_a, sine_a = angles(k1_order, index_a, factor_a)
    flat_rows = spread.reshape(factor_a, series * cols_local)
    both_a = jnp.concatenate([cosine_a, -sine_a], axis=0)
    section = matmul(both_a, flat_rows).reshape(2, factor_a, series, cols_local)
    section_real, section_imag = section[0], section[1]
    col_global = time_rank * cols_local + jnp.arange(cols_local, dtype=jnp.int32)
    cosine_t, sine_t = angles(k1_order, col_global, SAMPLES)
    twisted_real = section_real * cosine_t[:, None, :] + section_imag * sine_t[:, None, :]
    twisted_imag = section_imag * cosine_t[:, None, :] - section_real * sine_t[:, None, :]
    twisted = jnp.stack([twisted_real, twisted_imag], axis=2)
    moved = lax.all_to_all(twisted, "tm", split_axis=0, concat_axis=3, tiled=True)
    cosine_b, sine_b = angles(index_b, index_b, factor_b)
    forward_b = jnp.concatenate(
        [jnp.concatenate([cosine_b, -sine_b], axis=1), jnp.concatenate([sine_b, cosine_b], axis=1)],
        axis=0,
    )
    spec = matmul(moved.reshape(rows_local * series, 2 * factor_b), forward_b)
    banded = spec.reshape(rows_local // BAND, BAND, series, 2, factor_b)
    band_power = jnp.mean(
        banded[:, :, :, 0] * banded[:, :, :, 0] + banded[:, :, :, 1] * banded[:, :, :, 1],
        axis=1,
        keepdims=True,
    )
    band_scale = lax.rsqrt(band_power + epsilon)
    whitened = (banded * band_scale[:, :, :, None]).reshape(rows_local, series, 2, factor_b)
    if paired:
        scale_row = band_scale[:, 0].transpose(1, 0, 2)[None]
        sent = jnp.concatenate([spec.reshape(rows_local, series, 2, factor_b)[: BAND + 1], scale_row])

        def rebuilt(piece):
            spec_part = piece[: BAND + 1]
            scale_low = piece[BAND + 1, :, 0][None, :, None, :]
            scale_high = piece[BAND + 1, :, 1][None, :, None, :]
            conj_sign = (1 - 2 * lax.iota(jnp.int32, 2)).astype(jnp.float32)[None, None, :, None]
            mirrored = spec_part[1:BAND][::-1, :, :, ::-1] * conj_sign
            high = jnp.concatenate([spec_part[BAND:], mirrored])
            return jnp.concatenate([spec_part[:BAND] * scale_low, high * scale_high])

    else:
        sent = whitened

        def rebuilt(piece):
            return piece

    pieces = [whitened]
    for distance in range(1, REACH + 1):
        pieces.append(rebuilt(passed_along(sent, "sta", -distance)))
    nearby = jnp.stack(pieces).reshape(REACH + 1, rows_local, stations, hour_count, 2, factor_b)
    slot_total = pair_blocks.shape[0]
    first_off = pair_blocks[:, 0] - owner_id
    second_off = pair_blocks[:, 1] - owner_id
    left_spec = jnp.stack(
        [lax.dynamic_index_in_dim(nearby, first_off[s], 0, keepdims=False) for s in range(slot_total)]
    )
    right_spec = jnp.stack(
        [lax.dynamic_index_in_dim(nearby, second_off[s], 0, keepdims=False) for s in range(slot_total)]
    )
    left_real = left_spec[:, :, :, None, :, 0]
    left_imag = left_spec[:, :, :, None, :, 1]
    right_real = right_spec[:, :, None, :, :, 0]
    right_imag = right_spec[:, :, None, :, :, 1]
    cross_real = jnp.sum(left_real * right_real + left_imag * right_imag, axis=4)
    cross_imag = jnp.sum(left_imag * right_real - left_real * right_imag, axis=4)
    cross = jnp.concatenate([cross_real, cross_imag], axis=-1)
    inverse_b = jnp.concatenate(
        [jnp.concatenate([cosine_b, sine_b], axis=1), jnp.concatenate([-sine_b, cosine_b], axis=1)],
        axis=0,
    )
    lag = matmul(cross.reshape(-1, 2 * factor_b), inverse_b).reshape(
        slot_total, rows_local, stations, stations, 2, factor_b
    )
    lag_real, lag_imag = lag[:, :, :, :, 0], lag[:, :, :, :, 1]
    cosine_u, sine_u = angles(k1_ids, index_b, SAMPLES)
    turn_real = lag_real * cosine_u[None, :, None, None, :] - lag_imag * sine_u[None, :, None, None, :]
    turn_imag = lag_real * sine_u[None, :, None, None, :] + lag_imag * cosine_u[None, :, None, None, :]
    lag_ids = jnp.concatenate(
        [jnp.arange(LAGS, dtype=jnp.int32), factor_a - LAGS + jnp.arange(LAGS, dtype=jnp.int32)]
    )
    cosine_l, sine_l = angles(lag_ids, k1_ids, factor_a)
    lag_weights = jnp.concatenate([cosine_l, -sine_l], axis=1).reshape(
        time_devices, 2 * LAGS // time_devices, 2 * rows_local
    )
    turned = jnp.concatenate([turn_real, turn_imag], axis=1)
    scale_out = 1.0 / math.sqrt(SAMPLES * hour_count)
    live_mask = (jnp.arange(slot_total) < pair_count[0]).astype(jnp.float32) * scale_out
    lag_block = jnp.einsum(
        "dwp,spijm->dsijwm",
        lag_weights,
        turned,
        precision=highest,
        preferred_element_type=jnp.float32,
    )
    lag_block = lag_block * live_mask[None, :, None, None, None, None]
    gathered = lax.all_to_all(lag_block, "tm", split_axis=0, concat_axis=0, tiled=True)
    total = jnp.sum(gathered, axis=0)
    return total.reshape(slot_total, stations, stations, 2 * LAGS * factor_b // time_devices)


def solution(mesh):
    placed = (P("sta", None, "tm"), P("sta", None), P("sta"))
    return jax.shard_map(
        local, mesh=mesh, in_specs=placed, out_specs=P("sta", None, None, "tm"), check_vma=False
    )
```

```python
import math

import jax
import jax.numpy as jnp
from jax import lax
from jax.sharding import PartitionSpec as P

SAMPLES = 65536
FACTOR_A = 256
BAND = 32
LAGS = 4
REACH = 3


highest = lax.Precision.HIGHEST
epsilon = 1e-06


def passed_along(block, axis, distance):
    devices = range(lax.axis_size(axis))
    route = [(i - distance, i) for i in devices if i - distance in devices]
    return lax.ppermute(block, axis, route)


def angles(row_ids, col_ids, modulus):
    product = row_ids[:, None] * col_ids[None, :] % modulus
    radians = product.astype(jnp.float32) * (2.0 * math.pi / modulus)
    return (jnp.cos(radians), jnp.sin(radians))


def matmul(left_mat, right_mat):
    return jnp.dot(left_mat, right_mat, precision=highest, preferred_element_type=jnp.float32)


def local(records, pair_blocks, pair_count):
    stations, hour_count, time_cols = records.shape
    time_devices = lax.axis_size("tm")
    time_rank = lax.axis_index("tm")
    owner_id = lax.axis_index("sta")
    factor_a = FACTOR_A
    factor_b = SAMPLES // FACTOR_A
    rows_local = factor_a // time_devices
    cols_local = factor_b // time_devices
    series = stations * hour_count
    arranged = records.reshape(series, rows_local, factor_b).transpose(1, 0, 2)
    spread = lax.all_to_all(arranged, "tm", split_axis=2, concat_axis=0, tiled=True)
    index_a = jnp.arange(factor_a, dtype=jnp.int32)
    index_b = jnp.arange(factor_b, dtype=jnp.int32)
    paired = rows_local == 2 * BAND and factor_a == 2 * BAND * time_devices
    if paired:
        k1_ids = jnp.concatenate(
            [
                BAND * time_rank + jnp.arange(BAND, dtype=jnp.int32),
                factor_a - BAND * (time_rank + 1) + jnp.arange(BAND, dtype=jnp.int32),
            ]
        )
    else:
        k1_ids = time_rank * rows_local + jnp.arange(rows_local, dtype=jnp.int32)
    cosine_a, sine_a = angles(index_a, index_a, factor_a)
    flat_rows = spread.reshape(factor_a, series * cols_local)
    both_a = jnp.concatenate([cosine_a, -sine_a], axis=0)
    section = matmul(both_a, flat_rows).reshape(2, factor_a, series, cols_local)
    section_real, section_imag = section[0], section[1]
    col_global = time_rank * cols_local + jnp.arange(cols_local, dtype=jnp.int32)
    cosine_t, sine_t = angles(index_a, col_global, SAMPLES)
    twisted_real = section_real * cosine_t[:, None, :] + section_imag * sine_t[:, None, :]
    twisted_imag = section_imag * cosine_t[:, None, :] - section_real * sine_t[:, None, :]
    twisted = jnp.stack([twisted_real, twisted_imag], axis=2)
    if paired:
        bands = twisted.reshape(2, time_devices, BAND, series, 2, cols_local)
        twisted = jnp.stack([bands[0], bands[1][::-1]], axis=1).reshape(twisted.shape)
    moved = lax.all_to_all(twisted, "tm", split_axis=0, concat_axis=3, tiled=True)
    cosine_b, sine_b = angles(index_b, index_b, factor_b)
    forward_b = jnp.concatenate(
        [jnp.concatenate([cosine_b, -sine_b], axis=1), jnp.concatenate([sine_b, cosine_b], axis=1)],
        axis=0,
    )
    spec = matmul(moved.reshape(rows_local * series, 2 * factor_b), forward_b)
    banded = spec.reshape(rows_local // BAND, BAND, series, 2, factor_b)
    band_power = jnp.mean(
        banded[:, :, :, 0] * banded[:, :, :, 0] + banded[:, :, :, 1] * banded[:, :, :, 1],
        axis=1,
        keepdims=True,
    )
    band_scale = lax.rsqrt(band_power + epsilon)
    whitened = (banded * band_scale[:, :, :, None]).reshape(rows_local, series, 2, factor_b)
    if paired:
        scale_row = band_scale[:, 0].transpose(1, 0, 2)[None]
        sent = jnp.concatenate([spec.reshape(rows_local, series, 2, factor_b)[: BAND + 1], scale_row])

        def rebuilt(piece):
            spec_part = piece[: BAND + 1]
            scale_low = piece[BAND + 1, :, 0][None, :, None, :]
            scale_high = piece[BAND + 1, :, 1][None, :, None, :]
            conj_sign = (1 - 2 * lax.iota(jnp.int32, 2)).astype(jnp.float32)[None, None, :, None]
            mirrored = spec_part[1:BAND][::-1, :, :, ::-1] * conj_sign
            high = jnp.concatenate([spec_part[BAND:], mirrored])
            return jnp.concatenate([spec_part[:BAND] * scale_low, high * scale_high])

    else:
        sent = whitened

        def rebuilt(piece):
            return piece

    pieces = [whitened]
    for distance in range(1, REACH + 1):
        pieces.append(rebuilt(passed_along(sent, "sta", -distance)))
    nearby = jnp.stack(pieces).reshape(REACH + 1, rows_local, stations, hour_count, 2, factor_b)
    slot_total = pair_blocks.shape[0]
    first_off = pair_blocks[:, 0] - owner_id
    second_off = pair_blocks[:, 1] - owner_id
    left_spec = jnp.stack(
        [lax.dynamic_index_in_dim(nearby, first_off[s], 0, keepdims=False) for s in range(slot_total)]
    )
    right_spec = jnp.stack(
        [lax.dynamic_index_in_dim(nearby, second_off[s], 0, keepdims=False) for s in range(slot_total)]
    )
    left_real = left_spec[:, :, :, None, :, 0]
    left_imag = left_spec[:, :, :, None, :, 1]
    right_real = right_spec[:, :, None, :, :, 0]
    right_imag = right_spec[:, :, None, :, :, 1]
    cross_real = jnp.sum(left_real * right_real + left_imag * right_imag, axis=4)
    cross_imag = jnp.sum(left_imag * right_real - left_real * right_imag, axis=4)
    cross = jnp.concatenate([cross_real, cross_imag], axis=-1)
    inverse_b = jnp.concatenate(
        [jnp.concatenate([cosine_b, sine_b], axis=1), jnp.concatenate([-sine_b, cosine_b], axis=1)],
        axis=0,
    )
    lag = matmul(cross.reshape(-1, 2 * factor_b), inverse_b).reshape(
        slot_total, rows_local, stations, stations, 2, factor_b
    )
    lag_real, lag_imag = lag[:, :, :, :, 0], lag[:, :, :, :, 1]
    cosine_u, sine_u = angles(k1_ids, index_b, SAMPLES)
    turn_real = lag_real * cosine_u[None, :, None, None, :] - lag_imag * sine_u[None, :, None, None, :]
    turn_imag = lag_real * sine_u[None, :, None, None, :] + lag_imag * cosine_u[None, :, None, None, :]
    lag_ids = jnp.concatenate(
        [jnp.arange(LAGS, dtype=jnp.int32), factor_a - LAGS + jnp.arange(LAGS, dtype=jnp.int32)]
    )
    cosine_l, sine_l = angles(lag_ids, k1_ids, factor_a)
    lag_weights = jnp.concatenate([cosine_l, -sine_l], axis=1).reshape(
        time_devices, 2 * LAGS // time_devices, 2 * rows_local
    )
    turned = jnp.concatenate([turn_real, turn_imag], axis=1)
    scale_out = 1.0 / math.sqrt(SAMPLES * hour_count)
    live_mask = (jnp.arange(slot_total) < pair_count[0]).astype(jnp.float32) * scale_out
    lag_block = jnp.einsum(
        "dwp,spijm->dsijwm",
        lag_weights,
        turned,
        precision=highest,
        preferred_element_type=jnp.float32,
    )
    lag_block = lag_block * live_mask[None, :, None, None, None, None]
    gathered = lax.all_to_all(lag_block, "tm", split_axis=0, concat_axis=0, tiled=True)
    total = jnp.sum(gathered, axis=0)
    return total.reshape(slot_total, stations, stations, 2 * LAGS * factor_b // time_devices)


def solution(mesh):
    placed = (P("sta", None, "tm"), P("sta", None), P("sta"))
    return jax.shard_map(
        local, mesh=mesh, in_specs=placed, out_specs=P("sta", None, None, "tm"), check_vma=False
    )
```

```python
import math

import jax
import jax.numpy as jnp
from jax import lax
from jax.sharding import PartitionSpec as P

SAMPLES = 65536
FACTOR_A = 256
BAND = 32
LAGS = 4
REACH = 3


highest = lax.Precision.HIGHEST
epsilon = 1e-06


def passed_along(block, axis, distance):
    devices = range(lax.axis_size(axis))
    route = [(i - distance, i) for i in devices if i - distance in devices]
    return lax.ppermute(block, axis, route)


def angles(row_ids, col_ids, modulus):
    product = row_ids[:, None] * col_ids[None, :] % modulus
    radians = product.astype(jnp.float32) * (2.0 * math.pi / modulus)
    return (jnp.cos(radians), jnp.sin(radians))


def matmul(left_mat, right_mat):
    return jnp.dot(left_mat, right_mat, precision=highest, preferred_element_type=jnp.float32)


def local(records, pair_blocks, pair_count):
    stations, hour_count, time_cols = records.shape
    time_devices = lax.axis_size("tm")
    time_rank = lax.axis_index("tm")
    owner_id = lax.axis_index("sta")
    factor_a = FACTOR_A
    factor_b = SAMPLES // FACTOR_A
    rows_local = factor_a // time_devices
    cols_local = factor_b // time_devices
    series = stations * hour_count
    arranged = records.reshape(series, rows_local, factor_b).transpose(1, 0, 2)
    spread = lax.all_to_all(arranged, "tm", split_axis=2, concat_axis=0, tiled=True)
    index_a = jnp.arange(factor_a, dtype=jnp.int32)
    index_b = jnp.arange(factor_b, dtype=jnp.int32)
    paired = rows_local == 2 * BAND and factor_a == 2 * BAND * time_devices
    if paired:
        k1_ids = jnp.concatenate(
            [
                BAND * time_rank + jnp.arange(BAND, dtype=jnp.int32),
                factor_a - BAND * (time_rank + 1) + jnp.arange(BAND, dtype=jnp.int32),
            ]
        )
    else:
        k1_ids = time_rank * rows_local + jnp.arange(rows_local, dtype=jnp.int32)
    cosine_a, sine_a = angles(index_a, index_a, factor_a)
    flat_rows = spread.reshape(factor_a, series * cols_local)
    both_a = jnp.concatenate([cosine_a, -sine_a], axis=0)
    section = matmul(both_a, flat_rows).reshape(2, factor_a, series, cols_local)
    section_real, section_imag = section[0], section[1]
    col_global = time_rank * cols_local + jnp.arange(cols_local, dtype=jnp.int32)
    cosine_t, sine_t = angles(index_a, col_global, SAMPLES)
    twisted_real = section_real * cosine_t[:, None, :] + section_imag * sine_t[:, None, :]
    twisted_imag = section_imag * cosine_t[:, None, :] - section_real * sine_t[:, None, :]
    twisted = jnp.stack([twisted_real, twisted_imag], axis=2)
    if paired:
        bands = twisted.reshape(2, time_devices, BAND, series, 2, cols_local)
        twisted = jnp.stack([bands[0], bands[1][::-1]], axis=1).reshape(twisted.shape)
    moved = lax.all_to_all(twisted, "tm", split_axis=0, concat_axis=3, tiled=True)
    cosine_b, sine_b = angles(index_b, index_b, factor_b)
    forward_b = jnp.concatenate(
        [jnp.concatenate([cosine_b, -sine_b], axis=1), jnp.concatenate([sine_b, cosine_b], axis=1)],
        axis=0,
    )
    spec = matmul(moved.reshape(rows_local * series, 2 * factor_b), forward_b)
    banded = spec.reshape(rows_local // BAND, BAND, series, 2, factor_b)
    band_power = jnp.mean(
        banded[:, :, :, 0] * banded[:, :, :, 0] + banded[:, :, :, 1] * banded[:, :, :, 1],
        axis=1,
        keepdims=True,
    )
    band_scale = lax.rsqrt(band_power + epsilon)
    whitened = (banded * band_scale[:, :, :, None]).reshape(rows_local, series, 2, factor_b)
    if paired:
        scale_row = band_scale[:, 0].transpose(1, 0, 2)[None]
        sent = jnp.concatenate([spec.reshape(rows_local, series, 2, factor_b)[: BAND + 1], scale_row])

        def rebuilt(piece):
            spec_part = piece[:, : BAND + 1]
            scale_low = piece[:, BAND + 1, :, 0][:, None, :, None, :]
            scale_high = piece[:, BAND + 1, :, 1][:, None, :, None, :]
            conj_sign = (1 - 2 * lax.iota(jnp.int32, 2)).astype(jnp.float32)[None, None, None, :, None]
            mirrored = spec_part[:, 1:BAND][:, ::-1, :, :, ::-1] * conj_sign
            high = jnp.concatenate([spec_part[:, BAND:], mirrored], axis=1)
            return jnp.concatenate([spec_part[:, :BAND] * scale_low, high * scale_high], axis=1)

    else:
        sent = whitened

        def rebuilt(piece):
            return piece

    received = jnp.stack([passed_along(sent, "sta", -distance) for distance in range(1, REACH + 1)])
    nearby = jnp.concatenate([whitened[None], rebuilt(received)]).reshape(REACH + 1, rows_local, stations, hour_count, 2, factor_b)
    slot_total = pair_blocks.shape[0]
    first_off = pair_blocks[:, 0] - owner_id
    second_off = pair_blocks[:, 1] - owner_id
    def chosen(offsets):
        pick = offsets.reshape((slot_total,) + (1,) * (nearby.ndim - 1))
        result = jnp.broadcast_to(nearby[REACH], (slot_total,) + nearby.shape[1:])
        for distance in range(REACH - 1, -1, -1):
            result = jnp.where(pick == distance, nearby[distance], result)
        return result

    left_spec = chosen(first_off)
    right_spec = chosen(second_off)
    left_real = left_spec[:, :, :, None, :, 0]
    left_imag = left_spec[:, :, :, None, :, 1]
    right_real = right_spec[:, :, None, :, :, 0]
    right_imag = right_spec[:, :, None, :, :, 1]
    cross_real = jnp.sum(left_real * right_real + left_imag * right_imag, axis=4)
    cross_imag = jnp.sum(left_imag * right_real - left_real * right_imag, axis=4)
    cross = jnp.concatenate([cross_real, cross_imag], axis=-1)
    inverse_b = jnp.concatenate(
        [jnp.concatenate([cosine_b, sine_b], axis=1), jnp.concatenate([-sine_b, cosine_b], axis=1)],
        axis=0,
    )
    lag = matmul(cross.reshape(-1, 2 * factor_b), inverse_b).reshape(
        slot_total, rows_local, stations, stations, 2, factor_b
    )
    lag_real, lag_imag = lag[:, :, :, :, 0], lag[:, :, :, :, 1]
    cosine_u, sine_u = angles(k1_ids, index_b, SAMPLES)
    turn_real = lag_real * cosine_u[None, :, None, None, :] - lag_imag * sine_u[None, :, None, None, :]
    turn_imag = lag_real * sine_u[None, :, None, None, :] + lag_imag * cosine_u[None, :, None, None, :]
    lag_ids = jnp.concatenate(
        [jnp.arange(LAGS, dtype=jnp.int32), factor_a - LAGS + jnp.arange(LAGS, dtype=jnp.int32)]
    )
    cosine_l, sine_l = angles(lag_ids, k1_ids, factor_a)
    lag_weights = jnp.concatenate([cosine_l, -sine_l], axis=1).reshape(
        time_devices, 2 * LAGS // time_devices, 2 * rows_local
    )
    turned = jnp.concatenate([turn_real, turn_imag], axis=1)
    scale_out = 1.0 / math.sqrt(SAMPLES * hour_count)
    live_mask = (jnp.arange(slot_total) < pair_count).astype(jnp.float32) * scale_out
    lag_block = jnp.einsum(
        "dwp,spijm->dsijwm",
        lag_weights,
        turned,
        precision=highest,
        preferred_element_type=jnp.float32,
    )
    lag_block = lag_block * live_mask[None, :, None, None, None, None]
    gathered = lax.all_to_all(lag_block, "tm", split_axis=0, concat_axis=0, tiled=True)
    total = jnp.sum(gathered, axis=0)
    return total.reshape(slot_total, stations, stations, 2 * LAGS * factor_b // time_devices)


def solution(mesh):
    placed = (P("sta", None, "tm"), P("sta", None), P("sta"))
    return jax.shard_map(
        local, mesh=mesh, in_specs=placed, out_specs=P("sta", None, None, "tm"), check_vma=False
    )
```

```python
import math

import jax
import jax.numpy as jnp
from jax import lax
from jax.sharding import PartitionSpec as P

SAMPLES = 65536
FACTOR_A = 256
BAND = 32
LAGS = 4
REACH = 3


highest = lax.Precision.HIGHEST
epsilon = 1e-06


def passed_along(block, axis, distance):
    devices = range(lax.axis_size(axis))
    route = [(i - distance, i) for i in devices if i - distance in devices]
    return lax.ppermute(block, axis, route)


def angles(row_ids, col_ids, modulus):
    product = row_ids[:, None] * col_ids[None, :] % modulus
    radians = product.astype(jnp.float32) * (2.0 * math.pi / modulus)
    return (jnp.cos(radians), jnp.sin(radians))


def matmul(left_mat, right_mat):
    return jnp.dot(left_mat, right_mat, precision=highest, preferred_element_type=jnp.float32)


def local(records, pair_blocks, pair_count):
    stations, hour_count, time_cols = records.shape
    time_devices = lax.axis_size("tm")
    time_rank = lax.axis_index("tm")
    owner_id = lax.axis_index("sta")
    factor_a = FACTOR_A
    factor_b = SAMPLES // FACTOR_A
    rows_local = factor_a // time_devices
    cols_local = factor_b // time_devices
    series = stations * hour_count
    arranged = records.reshape(series, rows_local, factor_b).transpose(1, 0, 2)
    spread = lax.all_to_all(arranged, "tm", split_axis=2, concat_axis=0, tiled=True)
    index_a = jnp.arange(factor_a, dtype=jnp.int32)
    index_b = jnp.arange(factor_b, dtype=jnp.int32)
    paired = rows_local == 2 * BAND and factor_a == 2 * BAND * time_devices
    if paired:
        k1_ids = jnp.concatenate(
            [
                BAND * time_rank + jnp.arange(BAND, dtype=jnp.int32),
                factor_a - BAND * (time_rank + 1) + jnp.arange(BAND, dtype=jnp.int32),
            ]
        )
    else:
        k1_ids = time_rank * rows_local + jnp.arange(rows_local, dtype=jnp.int32)
    cosine_a, sine_a = angles(index_a, index_a, factor_a)
    flat_rows = spread.reshape(factor_a, series * cols_local)
    both_a = jnp.concatenate([cosine_a, -sine_a], axis=0)
    section = matmul(both_a, flat_rows).reshape(2, factor_a, series, cols_local)
    section_real, section_imag = section[0], section[1]
    col_global = time_rank * cols_local + jnp.arange(cols_local, dtype=jnp.int32)
    cosine_t, sine_t = angles(index_a, col_global, SAMPLES)
    twisted_real = section_real * cosine_t[:, None, :] + section_imag * sine_t[:, None, :]
    twisted_imag = section_imag * cosine_t[:, None, :] - section_real * sine_t[:, None, :]
    twisted = jnp.stack([twisted_real, twisted_imag], axis=2)
    if paired:
        bands = twisted.reshape(2, time_devices, BAND, series, 2, cols_local)
        grouped = jnp.stack([bands[0], bands[1][::-1]], axis=1)
        outgoing = grouped.reshape(time_devices, rows_local, series, 2, cols_local)[:, : BAND + 1]
        incoming = lax.all_to_all(outgoing, "tm", split_axis=0, concat_axis=4, tiled=True).reshape(
            BAND + 1, series, 2, factor_b
        )
        phase_cos, phase_sin = angles(jnp.ones((1,), jnp.int32), index_b, factor_b)
        source = incoming[1:BAND][::-1]
        source_real, source_imag = source[:, :, 0], source[:, :, 1]
        mirror = jnp.stack(
            [
                source_real * phase_cos - source_imag * phase_sin,
                -(source_real * phase_sin + source_imag * phase_cos),
            ],
            axis=2,
        )
        moved = jnp.concatenate([incoming, mirror])
    else:
        moved = lax.all_to_all(twisted, "tm", split_axis=0, concat_axis=3, tiled=True)
    cosine_b, sine_b = angles(index_b, index_b, factor_b)
    forward_b = jnp.concatenate(
        [jnp.concatenate([cosine_b, -sine_b], axis=1), jnp.concatenate([sine_b, cosine_b], axis=1)],
        axis=0,
    )
    spec = matmul(moved.reshape(rows_local * series, 2 * factor_b), forward_b)
    banded = spec.reshape(rows_local // BAND, BAND, series, 2, factor_b)
    band_power = jnp.mean(
        banded[:, :, :, 0] * banded[:, :, :, 0] + banded[:, :, :, 1] * banded[:, :, :, 1],
        axis=1,
        keepdims=True,
    )
    band_scale = lax.rsqrt(band_power + epsilon)
    whitened = (banded * band_scale[:, :, :, None]).reshape(rows_local, series, 2, factor_b)
    if paired:
        scale_row = band_scale[:, 0].transpose(1, 0, 2)[None]
        sent = jnp.concatenate([spec.reshape(rows_local, series, 2, factor_b)[: BAND + 1], scale_row])

        def rebuilt(piece):
            spec_part = piece[:, : BAND + 1]
            scale_low = piece[:, BAND + 1, :, 0][:, None, :, None, :]
            scale_high = piece[:, BAND + 1, :, 1][:, None, :, None, :]
            conj_sign = (1 - 2 * lax.iota(jnp.int32, 2)).astype(jnp.float32)[None, None, None, :, None]
            mirrored = spec_part[:, 1:BAND][:, ::-1, :, :, ::-1] * conj_sign
            high = jnp.concatenate([spec_part[:, BAND:], mirrored], axis=1)
            return jnp.concatenate([spec_part[:, :BAND] * scale_low, high * scale_high], axis=1)

    else:
        sent = whitened

        def rebuilt(piece):
            return piece

    received = jnp.stack([passed_along(sent, "sta", -distance) for distance in range(1, REACH + 1)])
    nearby = jnp.concatenate([whitened[None], rebuilt(received)]).reshape(REACH + 1, rows_local, stations, hour_count, 2, factor_b)
    slot_total = pair_blocks.shape[0]
    first_off = pair_blocks[:, 0] - owner_id
    second_off = pair_blocks[:, 1] - owner_id
    def chosen(offsets):
        pick = offsets.reshape((slot_total,) + (1,) * (nearby.ndim - 1))
        result = jnp.broadcast_to(nearby[REACH], (slot_total,) + nearby.shape[1:])
        for distance in range(REACH - 1, -1, -1):
            result = jnp.where(pick == distance, nearby[distance], result)
        return result

    left_spec = chosen(first_off)
    right_spec = chosen(second_off)
    left_real = left_spec[:, :, :, None, :, 0]
    left_imag = left_spec[:, :, :, None, :, 1]
    right_real = right_spec[:, :, None, :, :, 0]
    right_imag = right_spec[:, :, None, :, :, 1]
    cross_real = jnp.sum(left_real * right_real + left_imag * right_imag, axis=4)
    cross_imag = jnp.sum(left_imag * right_real - left_real * right_imag, axis=4)
    cross = jnp.concatenate([cross_real, cross_imag], axis=-1)
    inverse_b = jnp.concatenate(
        [jnp.concatenate([cosine_b, sine_b], axis=1), jnp.concatenate([-sine_b, cosine_b], axis=1)],
        axis=0,
    )
    lag = matmul(cross.reshape(-1, 2 * factor_b), inverse_b).reshape(
        slot_total, rows_local, stations, stations, 2, factor_b
    )
    lag_real, lag_imag = lag[:, :, :, :, 0], lag[:, :, :, :, 1]
    cosine_u, sine_u = angles(k1_ids, index_b, SAMPLES)
    turn_real = lag_real * cosine_u[None, :, None, None, :] - lag_imag * sine_u[None, :, None, None, :]
    turn_imag = lag_real * sine_u[None, :, None, None, :] + lag_imag * cosine_u[None, :, None, None, :]
    lag_ids = jnp.concatenate(
        [jnp.arange(LAGS, dtype=jnp.int32), factor_a - LAGS + jnp.arange(LAGS, dtype=jnp.int32)]
    )
    cosine_l, sine_l = angles(lag_ids, k1_ids, factor_a)
    lag_weights = jnp.concatenate([cosine_l, -sine_l], axis=1).reshape(
        time_devices, 2 * LAGS // time_devices, 2 * rows_local
    )
    turned = jnp.concatenate([turn_real, turn_imag], axis=1)
    scale_out = 1.0 / math.sqrt(SAMPLES * hour_count)
    live_mask = (jnp.arange(slot_total) < pair_count).astype(jnp.float32) * scale_out
    lag_block = jnp.einsum(
        "dwp,spijm->dsijwm",
        lag_weights,
        turned,
        precision=highest,
        preferred_element_type=jnp.float32,
    )
    lag_block = lag_block * live_mask[None, :, None, None, None, None]
    gathered = lax.all_to_all(lag_block, "tm", split_axis=0, concat_axis=0, tiled=True)
    total = jnp.sum(gathered, axis=0)
    return total.reshape(slot_total, stations, stations, 2 * LAGS * factor_b // time_devices)


def solution(mesh):
    placed = (P("sta", None, "tm"), P("sta", None), P("sta"))
    return jax.shard_map(
        local, mesh=mesh, in_specs=placed, out_specs=P("sta", None, None, "tm"), check_vma=False
    )
```

```python
import math

import jax
import jax.numpy as jnp
from jax import lax
from jax.sharding import PartitionSpec as P

SAMPLES = 65536
FACTOR_A = 256
BAND = 32
LAGS = 4
REACH = 3


highest = lax.Precision.HIGH
epsilon = 1e-06


def passed_along(block, axis, distance):
    devices = range(lax.axis_size(axis))
    route = [(i - distance, i) for i in devices if i - distance in devices]
    return lax.ppermute(block, axis, route)


def angles(row_ids, col_ids, modulus):
    product = row_ids[:, None] * col_ids[None, :] % modulus
    radians = product.astype(jnp.float32) * (2.0 * math.pi / modulus)
    return (jnp.cos(radians), jnp.sin(radians))


def matmul(left_mat, right_mat):
    return jnp.dot(left_mat, right_mat, precision=highest, preferred_element_type=jnp.float32)


def local(records, pair_blocks, pair_count):
    stations, hour_count, time_cols = records.shape
    time_devices = lax.axis_size("tm")
    time_rank = lax.axis_index("tm")
    owner_id = lax.axis_index("sta")
    factor_a = FACTOR_A
    factor_b = SAMPLES // FACTOR_A
    rows_local = factor_a // time_devices
    cols_local = factor_b // time_devices
    series = stations * hour_count
    arranged = records.reshape(series, rows_local, factor_b).transpose(1, 0, 2)
    spread = lax.all_to_all(arranged, "tm", split_axis=2, concat_axis=0, tiled=True)
    index_a = jnp.arange(factor_a, dtype=jnp.int32)
    index_b = jnp.arange(factor_b, dtype=jnp.int32)
    paired = rows_local == 2 * BAND and factor_a == 2 * BAND * time_devices
    if paired:
        k1_ids = jnp.concatenate(
            [
                BAND * time_rank + jnp.arange(BAND, dtype=jnp.int32),
                factor_a - BAND * (time_rank + 1) + jnp.arange(BAND, dtype=jnp.int32),
            ]
        )
    else:
        k1_ids = time_rank * rows_local + jnp.arange(rows_local, dtype=jnp.int32)
    cosine_a, sine_a = angles(index_a, index_a, factor_a)
    flat_rows = spread.reshape(factor_a, series * cols_local)
    both_a = jnp.concatenate([cosine_a, -sine_a], axis=0)
    section = matmul(both_a, flat_rows).reshape(2, factor_a, series, cols_local)
    section_real, section_imag = section[0], section[1]
    col_global = time_rank * cols_local + jnp.arange(cols_local, dtype=jnp.int32)
    cosine_t, sine_t = angles(index_a, col_global, SAMPLES)
    twisted_real = section_real * cosine_t[:, None, :] + section_imag * sine_t[:, None, :]
    twisted_imag = section_imag * cosine_t[:, None, :] - section_real * sine_t[:, None, :]
    twisted = jnp.stack([twisted_real, twisted_imag], axis=2)
    if paired:
        bands = twisted.reshape(2, time_devices, BAND, series, 2, cols_local)
        grouped = jnp.stack([bands[0], bands[1][::-1]], axis=1)
        outgoing = grouped.reshape(time_devices, rows_local, series, 2, cols_local)[:, : BAND + 1]
        incoming = lax.all_to_all(outgoing, "tm", split_axis=0, concat_axis=4, tiled=True).reshape(
            BAND + 1, series, 2, factor_b
        )
        phase_cos, phase_sin = angles(jnp.ones((1,), jnp.int32), index_b, factor_b)
        source = incoming[1:BAND][::-1]
        source_real, source_imag = source[:, :, 0], source[:, :, 1]
        mirror = jnp.stack(
            [
                source_real * phase_cos - source_imag * phase_sin,
                -(source_real * phase_sin + source_imag * phase_cos),
            ],
            axis=2,
        )
        moved = jnp.concatenate([incoming, mirror])
    else:
        moved = lax.all_to_all(twisted, "tm", split_axis=0, concat_axis=3, tiled=True)
    cosine_b, sine_b = angles(index_b, index_b, factor_b)
    forward_b = jnp.concatenate(
        [jnp.concatenate([cosine_b, -sine_b], axis=1), jnp.concatenate([sine_b, cosine_b], axis=1)],
        axis=0,
    )
    spec = matmul(moved.reshape(rows_local * series, 2 * factor_b), forward_b)
    banded = spec.reshape(rows_local // BAND, BAND, series, 2, factor_b)
    band_power = jnp.mean(
        banded[:, :, :, 0] * banded[:, :, :, 0] + banded[:, :, :, 1] * banded[:, :, :, 1],
        axis=1,
        keepdims=True,
    )
    band_scale = lax.rsqrt(band_power + epsilon)
    whitened = (banded * band_scale[:, :, :, None]).reshape(rows_local, series, 2, factor_b)
    if paired:
        scale_row = band_scale[:, 0].transpose(1, 0, 2)[None]
        sent = jnp.concatenate([spec.reshape(rows_local, series, 2, factor_b)[: BAND + 1], scale_row])

        def rebuilt(piece):
            spec_part = piece[:, : BAND + 1]
            scale_low = piece[:, BAND + 1, :, 0][:, None, :, None, :]
            scale_high = piece[:, BAND + 1, :, 1][:, None, :, None, :]
            conj_sign = (1 - 2 * lax.iota(jnp.int32, 2)).astype(jnp.float32)[None, None, None, :, None]
            mirrored = spec_part[:, 1:BAND][:, ::-1, :, :, ::-1] * conj_sign
            high = jnp.concatenate([spec_part[:, BAND:], mirrored], axis=1)
            return jnp.concatenate([spec_part[:, :BAND] * scale_low, high * scale_high], axis=1)

    else:
        sent = whitened

        def rebuilt(piece):
            return piece

    received = [rebuilt(passed_along(sent, "sta", -distance)[None]) for distance in range(1, REACH + 1)]
    nearby = jnp.concatenate([whitened[None]] + received).reshape(REACH + 1, rows_local, stations, hour_count, 2, factor_b)
    slot_total = pair_blocks.shape[0]
    first_off = pair_blocks[:, 0] - owner_id
    second_off = pair_blocks[:, 1] - owner_id
    def chosen(offsets):
        pick = offsets.reshape((slot_total,) + (1,) * (nearby.ndim - 1))
        result = jnp.broadcast_to(nearby[REACH], (slot_total,) + nearby.shape[1:])
        for distance in range(REACH - 1, -1, -1):
            result = jnp.where(pick == distance, nearby[distance], result)
        return result

    left_spec = chosen(first_off)
    right_spec = chosen(second_off)
    left_real = left_spec[:, :, :, None, :, 0]
    left_imag = left_spec[:, :, :, None, :, 1]
    right_real = right_spec[:, :, None, :, :, 0]
    right_imag = right_spec[:, :, None, :, :, 1]
    cross_real = jnp.sum(left_real * right_real + left_imag * right_imag, axis=4)
    cross_imag = jnp.sum(left_imag * right_real - left_real * right_imag, axis=4)
    cross = jnp.concatenate([cross_real, cross_imag], axis=-1)
    inverse_b = jnp.concatenate(
        [jnp.concatenate([cosine_b, sine_b], axis=1), jnp.concatenate([-sine_b, cosine_b], axis=1)],
        axis=0,
    )
    lag = matmul(cross.reshape(-1, 2 * factor_b), inverse_b).reshape(
        slot_total, rows_local, stations, stations, 2, factor_b
    )
    lag_real, lag_imag = lag[:, :, :, :, 0], lag[:, :, :, :, 1]
    cosine_u, sine_u = angles(k1_ids, index_b, SAMPLES)
    turn_real = lag_real * cosine_u[None, :, None, None, :] - lag_imag * sine_u[None, :, None, None, :]
    turn_imag = lag_real * sine_u[None, :, None, None, :] + lag_imag * cosine_u[None, :, None, None, :]
    lag_ids = jnp.concatenate(
        [jnp.arange(LAGS, dtype=jnp.int32), factor_a - LAGS + jnp.arange(LAGS, dtype=jnp.int32)]
    )
    cosine_l, sine_l = angles(lag_ids, k1_ids, factor_a)
    lag_weights = jnp.concatenate([cosine_l, -sine_l], axis=1).reshape(
        time_devices, 2 * LAGS // time_devices, 2 * rows_local
    )
    turned = jnp.concatenate([turn_real, turn_imag], axis=1)
    scale_out = 1.0 / math.sqrt(SAMPLES * hour_count)
    live_mask = (jnp.arange(slot_total) < pair_count).astype(jnp.float32) * scale_out
    lag_block = jnp.einsum(
        "dwp,spijm->dsijwm",
        lag_weights,
        turned,
        precision=highest,
        preferred_element_type=jnp.float32,
    )
    lag_block = lag_block * live_mask[None, :, None, None, None, None]
    gathered = lax.all_to_all(lag_block, "tm", split_axis=0, concat_axis=0, tiled=True)
    total = jnp.sum(gathered, axis=0)
    return total.reshape(slot_total, stations, stations, 2 * LAGS * factor_b // time_devices)


def solution(mesh):
    placed = (P("sta", None, "tm"), P("sta", None), P("sta"))
    return jax.shard_map(
        local, mesh=mesh, in_specs=placed, out_specs=P("sta", None, None, "tm"), check_vma=False
    )
```

```python
import math

import jax
import jax.numpy as jnp
from jax import lax
from jax.sharding import PartitionSpec as P

SAMPLES = 65536
FACTOR_A = 256
BAND = 32
LAGS = 4
REACH = 3


highest = lax.Precision.HIGH
epsilon = 1e-06


def passed_along(block, axis, distance):
    devices = range(lax.axis_size(axis))
    route = [(i - distance, i) for i in devices if i - distance in devices]
    return lax.ppermute(block, axis, route)


def angles(row_ids, col_ids, modulus):
    product = row_ids[:, None] * col_ids[None, :] % modulus
    radians = product.astype(jnp.float32) * (2.0 * math.pi / modulus)
    return (jnp.cos(radians), jnp.sin(radians))


def matmul(left_mat, right_mat):
    return jnp.dot(left_mat, right_mat, precision=highest, preferred_element_type=jnp.float32)


def local(records, pair_blocks, pair_count):
    stations, hour_count, _ = records.shape
    time_devices = lax.axis_size("tm")
    time_rank = lax.axis_index("tm")
    owner_id = lax.axis_index("sta")
    factor_a = FACTOR_A
    factor_b = SAMPLES // FACTOR_A
    rows_local = factor_a // time_devices
    cols_local = factor_b // time_devices
    series = stations * hour_count
    arranged = records.reshape(series, rows_local, factor_b).transpose(1, 0, 2)
    spread = lax.all_to_all(arranged, "tm", split_axis=2, concat_axis=0, tiled=True)
    index_a = jnp.arange(factor_a, dtype=jnp.int32)
    index_b = jnp.arange(factor_b, dtype=jnp.int32)
    paired = rows_local == 2 * BAND and factor_a == 2 * BAND * time_devices
    if paired:
        k1_ids = jnp.concatenate(
            [
                BAND * time_rank + jnp.arange(BAND, dtype=jnp.int32),
                factor_a - BAND * (time_rank + 1) + jnp.arange(BAND, dtype=jnp.int32),
            ]
        )
    else:
        k1_ids = time_rank * rows_local + jnp.arange(rows_local, dtype=jnp.int32)
    cosine_a, sine_a = angles(index_a, index_a, factor_a)
    flat_rows = spread.reshape(factor_a, series * cols_local)
    both_a = jnp.concatenate([cosine_a, -sine_a], axis=0)
    section = matmul(both_a, flat_rows).reshape(2, factor_a, series, cols_local)
    section_real, section_imag = section[0], section[1]
    col_global = time_rank * cols_local + jnp.arange(cols_local, dtype=jnp.int32)
    cosine_t, sine_t = angles(index_a, col_global, SAMPLES)
    twisted_real = section_real * cosine_t[:, None, :] + section_imag * sine_t[:, None, :]
    twisted_imag = section_imag * cosine_t[:, None, :] - section_real * sine_t[:, None, :]
    twisted = jnp.stack([twisted_real, twisted_imag], axis=2)
    if paired:
        bands = twisted.reshape(2, time_devices, BAND, series, 2, cols_local)
        grouped = jnp.stack([bands[0], bands[1][::-1]], axis=1)
        outgoing = grouped.reshape(time_devices, rows_local, series, 2, cols_local)[:, : BAND + 1]
        incoming = lax.all_to_all(outgoing, "tm", split_axis=0, concat_axis=4, tiled=True).reshape(
            BAND + 1, series, 2, factor_b
        )
        phase_cos, phase_sin = angles(jnp.ones((1,), jnp.int32), index_b, factor_b)
        source = incoming[1:BAND][::-1]
        source_real, source_imag = source[:, :, 0], source[:, :, 1]
        mirror = jnp.stack(
            [
                source_real * phase_cos - source_imag * phase_sin,
                -(source_real * phase_sin + source_imag * phase_cos),
            ],
            axis=2,
        )
        moved = jnp.concatenate([incoming, mirror])
    else:
        moved = lax.all_to_all(twisted, "tm", split_axis=0, concat_axis=3, tiled=True)
    cosine_b, sine_b = angles(index_b, index_b, factor_b)
    forward_b = jnp.concatenate(
        [jnp.concatenate([cosine_b, -sine_b], axis=1), jnp.concatenate([sine_b, cosine_b], axis=1)],
        axis=0,
    )
    spec = matmul(moved.reshape(rows_local * series, 2 * factor_b), forward_b)
    banded = spec.reshape(rows_local // BAND, BAND, series, 2, factor_b)
    band_power = jnp.mean(
        banded[:, :, :, 0] * banded[:, :, :, 0] + banded[:, :, :, 1] * banded[:, :, :, 1],
        axis=1,
        keepdims=True,
    )
    band_scale = lax.rsqrt(band_power + epsilon)
    whitened = (banded * band_scale[:, :, :, None]).reshape(rows_local, series, 2, factor_b)
    if paired:
        scale_row = band_scale[:, 0].transpose(1, 0, 2)[None]
        sent = jnp.concatenate([spec.reshape(rows_local, series, 2, factor_b)[: BAND + 1], scale_row])

        def rebuilt(piece):
            spec_part = piece[:, : BAND + 1]
            scale_low = piece[:, BAND + 1, :, 0][:, None, :, None, :]
            scale_high = piece[:, BAND + 1, :, 1][:, None, :, None, :]
            conj_sign = (1 - 2 * lax.iota(jnp.int32, 2)).astype(jnp.float32)[None, None, None, :, None]
            mirrored = spec_part[:, 1:BAND][:, ::-1, :, :, ::-1] * conj_sign
            high = jnp.concatenate([spec_part[:, BAND:], mirrored], axis=1)
            return jnp.concatenate([spec_part[:, :BAND] * scale_low, high * scale_high], axis=1)

    else:
        sent = whitened

        def rebuilt(piece):
            return piece

    arrived = {}
    for distance in range(REACH, 0, -1):
        arrived[distance] = passed_along(sent, "sta", -distance)
    received = [rebuilt(arrived[distance][None]) for distance in range(1, REACH + 1)]
    nearby = jnp.concatenate([whitened[None]] + received).reshape(REACH + 1, rows_local, stations, hour_count, 2, factor_b)
    slot_total = pair_blocks.shape[0]
    first_off = pair_blocks[:, 0] - owner_id
    second_off = pair_blocks[:, 1] - owner_id

    def chosen(offsets):
        pick = offsets.reshape((slot_total,) + (1,) * (nearby.ndim - 1))
        result = jnp.broadcast_to(nearby[REACH], (slot_total,) + nearby.shape[1:])
        for distance in range(REACH - 1, -1, -1):
            result = jnp.where(pick == distance, nearby[distance], result)
        return result

    left_spec = chosen(first_off)
    right_spec = chosen(second_off)
    left_real = left_spec[:, :, :, None, :, 0]
    left_imag = left_spec[:, :, :, None, :, 1]
    right_real = right_spec[:, :, None, :, :, 0]
    right_imag = right_spec[:, :, None, :, :, 1]
    cross_real = jnp.sum(left_real * right_real + left_imag * right_imag, axis=4)
    cross_imag = jnp.sum(left_imag * right_real - left_real * right_imag, axis=4)
    cross = jnp.concatenate([cross_real, cross_imag], axis=-1)
    inverse_b = jnp.concatenate(
        [jnp.concatenate([cosine_b, sine_b], axis=1), jnp.concatenate([-sine_b, cosine_b], axis=1)],
        axis=0,
    )
    lag = matmul(cross.reshape(-1, 2 * factor_b), inverse_b).reshape(
        slot_total, rows_local, stations, stations, 2, factor_b
    )
    lag_real, lag_imag = lag[:, :, :, :, 0], lag[:, :, :, :, 1]
    cosine_u, sine_u = angles(k1_ids, index_b, SAMPLES)
    turn_real = lag_real * cosine_u[None, :, None, None, :] - lag_imag * sine_u[None, :, None, None, :]
    turn_imag = lag_real * sine_u[None, :, None, None, :] + lag_imag * cosine_u[None, :, None, None, :]
    lag_ids = jnp.concatenate(
        [jnp.arange(LAGS, dtype=jnp.int32), factor_a - LAGS + jnp.arange(LAGS, dtype=jnp.int32)]
    )
    cosine_l, sine_l = angles(lag_ids, k1_ids, factor_a)
    lag_weights = jnp.concatenate([cosine_l, -sine_l], axis=1).reshape(
        time_devices, 2 * LAGS // time_devices, 2 * rows_local
    )
    turned = jnp.concatenate([turn_real, turn_imag], axis=1)
    scale_out = 1.0 / math.sqrt(SAMPLES * hour_count)
    live_mask = (jnp.arange(slot_total) < pair_count).astype(jnp.float32) * scale_out
    lag_block = jnp.einsum(
        "dwp,spijm->dsijwm",
        lag_weights,
        turned,
        precision=highest,
        preferred_element_type=jnp.float32,
    )
    lag_block = lag_block * live_mask[None, :, None, None, None, None]
    gathered = lax.all_to_all(lag_block, "tm", split_axis=0, concat_axis=0, tiled=True)
    total = jnp.sum(gathered, axis=0)
    return total.reshape(slot_total, stations, stations, 2 * LAGS * factor_b // time_devices)


def solution(mesh):
    placed = (P("sta", None, "tm"), P("sta", None), P("sta"))
    return jax.shard_map(local, mesh=mesh, in_specs=placed, out_specs=P("sta", None, None, "tm"), check_vma=False)
```

```python
import math

import jax
import jax.numpy as jnp
from jax import lax
from jax.sharding import PartitionSpec as P

SAMPLES = 65536
FACTOR_A = 256
BAND = 32
LAGS = 4
REACH = 3


highest = lax.Precision.HIGH
epsilon = 1e-06


def passed_along(block, axis, distance):
    devices = range(lax.axis_size(axis))
    route = [(i - distance, i) for i in devices if i - distance in devices]
    return lax.ppermute(block, axis, route)


def angles(row_ids, col_ids, modulus):
    product = row_ids[:, None] * col_ids[None, :] % modulus
    radians = product.astype(jnp.float32) * (2.0 * math.pi / modulus)
    return (jnp.cos(radians), jnp.sin(radians))


def matmul(left_mat, right_mat):
    return jnp.dot(left_mat, right_mat, precision=highest, preferred_element_type=jnp.float32)


def local(records, pair_blocks, pair_count):
    stations, hour_count, _ = records.shape
    time_devices = lax.axis_size("tm")
    time_rank = lax.axis_index("tm")
    owner_id = lax.axis_index("sta")
    factor_a = FACTOR_A
    factor_b = SAMPLES // FACTOR_A
    rows_local = factor_a // time_devices
    cols_local = factor_b // time_devices
    series = stations * hour_count
    arranged = records.reshape(series, rows_local, factor_b).transpose(1, 0, 2)
    spread = lax.all_to_all(arranged, "tm", split_axis=2, concat_axis=0, tiled=True)
    index_a = jnp.arange(factor_a, dtype=jnp.int32)
    index_b = jnp.arange(factor_b, dtype=jnp.int32)
    paired = rows_local == 2 * BAND and factor_a == 2 * BAND * time_devices
    if paired:
        k1_ids = jnp.concatenate(
            [
                BAND * time_rank + jnp.arange(BAND, dtype=jnp.int32),
                factor_a - BAND * (time_rank + 1) + jnp.arange(BAND, dtype=jnp.int32),
            ]
        )
    else:
        k1_ids = time_rank * rows_local + jnp.arange(rows_local, dtype=jnp.int32)
    cosine_a, sine_a = angles(index_a, index_a, factor_a)
    flat_rows = spread.reshape(factor_a, series * cols_local)
    both_a = jnp.concatenate([cosine_a, -sine_a], axis=0)
    section = matmul(both_a, flat_rows).reshape(2, factor_a, series, cols_local)
    section_real, section_imag = section[0], section[1]
    col_global = time_rank * cols_local + jnp.arange(cols_local, dtype=jnp.int32)
    cosine_t, sine_t = angles(index_a, col_global, SAMPLES)
    twisted_real = section_real * cosine_t[:, None, :] + section_imag * sine_t[:, None, :]
    twisted_imag = section_imag * cosine_t[:, None, :] - section_real * sine_t[:, None, :]
    twisted = jnp.stack([twisted_real, twisted_imag], axis=2)
    if paired:
        bands = twisted.reshape(2, time_devices, BAND, series, 2, cols_local)
        grouped = jnp.stack([bands[0], bands[1][::-1]], axis=1)
        outgoing = grouped.reshape(time_devices, rows_local, series, 2, cols_local)[:, : BAND + 1]
        incoming = lax.all_to_all(outgoing, "tm", split_axis=0, concat_axis=4, tiled=True).reshape(
            BAND + 1, series, 2, factor_b
        )
        phase_cos, phase_sin = angles(jnp.ones((1,), jnp.int32), index_b, factor_b)
        source = incoming[1:BAND][::-1]
        source_real, source_imag = source[:, :, 0], source[:, :, 1]
        mirror = jnp.stack(
            [
                source_real * phase_cos - source_imag * phase_sin,
                -(source_real * phase_sin + source_imag * phase_cos),
            ],
            axis=2,
        )
        moved = jnp.concatenate([incoming, mirror])
    else:
        moved = lax.all_to_all(twisted, "tm", split_axis=0, concat_axis=3, tiled=True)
    cosine_b, sine_b = angles(index_b, index_b, factor_b)
    forward_b = jnp.concatenate(
        [jnp.concatenate([cosine_b, -sine_b], axis=1), jnp.concatenate([sine_b, cosine_b], axis=1)],
        axis=0,
    )
    spec = matmul(moved.reshape(rows_local * series, 2 * factor_b), forward_b)
    banded = spec.reshape(rows_local // BAND, BAND, series, 2, factor_b)
    band_power = jnp.mean(
        banded[:, :, :, 0] * banded[:, :, :, 0] + banded[:, :, :, 1] * banded[:, :, :, 1],
        axis=1,
        keepdims=True,
    )
    band_scale = lax.rsqrt(band_power + epsilon)
    whitened = (banded * band_scale[:, :, :, None]).reshape(rows_local, series, 2, factor_b)
    if paired:
        scale_row = band_scale[:, 0].transpose(1, 0, 2)[None]
        sent = jnp.concatenate([spec.reshape(rows_local, series, 2, factor_b)[: BAND + 1], scale_row])
    else:
        sent = whitened
    arrived = {}
    for distance in range(REACH, 0, -1):
        arrived[distance] = passed_along(sent, "sta", -distance)
    nearby = jnp.stack([sent] + [arrived[distance] for distance in range(1, REACH + 1)])
    slot_total = pair_blocks.shape[0]
    first_off = pair_blocks[:, 0] - owner_id
    second_off = pair_blocks[:, 1] - owner_id

    def chosen(offsets):
        pick = offsets.reshape((slot_total,) + (1,) * (nearby.ndim - 1))
        result = jnp.broadcast_to(nearby[REACH], (slot_total,) + nearby.shape[1:])
        for distance in range(REACH - 1, -1, -1):
            result = jnp.where(pick == distance, nearby[distance], result)
        return result

    def domain(block):
        if not paired:
            return block
        spec_part = block[:, : BAND + 1]
        scale_low = block[:, BAND + 1, :, 0][:, None, :, None, :]
        scale_high = block[:, BAND + 1, :, 1]
        scale_turned = scale_high[:, :, ::-1][:, None, :, None, :]
        conj_sign = (1 - 2 * lax.iota(jnp.int32, 2)).astype(jnp.float32)[None, None, None, :, None]
        low = spec_part[:, :BAND] * scale_low
        middle = spec_part[:, BAND:] * scale_high[:, None, :, None, :]
        high = spec_part[:, 1:BAND] * conj_sign * scale_turned
        return jnp.concatenate([low, middle, high], axis=1)

    spec_shape = (slot_total, rows_local, stations, hour_count, 2, factor_b)
    left_spec = domain(chosen(first_off)).reshape(spec_shape)
    right_spec = domain(chosen(second_off)).reshape(spec_shape)
    left_real = left_spec[:, :, :, None, :, 0]
    left_imag = left_spec[:, :, :, None, :, 1]
    right_real = right_spec[:, :, None, :, :, 0]
    right_imag = right_spec[:, :, None, :, :, 1]
    cross_real = jnp.sum(left_real * right_real + left_imag * right_imag, axis=4)
    cross_imag = jnp.sum(left_imag * right_real - left_real * right_imag, axis=4)
    cross = jnp.concatenate([cross_real, cross_imag], axis=-1)

    def inverse_of(cosines, sines):
        return jnp.concatenate(
            [jnp.concatenate([cosines, sines], axis=1), jnp.concatenate([-sines, cosines], axis=1)],
            axis=0,
        )

    lag_shape = (slot_total, -1, stations, stations, 2, factor_b)
    if paired:
        cosine_r, sine_r = angles(factor_b - 1 - index_b, index_b, factor_b)
        lag_low = matmul(cross[:, : BAND + 1].reshape(-1, 2 * factor_b), inverse_of(cosine_b, sine_b))
        lag_high = matmul(cross[:, BAND + 1 :].reshape(-1, 2 * factor_b), inverse_of(cosine_r, sine_r))
        lag = jnp.concatenate([lag_low.reshape(lag_shape), lag_high.reshape(lag_shape)], axis=1)
        row_ids = jnp.concatenate([k1_ids[: BAND + 1], k1_ids[BAND + 1 :][::-1]])
    else:
        lag = matmul(cross.reshape(-1, 2 * factor_b), inverse_of(cosine_b, sine_b)).reshape(lag_shape)
        row_ids = k1_ids
    lag_real, lag_imag = lag[:, :, :, :, 0], lag[:, :, :, :, 1]
    cosine_u, sine_u = angles(row_ids, index_b, SAMPLES)
    turn_real = lag_real * cosine_u[None, :, None, None, :] - lag_imag * sine_u[None, :, None, None, :]
    turn_imag = lag_real * sine_u[None, :, None, None, :] + lag_imag * cosine_u[None, :, None, None, :]
    lag_ids = jnp.concatenate(
        [jnp.arange(LAGS, dtype=jnp.int32), factor_a - LAGS + jnp.arange(LAGS, dtype=jnp.int32)]
    )
    cosine_l, sine_l = angles(lag_ids, row_ids, factor_a)
    lag_weights = jnp.concatenate([cosine_l, -sine_l], axis=1).reshape(
        time_devices, 2 * LAGS // time_devices, 2 * rows_local
    )
    turned = jnp.concatenate([turn_real, turn_imag], axis=1)
    scale_out = 1.0 / math.sqrt(SAMPLES * hour_count)
    live_mask = (jnp.arange(slot_total) < pair_count).astype(jnp.float32) * scale_out
    lag_block = jnp.einsum(
        "dwp,spijm->dsijwm",
        lag_weights,
        turned,
        precision=highest,
        preferred_element_type=jnp.float32,
    )
    lag_block = lag_block * live_mask[None, :, None, None, None, None]
    gathered = lax.all_to_all(lag_block, "tm", split_axis=0, concat_axis=0, tiled=True)
    total = jnp.sum(gathered, axis=0)
    return total.reshape(slot_total, stations, stations, 2 * LAGS * factor_b // time_devices)


def solution(mesh):
    placed = (P("sta", None, "tm"), P("sta", None), P("sta"))
    return jax.shard_map(local, mesh=mesh, in_specs=placed, out_specs=P("sta", None, None, "tm"), check_vma=False)
```

```python
import math

import jax
import jax.numpy as jnp
from jax import lax
from jax.sharding import PartitionSpec as P

SAMPLES = 65536
FACTOR_A = 256
BAND = 32
LAGS = 4
REACH = 3


highest = lax.Precision.HIGH
epsilon = 1e-06


def passed_along(block, axis, distance):
    devices = range(lax.axis_size(axis))
    route = [(i - distance, i) for i in devices if i - distance in devices]
    return lax.ppermute(block, axis, route)


def angles(row_ids, col_ids, modulus):
    product = row_ids[:, None] * col_ids[None, :] % modulus
    radians = product.astype(jnp.float32) * (2.0 * math.pi / modulus)
    return (jnp.cos(radians), jnp.sin(radians))


def matmul(left_mat, right_mat):
    return jnp.dot(left_mat, right_mat, precision=highest, preferred_element_type=jnp.float32)


def local(records, pair_blocks, pair_count):
    stations, hour_count, _ = records.shape
    time_devices = lax.axis_size("tm")
    time_rank = lax.axis_index("tm")
    owner_id = lax.axis_index("sta")
    factor_a = FACTOR_A
    factor_b = SAMPLES // FACTOR_A
    rows_local = factor_a // time_devices
    cols_local = factor_b // time_devices
    series = stations * hour_count
    arranged = records.reshape(series, rows_local, factor_b).transpose(1, 0, 2)
    spread = lax.all_to_all(arranged, "tm", split_axis=2, concat_axis=0, tiled=True)
    index_a = jnp.arange(factor_a, dtype=jnp.int32)
    index_b = jnp.arange(factor_b, dtype=jnp.int32)
    paired = rows_local == 2 * BAND and factor_a == 2 * BAND * time_devices
    if paired:
        k1_ids = jnp.concatenate(
            [
                BAND * time_rank + jnp.arange(BAND, dtype=jnp.int32),
                factor_a - BAND * (time_rank + 1) + jnp.arange(BAND, dtype=jnp.int32),
            ]
        )
    else:
        k1_ids = time_rank * rows_local + jnp.arange(rows_local, dtype=jnp.int32)
    cosine_a, sine_a = angles(index_a, index_a, factor_a)
    flat_rows = spread.reshape(factor_a, series * cols_local)
    both_a = jnp.concatenate([cosine_a, -sine_a], axis=0)
    section = matmul(both_a, flat_rows).reshape(2, factor_a, series, cols_local)
    section_real, section_imag = section[0], section[1]
    col_global = time_rank * cols_local + jnp.arange(cols_local, dtype=jnp.int32)
    cosine_t, sine_t = angles(index_a, col_global, SAMPLES)
    twisted_real = section_real * cosine_t[:, None, :] + section_imag * sine_t[:, None, :]
    twisted_imag = section_imag * cosine_t[:, None, :] - section_real * sine_t[:, None, :]
    twisted = jnp.stack([twisted_real, twisted_imag], axis=2)
    if paired:
        bands = twisted.reshape(2, time_devices, BAND, series, 2, cols_local)
        grouped = jnp.stack([bands[0], bands[1][::-1]], axis=1)
        outgoing = grouped.reshape(time_devices, rows_local, series, 2, cols_local)[:, : BAND + 1]
        incoming = lax.all_to_all(outgoing, "tm", split_axis=0, concat_axis=4, tiled=True).reshape(
            BAND + 1, series, 2, factor_b
        )
        unit_row = lax.optimization_barrier((jnp.ones((1,), jnp.int32), spread))[0]
        phase_cos, phase_sin = angles(unit_row, index_b, factor_b)
        source = incoming[1:BAND][::-1]
        source_real, source_imag = source[:, :, 0], source[:, :, 1]
        mirror = jnp.stack(
            [
                source_real * phase_cos - source_imag * phase_sin,
                -(source_real * phase_sin + source_imag * phase_cos),
            ],
            axis=2,
        )
        moved = jnp.concatenate([incoming, mirror])
    else:
        moved = lax.all_to_all(twisted, "tm", split_axis=0, concat_axis=3, tiled=True)
    cosine_b, sine_b = angles(index_b, index_b, factor_b)
    forward_b = jnp.concatenate(
        [jnp.concatenate([cosine_b, -sine_b], axis=1), jnp.concatenate([sine_b, cosine_b], axis=1)],
        axis=0,
    )
    spec = matmul(moved.reshape(rows_local * series, 2 * factor_b), forward_b)
    banded = spec.reshape(rows_local // BAND, BAND, series, 2, factor_b)
    band_power = jnp.mean(
        banded[:, :, :, 0] * banded[:, :, :, 0] + banded[:, :, :, 1] * banded[:, :, :, 1],
        axis=1,
        keepdims=True,
    )
    band_scale = lax.rsqrt(band_power + epsilon)
    whitened = (banded * band_scale[:, :, :, None]).reshape(rows_local, series, 2, factor_b)
    if paired:
        scale_row = band_scale[:, 0].transpose(1, 0, 2)[None]
        sent = jnp.concatenate([spec.reshape(rows_local, series, 2, factor_b)[: BAND + 1], scale_row])
    else:
        sent = whitened
    if paired:
        row_ids = jnp.concatenate([k1_ids[: BAND + 1], k1_ids[BAND + 1 :][::-1]])
    else:
        row_ids = k1_ids
    row_ids, turned_index = lax.optimization_barrier((row_ids, factor_b - 1 - index_b, sent))[:2]
    arrived = {}
    for distance in range(REACH, 0, -1):
        arrived[distance] = passed_along(sent, "sta", -distance)
    nearby = jnp.stack([sent] + [arrived[distance] for distance in range(1, REACH + 1)])
    slot_total = pair_blocks.shape[0]
    first_off = pair_blocks[:, 0] - owner_id
    second_off = pair_blocks[:, 1] - owner_id

    def chosen(offsets):
        pick = offsets.reshape((slot_total,) + (1,) * (nearby.ndim - 1))
        result = jnp.broadcast_to(nearby[REACH], (slot_total,) + nearby.shape[1:])
        for distance in range(REACH - 1, -1, -1):
            result = jnp.where(pick == distance, nearby[distance], result)
        return result

    def domain(block):
        if not paired:
            return block
        spec_part = block[:, : BAND + 1]
        scale_low = block[:, BAND + 1, :, 0][:, None, :, None, :]
        scale_high = block[:, BAND + 1, :, 1]
        scale_turned = scale_high[:, :, ::-1][:, None, :, None, :]
        conj_sign = (1 - 2 * lax.iota(jnp.int32, 2)).astype(jnp.float32)[None, None, None, :, None]
        low = spec_part[:, :BAND] * scale_low
        middle = spec_part[:, BAND:] * scale_high[:, None, :, None, :]
        high = spec_part[:, 1:BAND] * conj_sign * scale_turned
        return jnp.concatenate([low, middle, high], axis=1)

    spec_shape = (slot_total, rows_local, stations, hour_count, 2, factor_b)
    left_spec = domain(chosen(first_off)).reshape(spec_shape)
    right_spec = domain(chosen(second_off)).reshape(spec_shape)
    left_real = left_spec[:, :, :, None, :, 0]
    left_imag = left_spec[:, :, :, None, :, 1]
    right_real = right_spec[:, :, None, :, :, 0]
    right_imag = right_spec[:, :, None, :, :, 1]
    cross_real = jnp.sum(left_real * right_real + left_imag * right_imag, axis=4)
    cross_imag = jnp.sum(left_imag * right_real - left_real * right_imag, axis=4)
    cross = jnp.concatenate([cross_real, cross_imag], axis=-1)

    def inverse_of(cosines, sines):
        return jnp.concatenate(
            [jnp.concatenate([cosines, sines], axis=1), jnp.concatenate([-sines, cosines], axis=1)],
            axis=0,
        )

    lag_shape = (slot_total, -1, stations, stations, 2, factor_b)
    if paired:
        cosine_r, sine_r = angles(turned_index, index_b, factor_b)
        lag_low = matmul(cross[:, : BAND + 1].reshape(-1, 2 * factor_b), inverse_of(cosine_b, sine_b))
        lag_high = matmul(cross[:, BAND + 1 :].reshape(-1, 2 * factor_b), inverse_of(cosine_r, sine_r))
        lag = jnp.concatenate([lag_low.reshape(lag_shape), lag_high.reshape(lag_shape)], axis=1)
    else:
        lag = matmul(cross.reshape(-1, 2 * factor_b), inverse_of(cosine_b, sine_b)).reshape(lag_shape)
    lag_real, lag_imag = lag[:, :, :, :, 0], lag[:, :, :, :, 1]
    cosine_u, sine_u = angles(row_ids, index_b, SAMPLES)
    turn_real = lag_real * cosine_u[None, :, None, None, :] - lag_imag * sine_u[None, :, None, None, :]
    turn_imag = lag_real * sine_u[None, :, None, None, :] + lag_imag * cosine_u[None, :, None, None, :]
    lag_ids = jnp.concatenate(
        [jnp.arange(LAGS, dtype=jnp.int32), factor_a - LAGS + jnp.arange(LAGS, dtype=jnp.int32)]
    )
    cosine_l, sine_l = angles(lag_ids, row_ids, factor_a)
    lag_weights = jnp.concatenate([cosine_l, -sine_l], axis=1).reshape(
        time_devices, 2 * LAGS // time_devices, 2 * rows_local
    )
    turned = jnp.concatenate([turn_real, turn_imag], axis=1)
    scale_out = 1.0 / math.sqrt(SAMPLES * hour_count)
    live_mask = (jnp.arange(slot_total) < pair_count).astype(jnp.float32) * scale_out
    lag_block = jnp.einsum(
        "dwp,spijm->dsijwm",
        lag_weights,
        turned,
        precision=highest,
        preferred_element_type=jnp.float32,
    )
    lag_block = lag_block * live_mask[None, :, None, None, None, None]
    gathered = lax.all_to_all(lag_block, "tm", split_axis=0, concat_axis=0, tiled=True)
    total = jnp.sum(gathered, axis=0)
    return total.reshape(slot_total, stations, stations, 2 * LAGS * factor_b // time_devices)


def solution(mesh):
    placed = (P("sta", None, "tm"), P("sta", None), P("sta"))
    return jax.shard_map(local, mesh=mesh, in_specs=placed, out_specs=P("sta", None, None, "tm"), check_vma=False)
```

```python
import math

import jax
import jax.numpy as jnp
from jax import lax
from jax.sharding import PartitionSpec as P

SAMPLES = 65536
FACTOR_A = 256
BAND = 32
LAGS = 4
REACH = 3


highest = lax.Precision.HIGH
epsilon = 1e-06


def passed_along(block, axis, distance):
    devices = range(lax.axis_size(axis))
    route = [(i - distance, i) for i in devices if i - distance in devices]
    return lax.ppermute(block, axis, route)


def angles(row_ids, col_ids, modulus):
    product = row_ids[:, None] * col_ids[None, :] % modulus
    radians = product.astype(jnp.float32) * (2.0 * math.pi / modulus)
    return (jnp.cos(radians), jnp.sin(radians))


def matmul(left_mat, right_mat):
    return jnp.dot(left_mat, right_mat, precision=highest, preferred_element_type=jnp.float32)


def local(records, pair_blocks, pair_count):
    stations, hour_count, _ = records.shape
    time_devices = lax.axis_size("tm")
    time_rank = lax.axis_index("tm")
    owner_id = lax.axis_index("sta")
    factor_a = FACTOR_A
    factor_b = SAMPLES // FACTOR_A
    rows_local = factor_a // time_devices
    cols_local = factor_b // time_devices
    series = stations * hour_count
    arranged = records.reshape(series, rows_local, time_devices, cols_local).transpose(2, 1, 0, 3)
    spread = lax.all_to_all(
        arranged.reshape(time_devices, -1), "tm", split_axis=0, concat_axis=0, tiled=True
    ).reshape(factor_a, series, cols_local)
    index_a = jnp.arange(factor_a, dtype=jnp.int32)
    index_b = jnp.arange(factor_b, dtype=jnp.int32)
    paired = rows_local == 2 * BAND and factor_a == 2 * BAND * time_devices
    if paired:
        k1_ids = jnp.concatenate(
            [
                BAND * time_rank + jnp.arange(BAND, dtype=jnp.int32),
                factor_a - BAND * (time_rank + 1) + jnp.arange(BAND, dtype=jnp.int32),
            ]
        )
    else:
        k1_ids = time_rank * rows_local + jnp.arange(rows_local, dtype=jnp.int32)
    cosine_a, sine_a = angles(index_a, index_a, factor_a)
    flat_rows = spread.reshape(factor_a, series * cols_local)
    both_a = jnp.concatenate([cosine_a, -sine_a], axis=0)
    section = matmul(both_a, flat_rows).reshape(2, factor_a, series, cols_local)
    section_real, section_imag = section[0], section[1]
    col_global = time_rank * cols_local + jnp.arange(cols_local, dtype=jnp.int32)
    cosine_t, sine_t = angles(index_a, col_global, SAMPLES)
    twisted_real = section_real * cosine_t[:, None, :] + section_imag * sine_t[:, None, :]
    twisted_imag = section_imag * cosine_t[:, None, :] - section_real * sine_t[:, None, :]
    twisted = jnp.stack([twisted_real, twisted_imag], axis=2)
    if paired:
        bands = twisted.reshape(2, time_devices, BAND, series, 2, cols_local)
        grouped = jnp.stack([bands[0], bands[1][::-1]], axis=1)
        outgoing = grouped.reshape(time_devices, rows_local, series, 2, cols_local)[:, : BAND + 1]
        incoming = lax.all_to_all(outgoing, "tm", split_axis=0, concat_axis=4, tiled=True).reshape(
            BAND + 1, series, 2, factor_b
        )
        unit_row = lax.optimization_barrier((jnp.ones((1,), jnp.int32), spread))[0]
        phase_cos, phase_sin = angles(unit_row, index_b, factor_b)
        source = incoming[1:BAND][::-1]
        source_real, source_imag = source[:, :, 0], source[:, :, 1]
        mirror = jnp.stack(
            [
                source_real * phase_cos - source_imag * phase_sin,
                -(source_real * phase_sin + source_imag * phase_cos),
            ],
            axis=2,
        )
        moved = jnp.concatenate([incoming, mirror])
    else:
        moved = lax.all_to_all(twisted, "tm", split_axis=0, concat_axis=3, tiled=True)
    cosine_b, sine_b = angles(index_b, index_b, factor_b)
    forward_b = jnp.concatenate(
        [jnp.concatenate([cosine_b, -sine_b], axis=1), jnp.concatenate([sine_b, cosine_b], axis=1)],
        axis=0,
    )
    spec = matmul(moved.reshape(rows_local * series, 2 * factor_b), forward_b)
    banded = spec.reshape(rows_local // BAND, BAND, series, 2, factor_b)
    band_power = jnp.mean(
        banded[:, :, :, 0] * banded[:, :, :, 0] + banded[:, :, :, 1] * banded[:, :, :, 1],
        axis=1,
        keepdims=True,
    )
    band_scale = lax.rsqrt(band_power + epsilon)
    whitened = (banded * band_scale[:, :, :, None]).reshape(rows_local, series, 2, factor_b)
    if paired:
        scale_row = band_scale[:, 0].transpose(1, 0, 2)[None]
        sent = jnp.concatenate([spec.reshape(rows_local, series, 2, factor_b)[: BAND + 1], scale_row])
    else:
        sent = whitened
    if paired:
        row_ids = jnp.concatenate([k1_ids[: BAND + 1], k1_ids[BAND + 1 :][::-1]])
    else:
        row_ids = k1_ids
    row_ids, turned_index = lax.optimization_barrier((row_ids, factor_b - 1 - index_b, sent))[:2]
    arrived = {}
    for distance in range(REACH, 0, -1):
        arrived[distance] = passed_along(sent, "sta", -distance)
    nearby = jnp.stack([sent] + [arrived[distance] for distance in range(1, REACH + 1)])
    slot_total = pair_blocks.shape[0]
    first_off = pair_blocks[:, 0] - owner_id
    second_off = pair_blocks[:, 1] - owner_id

    def chosen(offsets):
        pick = offsets.reshape((slot_total,) + (1,) * (nearby.ndim - 1))
        result = jnp.broadcast_to(nearby[REACH], (slot_total,) + nearby.shape[1:])
        for distance in range(REACH - 1, -1, -1):
            result = jnp.where(pick == distance, nearby[distance], result)
        return result

    def domain(block):
        if not paired:
            return block
        spec_part = block[:, : BAND + 1]
        scale_low = block[:, BAND + 1, :, 0][:, None, :, None, :]
        scale_high = block[:, BAND + 1, :, 1]
        scale_turned = scale_high[:, :, ::-1][:, None, :, None, :]
        conj_sign = (1 - 2 * lax.iota(jnp.int32, 2)).astype(jnp.float32)[None, None, None, :, None]
        low = spec_part[:, :BAND] * scale_low
        middle = spec_part[:, BAND:] * scale_high[:, None, :, None, :]
        high = spec_part[:, 1:BAND] * conj_sign * scale_turned
        return jnp.concatenate([low, middle, high], axis=1)

    spec_shape = (slot_total, rows_local, stations, hour_count, 2, factor_b)
    left_spec = domain(chosen(first_off)).reshape(spec_shape)
    right_spec = domain(chosen(second_off)).reshape(spec_shape)
    left_real = left_spec[:, :, :, None, :, 0]
    left_imag = left_spec[:, :, :, None, :, 1]
    right_real = right_spec[:, :, None, :, :, 0]
    right_imag = right_spec[:, :, None, :, :, 1]
    cross_real = jnp.sum(left_real * right_real + left_imag * right_imag, axis=4)
    cross_imag = jnp.sum(left_imag * right_real - left_real * right_imag, axis=4)
    cross = jnp.concatenate([cross_real, cross_imag], axis=-1)

    def inverse_of(cosines, sines):
        return jnp.concatenate(
            [jnp.concatenate([cosines, sines], axis=1), jnp.concatenate([-sines, cosines], axis=1)],
            axis=0,
        )

    lag_shape = (slot_total, -1, stations, stations, 2, factor_b)
    if paired:
        cosine_r, sine_r = angles(turned_index, index_b, factor_b)
        lag_low = matmul(cross[:, : BAND + 1].reshape(-1, 2 * factor_b), inverse_of(cosine_b, sine_b))
        lag_high = matmul(cross[:, BAND + 1 :].reshape(-1, 2 * factor_b), inverse_of(cosine_r, sine_r))
        lag = jnp.concatenate([lag_low.reshape(lag_shape), lag_high.reshape(lag_shape)], axis=1)
    else:
        lag = matmul(cross.reshape(-1, 2 * factor_b), inverse_of(cosine_b, sine_b)).reshape(lag_shape)
    lag_real, lag_imag = lag[:, :, :, :, 0], lag[:, :, :, :, 1]
    cosine_u, sine_u = angles(row_ids, index_b, SAMPLES)
    turn_real = lag_real * cosine_u[None, :, None, None, :] - lag_imag * sine_u[None, :, None, None, :]
    turn_imag = lag_real * sine_u[None, :, None, None, :] + lag_imag * cosine_u[None, :, None, None, :]
    lag_ids = jnp.concatenate(
        [jnp.arange(LAGS, dtype=jnp.int32), factor_a - LAGS + jnp.arange(LAGS, dtype=jnp.int32)]
    )
    cosine_l, sine_l = angles(lag_ids, row_ids, factor_a)
    lag_weights = jnp.concatenate([cosine_l, -sine_l], axis=1).reshape(
        time_devices, 2 * LAGS // time_devices, 2 * rows_local
    )
    turned = jnp.concatenate([turn_real, turn_imag], axis=1)
    scale_out = 1.0 / math.sqrt(SAMPLES * hour_count)
    live_mask = (jnp.arange(slot_total) < pair_count).astype(jnp.float32) * scale_out
    lag_block = jnp.einsum(
        "dwp,spijm->dsijwm",
        lag_weights,
        turned,
        precision=highest,
        preferred_element_type=jnp.float32,
    )
    lag_block = lag_block * live_mask[None, :, None, None, None, None]
    gathered = lax.all_to_all(
        lag_block.reshape(time_devices, -1), "tm", split_axis=0, concat_axis=0, tiled=True
    )
    total = jnp.sum(gathered, axis=0)
    return total.reshape(slot_total, stations, stations, 2 * LAGS * factor_b // time_devices)


def solution(mesh):
    placed = (P("sta", None, "tm"), P("sta", None), P("sta"))
    return jax.shard_map(local, mesh=mesh, in_specs=placed, out_specs=P("sta", None, None, "tm"), check_vma=False)
```

```python
import math

import jax
import jax.numpy as jnp
from jax import lax
from jax.sharding import PartitionSpec as P

SAMPLES = 65536
FACTOR_A = 256
BAND = 32
LAGS = 4
REACH = 3


highest = lax.Precision.HIGH
epsilon = 1e-06


def passed_along(block, axis, distance):
    devices = range(lax.axis_size(axis))
    route = [(i - distance, i) for i in devices if i - distance in devices]
    return lax.ppermute(block, axis, route)


def angles(row_ids, col_ids, modulus):
    product = row_ids[:, None] * col_ids[None, :] % modulus
    radians = product.astype(jnp.float32) * (2.0 * math.pi / modulus)
    return (jnp.cos(radians), jnp.sin(radians))


def matmul(left_mat, right_mat):
    return jnp.dot(left_mat, right_mat, precision=highest, preferred_element_type=jnp.float32)


def local(records, pair_blocks, pair_count):
    stations, hour_count, _ = records.shape
    time_devices = lax.axis_size("tm")
    time_rank = lax.axis_index("tm")
    owner_id = lax.axis_index("sta")
    factor_a = FACTOR_A
    factor_b = SAMPLES // FACTOR_A
    rows_local = factor_a // time_devices
    cols_local = factor_b // time_devices
    series = stations * hour_count
    arranged = records.reshape(series, rows_local, time_devices, cols_local).transpose(2, 1, 0, 3)
    spread = lax.all_to_all(
        arranged.reshape(time_devices, -1), "tm", split_axis=0, concat_axis=0, tiled=True
    ).reshape(factor_a, series, cols_local)
    index_a = jnp.arange(factor_a, dtype=jnp.int32)
    index_b = jnp.arange(factor_b, dtype=jnp.int32)
    paired = rows_local == 2 * BAND and factor_a == 2 * BAND * time_devices
    if paired:
        k1_ids = jnp.concatenate(
            [
                BAND * time_rank + jnp.arange(BAND, dtype=jnp.int32),
                factor_a - BAND * (time_rank + 1) + jnp.arange(BAND, dtype=jnp.int32),
            ]
        )
    else:
        k1_ids = time_rank * rows_local + jnp.arange(rows_local, dtype=jnp.int32)
    cosine_a, sine_a = angles(index_a, index_a, factor_a)
    flat_rows = spread.reshape(factor_a, series * cols_local)
    both_a = jnp.concatenate([cosine_a, -sine_a], axis=0)
    section = matmul(both_a, flat_rows).reshape(2, factor_a, series, cols_local)
    section_real, section_imag = section[0], section[1]
    col_global = time_rank * cols_local + jnp.arange(cols_local, dtype=jnp.int32)
    cosine_t, sine_t = angles(index_a, col_global, SAMPLES)
    twisted_real = section_real * cosine_t[:, None, :] + section_imag * sine_t[:, None, :]
    twisted_imag = section_imag * cosine_t[:, None, :] - section_real * sine_t[:, None, :]
    twisted = jnp.stack([twisted_real, twisted_imag], axis=2)
    if paired:
        bands = twisted.reshape(2, time_devices, BAND, series, 2, cols_local)
        grouped = jnp.stack([bands[0], bands[1][::-1]], axis=1)
        outgoing = grouped.reshape(time_devices, rows_local, series, 2, cols_local)[:, : BAND + 1]
        incoming = (
            lax.all_to_all(outgoing.reshape(time_devices, -1), "tm", split_axis=0, concat_axis=0, tiled=True)
            .reshape(time_devices, BAND + 1, series, 2, cols_local)
            .transpose(1, 2, 3, 0, 4)
            .reshape(BAND + 1, series, 2, factor_b)
        )
        unit_row = lax.optimization_barrier((jnp.ones((1,), jnp.int32), spread))[0]
        phase_cos, phase_sin = angles(unit_row, index_b, factor_b)
        source = incoming[1:BAND][::-1]
        source_real, source_imag = source[:, :, 0], source[:, :, 1]
        mirror = jnp.stack(
            [
                source_real * phase_cos - source_imag * phase_sin,
                -(source_real * phase_sin + source_imag * phase_cos),
            ],
            axis=2,
        )
        moved = jnp.concatenate([incoming, mirror])
    else:
        moved = lax.all_to_all(twisted, "tm", split_axis=0, concat_axis=3, tiled=True)
    cosine_b, sine_b = angles(index_b, index_b, factor_b)
    forward_b = jnp.concatenate(
        [jnp.concatenate([cosine_b, -sine_b], axis=1), jnp.concatenate([sine_b, cosine_b], axis=1)],
        axis=0,
    )
    spec = matmul(moved.reshape(rows_local * series, 2 * factor_b), forward_b)
    banded = spec.reshape(rows_local // BAND, BAND, series, 2, factor_b)
    band_power = jnp.mean(
        banded[:, :, :, 0] * banded[:, :, :, 0] + banded[:, :, :, 1] * banded[:, :, :, 1],
        axis=1,
        keepdims=True,
    )
    band_scale = lax.rsqrt(band_power + epsilon)
    whitened = (banded * band_scale[:, :, :, None]).reshape(rows_local, series, 2, factor_b)
    if paired:
        scale_row = band_scale[:, 0].transpose(1, 0, 2)[None]
        sent = jnp.concatenate([spec.reshape(rows_local, series, 2, factor_b)[: BAND + 1], scale_row])
    else:
        sent = whitened
    if paired:
        row_ids = jnp.concatenate([k1_ids[: BAND + 1], k1_ids[BAND + 1 :][::-1]])
    else:
        row_ids = k1_ids
    row_ids, turned_index = lax.optimization_barrier((row_ids, factor_b - 1 - index_b, sent))[:2]
    arrived = {}
    for distance in range(REACH, 0, -1):
        arrived[distance] = passed_along(sent, "sta", -distance)
    nearby = jnp.stack([sent] + [arrived[distance] for distance in range(1, REACH + 1)])
    slot_total = pair_blocks.shape[0]
    first_off = pair_blocks[:, 0] - owner_id
    second_off = pair_blocks[:, 1] - owner_id

    def chosen(offsets):
        pick = offsets.reshape((slot_total,) + (1,) * (nearby.ndim - 1))
        result = jnp.broadcast_to(nearby[REACH], (slot_total,) + nearby.shape[1:])
        for distance in range(REACH - 1, -1, -1):
            result = jnp.where(pick == distance, nearby[distance], result)
        return result

    def domain(block):
        if not paired:
            return block
        spec_part = block[:, : BAND + 1]
        scale_low = block[:, BAND + 1, :, 0][:, None, :, None, :]
        scale_high = block[:, BAND + 1, :, 1]
        scale_turned = scale_high[:, :, ::-1][:, None, :, None, :]
        conj_sign = (1 - 2 * lax.iota(jnp.int32, 2)).astype(jnp.float32)[None, None, None, :, None]
        low = spec_part[:, :BAND] * scale_low
        middle = spec_part[:, BAND:] * scale_high[:, None, :, None, :]
        high = spec_part[:, 1:BAND] * conj_sign * scale_turned
        return jnp.concatenate([low, middle, high], axis=1)

    spec_shape = (slot_total, rows_local, stations, hour_count, 2, factor_b)
    left_spec = domain(chosen(first_off)).reshape(spec_shape)
    right_spec = domain(chosen(second_off)).reshape(spec_shape)
    left_real = left_spec[:, :, :, None, :, 0]
    left_imag = left_spec[:, :, :, None, :, 1]
    right_real = right_spec[:, :, None, :, :, 0]
    right_imag = right_spec[:, :, None, :, :, 1]
    cross_real = jnp.sum(left_real * right_real + left_imag * right_imag, axis=4)
    cross_imag = jnp.sum(left_imag * right_real - left_real * right_imag, axis=4)
    cross = jnp.concatenate([cross_real, cross_imag], axis=-1)

    def inverse_of(cosines, sines):
        return jnp.concatenate(
            [jnp.concatenate([cosines, sines], axis=1), jnp.concatenate([-sines, cosines], axis=1)],
            axis=0,
        )

    lag_shape = (slot_total, -1, stations, stations, 2, factor_b)
    if paired:
        cosine_r, sine_r = angles(turned_index, index_b, factor_b)
        lag_low = matmul(cross[:, : BAND + 1].reshape(-1, 2 * factor_b), inverse_of(cosine_b, sine_b))
        lag_high = matmul(cross[:, BAND + 1 :].reshape(-1, 2 * factor_b), inverse_of(cosine_r, sine_r))
        lag = jnp.concatenate([lag_low.reshape(lag_shape), lag_high.reshape(lag_shape)], axis=1)
    else:
        lag = matmul(cross.reshape(-1, 2 * factor_b), inverse_of(cosine_b, sine_b)).reshape(lag_shape)
    lag_real, lag_imag = lag[:, :, :, :, 0], lag[:, :, :, :, 1]
    cosine_u, sine_u = angles(row_ids, index_b, SAMPLES)
    turn_real = lag_real * cosine_u[None, :, None, None, :] - lag_imag * sine_u[None, :, None, None, :]
    turn_imag = lag_real * sine_u[None, :, None, None, :] + lag_imag * cosine_u[None, :, None, None, :]
    lag_ids = jnp.concatenate(
        [jnp.arange(LAGS, dtype=jnp.int32), factor_a - LAGS + jnp.arange(LAGS, dtype=jnp.int32)]
    )
    cosine_l, sine_l = angles(lag_ids, row_ids, factor_a)
    lag_weights = jnp.concatenate([cosine_l, -sine_l], axis=1).reshape(
        time_devices, 2 * LAGS // time_devices, 2 * rows_local
    )
    turned = jnp.concatenate([turn_real, turn_imag], axis=1)
    scale_out = 1.0 / math.sqrt(SAMPLES * hour_count)
    live_mask = (jnp.arange(slot_total) < pair_count).astype(jnp.float32) * scale_out
    lag_block = jnp.einsum(
        "dwp,spijm->dsijwm",
        lag_weights,
        turned,
        precision=highest,
        preferred_element_type=jnp.float32,
    )
    lag_block = lag_block * live_mask[None, :, None, None, None, None]
    gathered = lax.all_to_all(
        lag_block.reshape(time_devices, -1), "tm", split_axis=0, concat_axis=0, tiled=True
    )
    total = jnp.sum(gathered, axis=0)
    return total.reshape(slot_total, stations, stations, 2 * LAGS * factor_b // time_devices)


def solution(mesh):
    placed = (P("sta", None, "tm"), P("sta", None), P("sta"))
    return jax.shard_map(local, mesh=mesh, in_specs=placed, out_specs=P("sta", None, None, "tm"), check_vma=False)
```

```python
import math

import jax
import jax.numpy as jnp
from jax import lax
from jax.sharding import PartitionSpec as P

SAMPLES = 65536
FACTOR_A = 256
BAND = 32
LAGS = 4
REACH = 3


highest = lax.Precision.HIGH
epsilon = 1e-06


def passed_along(block, axis, distance):
    devices = range(lax.axis_size(axis))
    route = [(i - distance, i) for i in devices if i - distance in devices]
    return lax.ppermute(block, axis, route)


def angles(row_ids, col_ids, modulus):
    product = row_ids[:, None] * col_ids[None, :] % modulus
    radians = product.astype(jnp.float32) * (2.0 * math.pi / modulus)
    return (jnp.cos(radians), jnp.sin(radians))


def matmul(left_mat, right_mat):
    return jnp.dot(left_mat, right_mat, precision=highest, preferred_element_type=jnp.float32)


def local(records, pair_blocks, pair_count):
    stations, hour_count, _ = records.shape
    time_devices = lax.axis_size("tm")
    time_rank = lax.axis_index("tm")
    owner_id = lax.axis_index("sta")
    factor_a = FACTOR_A
    factor_b = SAMPLES // FACTOR_A
    rows_local = factor_a // time_devices
    cols_local = factor_b // time_devices
    series = stations * hour_count
    arranged = records.reshape(series, rows_local, time_devices, cols_local).transpose(2, 1, 0, 3)
    spread = lax.all_to_all(
        arranged.reshape(time_devices, -1), "tm", split_axis=0, concat_axis=0, tiled=True
    ).reshape(factor_a, series, cols_local)
    index_a = jnp.arange(factor_a, dtype=jnp.int32)
    index_b = jnp.arange(factor_b, dtype=jnp.int32)
    paired = rows_local == 2 * BAND and factor_a == 2 * BAND * time_devices
    if paired:
        k1_ids = jnp.concatenate(
            [
                BAND * time_rank + jnp.arange(BAND, dtype=jnp.int32),
                factor_a - BAND * (time_rank + 1) + jnp.arange(BAND, dtype=jnp.int32),
            ]
        )
    else:
        k1_ids = time_rank * rows_local + jnp.arange(rows_local, dtype=jnp.int32)
    cosine_a, sine_a = angles(index_a, index_a, factor_a)
    flat_rows = spread.reshape(factor_a, series * cols_local)
    both_a = jnp.concatenate([cosine_a, -sine_a], axis=0)
    section = matmul(both_a, flat_rows).reshape(2, factor_a, series, cols_local)
    section_real, section_imag = section[0], section[1]
    col_global = time_rank * cols_local + jnp.arange(cols_local, dtype=jnp.int32)
    cosine_t, sine_t = angles(index_a, col_global, SAMPLES)
    twisted_real = section_real * cosine_t[:, None, :] + section_imag * sine_t[:, None, :]
    twisted_imag = section_imag * cosine_t[:, None, :] - section_real * sine_t[:, None, :]
    twisted = jnp.stack([twisted_real, twisted_imag], axis=2)
    if paired:
        bands = twisted.reshape(2, time_devices, BAND, series, 2, cols_local)
        grouped = jnp.stack([bands[0], bands[1][::-1]], axis=1)
        outgoing = grouped.reshape(time_devices, rows_local, series, 2, cols_local)[:, : BAND + 1]
        incoming = (
            lax.all_to_all(outgoing.reshape(time_devices, -1), "tm", split_axis=0, concat_axis=0, tiled=True)
            .reshape(time_devices, BAND + 1, series, 2, cols_local)
            .transpose(1, 2, 3, 0, 4)
            .reshape(BAND + 1, series, 2, factor_b)
        )
        unit_row = lax.optimization_barrier((jnp.ones((1,), jnp.int32), spread))[0]
        phase_cos, phase_sin = angles(unit_row, index_b, factor_b)
        source = incoming[1:BAND][::-1]
        source_real, source_imag = source[:, :, 0], source[:, :, 1]
        mirror = jnp.stack(
            [
                source_real * phase_cos - source_imag * phase_sin,
                -(source_real * phase_sin + source_imag * phase_cos),
            ],
            axis=2,
        )
        moved = jnp.concatenate([incoming, mirror])
    else:
        moved = lax.all_to_all(twisted, "tm", split_axis=0, concat_axis=3, tiled=True)
    cosine_b, sine_b = angles(index_b, index_b, factor_b)
    forward_b = jnp.concatenate(
        [jnp.concatenate([cosine_b, -sine_b], axis=1), jnp.concatenate([sine_b, cosine_b], axis=1)],
        axis=0,
    )
    spec = matmul(moved.reshape(rows_local * series, 2 * factor_b), forward_b)
    banded = spec.reshape(rows_local // BAND, BAND, series, 2, factor_b)
    band_power = jnp.mean(
        banded[:, :, :, 0] * banded[:, :, :, 0] + banded[:, :, :, 1] * banded[:, :, :, 1],
        axis=1,
        keepdims=True,
    )
    band_scale = lax.rsqrt(band_power + epsilon)
    whitened = (banded * band_scale[:, :, :, None]).reshape(rows_local, series, 2, factor_b)
    if paired:
        scale_row = band_scale[:, 0].transpose(1, 0, 2)[None]
        sent = jnp.concatenate([spec.reshape(rows_local, series, 2, factor_b)[: BAND + 1], scale_row])
    else:
        sent = whitened
    k1_ids = lax.optimization_barrier((k1_ids, sent))[0]
    arrived = {}
    for distance in range(REACH, 0, -1):
        arrived[distance] = passed_along(sent, "sta", -distance)
    nearby = jnp.stack([sent] + [arrived[distance] for distance in range(1, REACH + 1)])
    slot_total = pair_blocks.shape[0]
    first_off = pair_blocks[:, 0] - owner_id
    second_off = pair_blocks[:, 1] - owner_id

    def chosen(offsets):
        pick = offsets.reshape((slot_total,) + (1,) * (nearby.ndim - 1))
        result = jnp.broadcast_to(nearby[REACH], (slot_total,) + nearby.shape[1:])
        for distance in range(REACH - 1, -1, -1):
            result = jnp.where(pick == distance, nearby[distance], result)
        return result

    def inverse_of(cosines, sines):
        return jnp.concatenate(
            [jnp.concatenate([cosines, sines], axis=1), jnp.concatenate([-sines, cosines], axis=1)],
            axis=0,
        )

    left_block = chosen(first_off)
    right_block = chosen(second_off)
    if paired:
        kept = BAND + 1
        spec_shape = (slot_total, kept, stations, hour_count, 2, factor_b)
        scale_shape = (slot_total, stations, hour_count, factor_b)
        left_spec = left_block[:, :kept].reshape(spec_shape)
        right_spec = right_block[:, :kept].reshape(spec_shape)

        def weight(left_scale, right_scale):
            return left_scale[:, None, :, None] * right_scale[:, None, None, :]

        left_low = left_block[:, kept, :, 0].reshape(scale_shape)
        left_high = left_block[:, kept, :, 1].reshape(scale_shape)
        right_low = right_block[:, kept, :, 0].reshape(scale_shape)
        right_high = right_block[:, kept, :, 1].reshape(scale_shape)
        weight_low = weight(left_low, right_low)
        weight_high = weight(left_high, right_high)
        weight_paired = weight_low + weight(left_high[..., ::-1], right_high[..., ::-1])
        row_weight = jnp.concatenate(
            [weight_low, jnp.broadcast_to(weight_paired, (slot_total, BAND - 1) + weight_paired.shape[2:]), weight_high],
            axis=1,
        )
    else:
        kept = rows_local
        spec_shape = (slot_total, kept, stations, hour_count, 2, factor_b)
        left_spec = left_block.reshape(spec_shape)
        right_spec = right_block.reshape(spec_shape)
        row_weight = jnp.ones((1, 1, 1, 1, 1, 1), jnp.float32)
    left_real = left_spec[:, :, :, None, :, 0]
    left_imag = left_spec[:, :, :, None, :, 1]
    right_real = right_spec[:, :, None, :, :, 0]
    right_imag = right_spec[:, :, None, :, :, 1]
    cross_real = jnp.sum((left_real * right_real + left_imag * right_imag) * row_weight, axis=4)
    cross_imag = jnp.sum((left_imag * right_real - left_real * right_imag) * row_weight, axis=4)
    cross = jnp.concatenate([cross_real, cross_imag], axis=-1)
    lag = matmul(cross.reshape(-1, 2 * factor_b), inverse_of(cosine_b, sine_b)).reshape(
        slot_total, kept, stations, stations, 2, factor_b
    )
    row_ids = k1_ids[:kept]
    lag_real, lag_imag = lag[:, :, :, :, 0], lag[:, :, :, :, 1]
    cosine_u, sine_u = angles(row_ids, index_b, SAMPLES)
    turn_real = lag_real * cosine_u[None, :, None, None, :] - lag_imag * sine_u[None, :, None, None, :]
    turn_imag = lag_real * sine_u[None, :, None, None, :] + lag_imag * cosine_u[None, :, None, None, :]
    lag_ids = jnp.concatenate(
        [jnp.arange(LAGS, dtype=jnp.int32), factor_a - LAGS + jnp.arange(LAGS, dtype=jnp.int32)]
    )
    cosine_l, sine_l = angles(lag_ids, row_ids, factor_a)
    lag_weights = jnp.concatenate([cosine_l, -sine_l], axis=1).reshape(
        time_devices, 2 * LAGS // time_devices, 2 * kept
    )
    turned = jnp.concatenate([turn_real, turn_imag], axis=1)
    scale_out = 1.0 / math.sqrt(SAMPLES * hour_count)
    live_mask = (jnp.arange(slot_total) < pair_count).astype(jnp.float32) * scale_out
    lag_block = jnp.einsum(
        "dwp,spijm->dsijwm",
        lag_weights,
        turned,
        precision=highest,
        preferred_element_type=jnp.float32,
    )
    lag_block = lag_block * live_mask[None, :, None, None, None, None]
    gathered = lax.all_to_all(
        lag_block.reshape(time_devices, -1), "tm", split_axis=0, concat_axis=0, tiled=True
    )
    total = jnp.sum(gathered, axis=0)
    return total.reshape(slot_total, stations, stations, 2 * LAGS * factor_b // time_devices)


def solution(mesh):
    placed = (P("sta", None, "tm"), P("sta", None), P("sta"))
    return jax.shard_map(local, mesh=mesh, in_specs=placed, out_specs=P("sta", None, None, "tm"), check_vma=False)
```

```python
import math

import jax
import jax.numpy as jnp
from jax import lax
from jax.sharding import PartitionSpec as P

SAMPLES = 65536
FACTOR_A = 256
BAND = 32
LAGS = 4
REACH = 3


highest = lax.Precision.HIGH
epsilon = 1e-06


def passed_along(block, axis, distance):
    devices = range(lax.axis_size(axis))
    route = [(i - distance, i) for i in devices if i - distance in devices]
    return lax.ppermute(block, axis, route)


def angles(row_ids, col_ids, modulus):
    product = row_ids[:, None] * col_ids[None, :] % modulus
    radians = product.astype(jnp.float32) * (2.0 * math.pi / modulus)
    return (jnp.cos(radians), jnp.sin(radians))


def matmul(left_mat, right_mat):
    return jnp.dot(left_mat, right_mat, precision=highest, preferred_element_type=jnp.float32)


def local(records, pair_blocks, pair_count):
    stations, hour_count, _ = records.shape
    time_devices = lax.axis_size("tm")
    time_rank = lax.axis_index("tm")
    owner_id = lax.axis_index("sta")
    factor_a = FACTOR_A
    factor_b = SAMPLES // FACTOR_A
    rows_local = factor_a // time_devices
    cols_local = factor_b // time_devices
    series = stations * hour_count
    arranged = records.reshape(series, rows_local, time_devices, cols_local).transpose(2, 1, 0, 3)
    spread = lax.all_to_all(
        arranged.reshape(time_devices, -1), "tm", split_axis=0, concat_axis=0, tiled=True
    ).reshape(factor_a, series, cols_local)
    index_a = jnp.arange(factor_a, dtype=jnp.int32)
    index_b = jnp.arange(factor_b, dtype=jnp.int32)
    paired = rows_local == 2 * BAND and factor_a == 2 * BAND * time_devices
    if paired:
        k1_ids = jnp.concatenate(
            [
                BAND * time_rank + jnp.arange(BAND, dtype=jnp.int32),
                factor_a - BAND * (time_rank + 1) + jnp.arange(BAND, dtype=jnp.int32),
            ]
        )
    else:
        k1_ids = time_rank * rows_local + jnp.arange(rows_local, dtype=jnp.int32)
    cosine_a, sine_a = angles(index_a, index_a, factor_a)
    flat_rows = spread.reshape(factor_a, series * cols_local)
    both_a = jnp.concatenate([cosine_a, -sine_a], axis=0)
    section = matmul(both_a, flat_rows).reshape(2, factor_a, series, cols_local)
    section_real, section_imag = section[0], section[1]
    col_global = time_rank * cols_local + jnp.arange(cols_local, dtype=jnp.int32)
    cosine_t, sine_t = angles(index_a, col_global, SAMPLES)
    twisted_real = section_real * cosine_t[:, None, :] + section_imag * sine_t[:, None, :]
    twisted_imag = section_imag * cosine_t[:, None, :] - section_real * sine_t[:, None, :]
    twisted = jnp.stack([twisted_real, twisted_imag], axis=2)
    if paired:
        bands = twisted.reshape(2, time_devices, BAND, series, 2, cols_local)
        grouped = jnp.stack([bands[0], bands[1][::-1]], axis=1)
        outgoing = grouped.reshape(time_devices, rows_local, series, 2, cols_local)[:, : BAND + 1]
        incoming = (
            lax.all_to_all(outgoing.reshape(time_devices, -1), "tm", split_axis=0, concat_axis=0, tiled=True)
            .reshape(time_devices, BAND + 1, series, 2, cols_local)
            .transpose(1, 2, 3, 0, 4)
            .reshape(BAND + 1, series, 2, factor_b)
        )
    else:
        moved = lax.all_to_all(twisted, "tm", split_axis=0, concat_axis=3, tiled=True)
    cosine_b, sine_b = angles(index_b, index_b, factor_b)
    forward_b = jnp.concatenate(
        [jnp.concatenate([cosine_b, -sine_b], axis=1), jnp.concatenate([sine_b, cosine_b], axis=1)],
        axis=0,
    )
    if paired:
        spec = matmul(incoming.reshape((BAND + 1) * series, 2 * factor_b), forward_b).reshape(
            BAND + 1, series, 2, factor_b
        )
        energy = spec[:, :, 0] * spec[:, :, 0] + spec[:, :, 1] * spec[:, :, 1]
        power_low = jnp.mean(energy[:BAND], axis=0)
        power_high = (energy[BAND] + jnp.sum(energy[1:BAND], axis=0)[:, ::-1]) / BAND
        scale_row = lax.rsqrt(jnp.stack([power_low, power_high], axis=1) + epsilon)[None]
        sent = jnp.concatenate([spec, scale_row])
    else:
        spec = matmul(moved.reshape(rows_local * series, 2 * factor_b), forward_b)
        banded = spec.reshape(rows_local // BAND, BAND, series, 2, factor_b)
        band_power = jnp.mean(
            banded[:, :, :, 0] * banded[:, :, :, 0] + banded[:, :, :, 1] * banded[:, :, :, 1],
            axis=1,
            keepdims=True,
        )
        band_scale = lax.rsqrt(band_power + epsilon)
        sent = (banded * band_scale[:, :, :, None]).reshape(rows_local, series, 2, factor_b)
    k1_ids = lax.optimization_barrier((k1_ids, sent))[0]
    arrived = {}
    for distance in range(REACH, 0, -1):
        arrived[distance] = passed_along(sent.reshape(-1, factor_b), "sta", -distance).reshape(sent.shape)
    nearby = jnp.stack([sent] + [arrived[distance] for distance in range(1, REACH + 1)])
    slot_total = pair_blocks.shape[0]
    first_off = pair_blocks[:, 0] - owner_id
    second_off = pair_blocks[:, 1] - owner_id

    def chosen(offsets):
        pick = offsets.reshape((slot_total,) + (1,) * (nearby.ndim - 1))
        result = jnp.broadcast_to(nearby[REACH], (slot_total,) + nearby.shape[1:])
        for distance in range(REACH - 1, -1, -1):
            result = jnp.where(pick == distance, nearby[distance], result)
        return result

    def inverse_of(cosines, sines):
        return jnp.concatenate(
            [jnp.concatenate([cosines, sines], axis=1), jnp.concatenate([-sines, cosines], axis=1)],
            axis=0,
        )

    left_block = chosen(first_off)
    right_block = chosen(second_off)
    if paired:
        kept = BAND + 1
        spec_shape = (slot_total, kept, stations, hour_count, 2, factor_b)
        scale_shape = (slot_total, stations, hour_count, factor_b)
        left_spec = left_block[:, :kept].reshape(spec_shape)
        right_spec = right_block[:, :kept].reshape(spec_shape)

        def weight(left_scale, right_scale):
            return left_scale[:, None, :, None] * right_scale[:, None, None, :]

        left_low = left_block[:, kept, :, 0].reshape(scale_shape)
        left_high = left_block[:, kept, :, 1].reshape(scale_shape)
        right_low = right_block[:, kept, :, 0].reshape(scale_shape)
        right_high = right_block[:, kept, :, 1].reshape(scale_shape)
        weight_low = weight(left_low, right_low)
        weight_high = weight(left_high, right_high)
        weight_paired = weight_low + weight(left_high[..., ::-1], right_high[..., ::-1])
        row_weight = jnp.concatenate(
            [weight_low, jnp.broadcast_to(weight_paired, (slot_total, BAND - 1) + weight_paired.shape[2:]), weight_high],
            axis=1,
        )
    else:
        kept = rows_local
        spec_shape = (slot_total, kept, stations, hour_count, 2, factor_b)
        left_spec = left_block.reshape(spec_shape)
        right_spec = right_block.reshape(spec_shape)
        row_weight = jnp.ones((1, 1, 1, 1, 1, 1), jnp.float32)
    left_real = left_spec[:, :, :, None, :, 0]
    left_imag = left_spec[:, :, :, None, :, 1]
    right_real = right_spec[:, :, None, :, :, 0]
    right_imag = right_spec[:, :, None, :, :, 1]
    cross_real = jnp.sum((left_real * right_real + left_imag * right_imag) * row_weight, axis=4)
    cross_imag = jnp.sum((left_imag * right_real - left_real * right_imag) * row_weight, axis=4)
    cross = jnp.concatenate([cross_real, cross_imag], axis=-1)
    lag = matmul(cross.reshape(-1, 2 * factor_b), inverse_of(cosine_b, sine_b)).reshape(
        slot_total, kept, stations, stations, 2, factor_b
    )
    row_ids = k1_ids[:kept]
    lag_real, lag_imag = lag[:, :, :, :, 0], lag[:, :, :, :, 1]
    cosine_u, sine_u = angles(row_ids, index_b, SAMPLES)
    turn_real = lag_real * cosine_u[None, :, None, None, :] - lag_imag * sine_u[None, :, None, None, :]
    turn_imag = lag_real * sine_u[None, :, None, None, :] + lag_imag * cosine_u[None, :, None, None, :]
    lag_ids = jnp.concatenate(
        [jnp.arange(LAGS, dtype=jnp.int32), factor_a - LAGS + jnp.arange(LAGS, dtype=jnp.int32)]
    )
    cosine_l, sine_l = angles(lag_ids, row_ids, factor_a)
    lag_weights = jnp.concatenate([cosine_l, -sine_l], axis=1).reshape(
        time_devices, 2 * LAGS // time_devices, 2 * kept
    )
    turned = jnp.concatenate([turn_real, turn_imag], axis=1)
    scale_out = 1.0 / math.sqrt(SAMPLES * hour_count)
    live_mask = (jnp.arange(slot_total) < pair_count).astype(jnp.float32) * scale_out
    lag_block = jnp.einsum(
        "dwp,spijm->dsijwm",
        lag_weights,
        turned,
        precision=highest,
        preferred_element_type=jnp.float32,
    )
    lag_block = lag_block * live_mask[None, :, None, None, None, None]
    gathered = lax.all_to_all(
        lag_block.reshape(time_devices, -1), "tm", split_axis=0, concat_axis=0, tiled=True
    )
    total = jnp.sum(gathered, axis=0)
    return total.reshape(slot_total, stations, stations, 2 * LAGS * factor_b // time_devices)


def solution(mesh):
    placed = (P("sta", None, "tm"), P("sta", None), P("sta"))
    return jax.shard_map(local, mesh=mesh, in_specs=placed, out_specs=P("sta", None, None, "tm"), check_vma=False)
```

```python
import math

import jax
import jax.numpy as jnp
from jax import lax
from jax.sharding import PartitionSpec as P

SAMPLES = 65536
FACTOR_A = 256
BAND = 32
LAGS = 4
REACH = 3


highest = lax.Precision.HIGH
epsilon = 1e-06


def passed_along(block, axis, distance):
    devices = range(lax.axis_size(axis))
    route = [(i - distance, i) for i in devices if i - distance in devices]
    return lax.ppermute(block, axis, route)


def angles(row_ids, col_ids, modulus):
    product = row_ids[:, None] * col_ids[None, :] % modulus
    radians = product.astype(jnp.float32) * (2.0 * math.pi / modulus)
    return (jnp.cos(radians), jnp.sin(radians))


def matmul(left_mat, right_mat):
    return jnp.dot(left_mat, right_mat, precision=highest, preferred_element_type=jnp.float32)


def local(records, pair_blocks, pair_count):
    stations, hour_count, _ = records.shape
    time_devices = lax.axis_size("tm")
    time_rank = lax.axis_index("tm")
    owner_id = lax.axis_index("sta")
    factor_a = FACTOR_A
    factor_b = SAMPLES // FACTOR_A
    rows_local = factor_a // time_devices
    cols_local = factor_b // time_devices
    series = stations * hour_count
    arranged = records.reshape(series, rows_local, time_devices, cols_local).transpose(2, 1, 0, 3)
    spread = lax.all_to_all(
        arranged.reshape(time_devices, -1), "tm", split_axis=0, concat_axis=0, tiled=True
    ).reshape(factor_a, series, cols_local)
    index_a = jnp.arange(factor_a, dtype=jnp.int32)
    index_b = jnp.arange(factor_b, dtype=jnp.int32)
    paired = rows_local == 2 * BAND and factor_a == 2 * BAND * time_devices
    if paired:
        k1_ids = jnp.concatenate(
            [
                BAND * time_rank + jnp.arange(BAND, dtype=jnp.int32),
                factor_a - BAND * (time_rank + 1) + jnp.arange(BAND, dtype=jnp.int32),
            ]
        )
    else:
        k1_ids = time_rank * rows_local + jnp.arange(rows_local, dtype=jnp.int32)
    cosine_a, sine_a = angles(index_a, index_a, factor_a)
    flat_rows = spread.reshape(factor_a, series * cols_local)
    both_a = jnp.concatenate([cosine_a, -sine_a], axis=0)
    section = matmul(both_a, flat_rows).reshape(2, factor_a, series, cols_local)
    section_real, section_imag = section[0], section[1]
    col_global = time_rank * cols_local + jnp.arange(cols_local, dtype=jnp.int32)
    cosine_t, sine_t = angles(index_a, col_global, SAMPLES)
    twisted_real = section_real * cosine_t[:, None, :] + section_imag * sine_t[:, None, :]
    twisted_imag = section_imag * cosine_t[:, None, :] - section_real * sine_t[:, None, :]
    twisted = jnp.stack([twisted_real, twisted_imag], axis=2)
    if paired:
        bands = twisted.reshape(2, time_devices, BAND, series, 2, cols_local)
        grouped = jnp.stack([bands[0], bands[1][::-1]], axis=1)
        outgoing = grouped.reshape(time_devices, rows_local, series, 2, cols_local)[:, : BAND + 1]
        incoming = (
            lax.all_to_all(outgoing.reshape(time_devices, -1), "tm", split_axis=0, concat_axis=0, tiled=True)
            .reshape(time_devices, BAND + 1, series, 2, cols_local)
            .transpose(1, 2, 3, 0, 4)
            .reshape(BAND + 1, series, 2, factor_b)
        )
    else:
        moved = lax.all_to_all(twisted, "tm", split_axis=0, concat_axis=3, tiled=True)
    cosine_b, sine_b = angles(index_b, index_b, factor_b)
    forward_b = jnp.concatenate(
        [jnp.concatenate([cosine_b, -sine_b], axis=1), jnp.concatenate([sine_b, cosine_b], axis=1)],
        axis=0,
    )
    if paired:
        spec = matmul(incoming.reshape((BAND + 1) * series, 2 * factor_b), forward_b).reshape(
            BAND + 1, series, 2, factor_b
        )
        energy = spec[:, :, 0] * spec[:, :, 0] + spec[:, :, 1] * spec[:, :, 1]
        power_low = jnp.mean(energy[:BAND], axis=0)
        power_high = (energy[BAND] + jnp.sum(energy[1:BAND], axis=0)[:, ::-1]) / BAND
        scale_low = lax.rsqrt(power_low + epsilon)
        scale_high = lax.rsqrt(power_high + epsilon)
        scale_row = jnp.stack([scale_low, scale_high[:, ::-1]], axis=1)[None]
        sent = jnp.concatenate(
            [
                spec[:1] * scale_low[None, :, None, :],
                spec[1:BAND],
                spec[BAND:] * scale_high[None, :, None, :],
                scale_row,
            ]
        )
    else:
        spec = matmul(moved.reshape(rows_local * series, 2 * factor_b), forward_b)
        banded = spec.reshape(rows_local // BAND, BAND, series, 2, factor_b)
        band_power = jnp.mean(
            banded[:, :, :, 0] * banded[:, :, :, 0] + banded[:, :, :, 1] * banded[:, :, :, 1],
            axis=1,
            keepdims=True,
        )
        band_scale = lax.rsqrt(band_power + epsilon)
        sent = (banded * band_scale[:, :, :, None]).reshape(rows_local, series, 2, factor_b)
    k1_ids = lax.optimization_barrier((k1_ids, sent))[0]
    arrived = {}
    for distance in range(REACH, 0, -1):
        arrived[distance] = passed_along(sent.reshape(-1, factor_b), "sta", -distance).reshape(sent.shape)
    nearby = jnp.stack([sent] + [arrived[distance] for distance in range(1, REACH + 1)])
    slot_total = pair_blocks.shape[0]
    first_off = pair_blocks[:, 0] - owner_id
    second_off = pair_blocks[:, 1] - owner_id

    def chosen(offsets):
        pick = offsets.reshape((slot_total,) + (1,) * (nearby.ndim - 1))
        result = jnp.broadcast_to(nearby[REACH], (slot_total,) + nearby.shape[1:])
        for distance in range(REACH - 1, -1, -1):
            result = jnp.where(pick == distance, nearby[distance], result)
        return result

    def inverse_of(cosines, sines):
        return jnp.concatenate(
            [jnp.concatenate([cosines, sines], axis=1), jnp.concatenate([-sines, cosines], axis=1)],
            axis=0,
        )

    left_block = chosen(first_off)
    right_block = chosen(second_off)
    if paired:
        kept = BAND + 1
        spec_shape = (slot_total, kept, stations, hour_count, 2, factor_b)
        scale_shape = (slot_total, stations, hour_count, factor_b)
        left_spec = left_block[:, :kept].reshape(spec_shape)
        right_spec = right_block[:, :kept].reshape(spec_shape)

        def weight(left_scale, right_scale):
            return left_scale[:, None, :, None] * right_scale[:, None, None, :]

        left_low = left_block[:, kept, :, 0].reshape(scale_shape)
        left_turned = left_block[:, kept, :, 1].reshape(scale_shape)
        right_low = right_block[:, kept, :, 0].reshape(scale_shape)
        right_turned = right_block[:, kept, :, 1].reshape(scale_shape)
        weight_paired = weight(left_low, right_low) + weight(left_turned, right_turned)
        single = jnp.ones((slot_total, 1) + weight_paired.shape[2:], jnp.float32)
        row_weight = jnp.concatenate(
            [single, jnp.broadcast_to(weight_paired, (slot_total, BAND - 1) + weight_paired.shape[2:]), single],
            axis=1,
        )
    else:
        kept = rows_local
        spec_shape = (slot_total, kept, stations, hour_count, 2, factor_b)
        left_spec = left_block.reshape(spec_shape)
        right_spec = right_block.reshape(spec_shape)
        row_weight = jnp.ones((1, 1, 1, 1, 1, 1), jnp.float32)
    left_real = left_spec[:, :, :, None, :, 0]
    left_imag = left_spec[:, :, :, None, :, 1]
    right_real = right_spec[:, :, None, :, :, 0]
    right_imag = right_spec[:, :, None, :, :, 1]
    cross_real = jnp.sum((left_real * right_real + left_imag * right_imag) * row_weight, axis=4)
    cross_imag = jnp.sum((left_imag * right_real - left_real * right_imag) * row_weight, axis=4)
    cross = jnp.concatenate([cross_real, cross_imag], axis=-1)
    lag = matmul(cross.reshape(-1, 2 * factor_b), inverse_of(cosine_b, sine_b)).reshape(
        slot_total, kept, stations, stations, 2, factor_b
    )
    row_ids = k1_ids[:kept]
    lag_real, lag_imag = lag[:, :, :, :, 0], lag[:, :, :, :, 1]
    cosine_u, sine_u = angles(row_ids, index_b, SAMPLES)
    turn_real = lag_real * cosine_u[None, :, None, None, :] - lag_imag * sine_u[None, :, None, None, :]
    turn_imag = lag_real * sine_u[None, :, None, None, :] + lag_imag * cosine_u[None, :, None, None, :]
    lag_ids = jnp.concatenate(
        [jnp.arange(LAGS, dtype=jnp.int32), factor_a - LAGS + jnp.arange(LAGS, dtype=jnp.int32)]
    )
    cosine_l, sine_l = angles(lag_ids, row_ids, factor_a)
    lag_weights = jnp.concatenate([cosine_l, -sine_l], axis=1).reshape(
        time_devices, 2 * LAGS // time_devices, 2 * kept
    )
    turned = jnp.concatenate([turn_real, turn_imag], axis=1)
    scale_out = 1.0 / math.sqrt(SAMPLES * hour_count)
    live_mask = (jnp.arange(slot_total) < pair_count).astype(jnp.float32) * scale_out
    lag_block = jnp.einsum(
        "dwp,spijm->dsijwm",
        lag_weights,
        turned,
        precision=highest,
        preferred_element_type=jnp.float32,
    )
    lag_block = lag_block * live_mask[None, :, None, None, None, None]
    gathered = lax.all_to_all(
        lag_block.reshape(time_devices, -1), "tm", split_axis=0, concat_axis=0, tiled=True
    )
    total = jnp.sum(gathered, axis=0)
    return total.reshape(slot_total, stations, stations, 2 * LAGS * factor_b // time_devices)


def solution(mesh):
    placed = (P("sta", None, "tm"), P("sta", None), P("sta"))
    return jax.shard_map(local, mesh=mesh, in_specs=placed, out_specs=P("sta", None, None, "tm"), check_vma=False)
```

```python
import math

import jax
import jax.numpy as jnp
from jax import lax
from jax.sharding import PartitionSpec as P

SAMPLES = 65536
FACTOR_A = 256
BAND = 32
LAGS = 4
REACH = 3


highest = lax.Precision.HIGH
epsilon = 1e-06


def passed_along(block, axis, distance):
    devices = range(lax.axis_size(axis))
    route = [(i - distance, i) for i in devices if i - distance in devices]
    return lax.ppermute(block, axis, route)


def angles(row_ids, col_ids, modulus):
    product = row_ids[:, None] * col_ids[None, :] % modulus
    radians = product.astype(jnp.float32) * (2.0 * math.pi / modulus)
    return (jnp.cos(radians), jnp.sin(radians))


def matmul(left_mat, right_mat):
    return jnp.dot(left_mat, right_mat, precision=highest, preferred_element_type=jnp.float32)


def local(records, pair_blocks, pair_count):
    stations, hour_count, _ = records.shape
    time_devices = lax.axis_size("tm")
    time_rank = lax.axis_index("tm")
    owner_id = lax.axis_index("sta")
    factor_a = FACTOR_A
    factor_b = SAMPLES // FACTOR_A
    rows_local = factor_a // time_devices
    cols_local = factor_b // time_devices
    series = stations * hour_count
    arranged = records.reshape(series, rows_local, time_devices, cols_local).transpose(2, 1, 0, 3)
    spread = lax.all_to_all(
        arranged.reshape(time_devices, -1), "tm", split_axis=0, concat_axis=0, tiled=True
    ).reshape(factor_a, series, cols_local)
    index_a = jnp.arange(factor_a, dtype=jnp.int32)
    index_b = jnp.arange(factor_b, dtype=jnp.int32)
    paired = rows_local == 2 * BAND and factor_a == 2 * BAND * time_devices
    if paired:
        k1_ids = jnp.concatenate(
            [
                BAND * time_rank + jnp.arange(BAND, dtype=jnp.int32),
                factor_a - BAND * (time_rank + 1) + jnp.arange(BAND, dtype=jnp.int32),
            ]
        )
    else:
        k1_ids = time_rank * rows_local + jnp.arange(rows_local, dtype=jnp.int32)
    cosine_a, sine_a = angles(index_a, index_a, factor_a)
    flat_rows = spread.reshape(factor_a, series * cols_local)
    both_a = jnp.concatenate([cosine_a, -sine_a], axis=0)
    section = matmul(both_a, flat_rows).reshape(2, factor_a, series, cols_local)
    section_real, section_imag = section[0], section[1]
    col_global = time_rank * cols_local + jnp.arange(cols_local, dtype=jnp.int32)
    cosine_t, sine_t = angles(index_a, col_global, SAMPLES)
    twisted_real = section_real * cosine_t[:, None, :] + section_imag * sine_t[:, None, :]
    twisted_imag = section_imag * cosine_t[:, None, :] - section_real * sine_t[:, None, :]
    twisted = jnp.stack([twisted_real, twisted_imag], axis=2)
    if paired:
        bands = twisted.reshape(2, time_devices, BAND, series, 2, cols_local)
        grouped = jnp.stack([bands[0], bands[1][::-1]], axis=1)
        outgoing = grouped.reshape(time_devices, rows_local, series, 2, cols_local)[:, : BAND + 1]
        incoming = (
            lax.all_to_all(outgoing.reshape(time_devices, -1), "tm", split_axis=0, concat_axis=0, tiled=True)
            .reshape(time_devices, BAND + 1, series, 2, cols_local)
            .transpose(1, 2, 3, 0, 4)
            .reshape(BAND + 1, series, 2, factor_b)
        )
    else:
        moved = lax.all_to_all(twisted, "tm", split_axis=0, concat_axis=3, tiled=True)
    cosine_b, sine_b = angles(index_b, index_b, factor_b)
    forward_b = jnp.concatenate(
        [jnp.concatenate([cosine_b, -sine_b], axis=1), jnp.concatenate([sine_b, cosine_b], axis=1)],
        axis=0,
    )
    if paired:
        spec = matmul(incoming.reshape((BAND + 1) * series, 2 * factor_b), forward_b).reshape(
            BAND + 1, series, 2, factor_b
        )
        energy = spec[:, :, 0] * spec[:, :, 0] + spec[:, :, 1] * spec[:, :, 1]
        power_low = jnp.mean(energy[:BAND], axis=0)
        power_high = (energy[BAND] + jnp.sum(energy[1:BAND], axis=0)[:, ::-1]) / BAND
        scale_low = lax.rsqrt(power_low + epsilon)
        scale_high = lax.rsqrt(power_high + epsilon)
        scale_row = jnp.stack([scale_low, scale_high[:, ::-1]], axis=1)[None]
        sent = jnp.concatenate(
            [
                spec[:1] * scale_low[None, :, None, :],
                spec[1:BAND],
                spec[BAND:] * scale_high[None, :, None, :],
                scale_row,
            ]
        )
    else:
        spec = matmul(moved.reshape(rows_local * series, 2 * factor_b), forward_b)
        banded = spec.reshape(rows_local // BAND, BAND, series, 2, factor_b)
        band_power = jnp.mean(
            banded[:, :, :, 0] * banded[:, :, :, 0] + banded[:, :, :, 1] * banded[:, :, :, 1],
            axis=1,
            keepdims=True,
        )
        band_scale = lax.rsqrt(band_power + epsilon)
        sent = (banded * band_scale[:, :, :, None]).reshape(rows_local, series, 2, factor_b)
    k1_ids = lax.optimization_barrier((k1_ids, sent))[0]
    flat_sent = sent.reshape(-1, factor_b)
    near = passed_along(flat_sent, "sta", -1)
    relayed = passed_along(jnp.concatenate([flat_sent, near]), "sta", -2)
    arrived = {1: near, 2: relayed[: flat_sent.shape[0]], 3: relayed[flat_sent.shape[0] :]}
    arrived = {distance: piece.reshape(sent.shape) for distance, piece in arrived.items()}
    nearby = jnp.stack([sent] + [arrived[distance] for distance in range(1, REACH + 1)])
    slot_total = pair_blocks.shape[0]
    first_off = pair_blocks[:, 0] - owner_id
    second_off = pair_blocks[:, 1] - owner_id

    def chosen(offsets):
        pick = offsets.reshape((slot_total,) + (1,) * (nearby.ndim - 1))
        result = jnp.broadcast_to(nearby[REACH], (slot_total,) + nearby.shape[1:])
        for distance in range(REACH - 1, -1, -1):
            result = jnp.where(pick == distance, nearby[distance], result)
        return result

    def inverse_of(cosines, sines):
        return jnp.concatenate(
            [jnp.concatenate([cosines, sines], axis=1), jnp.concatenate([-sines, cosines], axis=1)],
            axis=0,
        )

    left_block = chosen(first_off)
    right_block = chosen(second_off)
    if paired:
        kept = BAND + 1
        spec_shape = (slot_total, kept, stations, hour_count, 2, factor_b)
        scale_shape = (slot_total, stations, hour_count, factor_b)
        left_spec = left_block[:, :kept].reshape(spec_shape)
        right_spec = right_block[:, :kept].reshape(spec_shape)

        def weight(left_scale, right_scale):
            return left_scale[:, None, :, None] * right_scale[:, None, None, :]

        left_low = left_block[:, kept, :, 0].reshape(scale_shape)
        left_turned = left_block[:, kept, :, 1].reshape(scale_shape)
        right_low = right_block[:, kept, :, 0].reshape(scale_shape)
        right_turned = right_block[:, kept, :, 1].reshape(scale_shape)
        weight_paired = weight(left_low, right_low) + weight(left_turned, right_turned)
        single = jnp.ones((slot_total, 1) + weight_paired.shape[2:], jnp.float32)
        row_weight = jnp.concatenate(
            [single, jnp.broadcast_to(weight_paired, (slot_total, BAND - 1) + weight_paired.shape[2:]), single],
            axis=1,
        )
    else:
        kept = rows_local
        spec_shape = (slot_total, kept, stations, hour_count, 2, factor_b)
        left_spec = left_block.reshape(spec_shape)
        right_spec = right_block.reshape(spec_shape)
        row_weight = jnp.ones((1, 1, 1, 1, 1, 1), jnp.float32)
    left_real = left_spec[:, :, :, None, :, 0]
    left_imag = left_spec[:, :, :, None, :, 1]
    right_real = right_spec[:, :, None, :, :, 0]
    right_imag = right_spec[:, :, None, :, :, 1]
    cross_real = jnp.sum((left_real * right_real + left_imag * right_imag) * row_weight, axis=4)
    cross_imag = jnp.sum((left_imag * right_real - left_real * right_imag) * row_weight, axis=4)
    cross = jnp.concatenate([cross_real, cross_imag], axis=-1)
    lag = matmul(cross.reshape(-1, 2 * factor_b), inverse_of(cosine_b, sine_b)).reshape(
        slot_total, kept, stations, stations, 2, factor_b
    )
    row_ids = k1_ids[:kept]
    lag_real, lag_imag = lag[:, :, :, :, 0], lag[:, :, :, :, 1]
    cosine_u, sine_u = angles(row_ids, index_b, SAMPLES)
    turn_real = lag_real * cosine_u[None, :, None, None, :] - lag_imag * sine_u[None, :, None, None, :]
    turn_imag = lag_real * sine_u[None, :, None, None, :] + lag_imag * cosine_u[None, :, None, None, :]
    lag_ids = jnp.concatenate(
        [jnp.arange(LAGS, dtype=jnp.int32), factor_a - LAGS + jnp.arange(LAGS, dtype=jnp.int32)]
    )
    cosine_l, sine_l = angles(lag_ids, row_ids, factor_a)
    lag_weights = jnp.concatenate([cosine_l, -sine_l], axis=1).reshape(
        time_devices, 2 * LAGS // time_devices, 2 * kept
    )
    turned = jnp.concatenate([turn_real, turn_imag], axis=1)
    scale_out = 1.0 / math.sqrt(SAMPLES * hour_count)
    live_mask = (jnp.arange(slot_total) < pair_count).astype(jnp.float32) * scale_out
    lag_block = jnp.einsum(
        "dwp,spijm->dsijwm",
        lag_weights,
        turned,
        precision=highest,
        preferred_element_type=jnp.float32,
    )
    lag_block = lag_block * live_mask[None, :, None, None, None, None]
    gathered = lax.all_to_all(
        lag_block.reshape(time_devices, -1), "tm", split_axis=0, concat_axis=0, tiled=True
    )
    total = jnp.sum(gathered, axis=0)
    return total.reshape(slot_total, stations, stations, 2 * LAGS * factor_b // time_devices)


def solution(mesh):
    placed = (P("sta", None, "tm"), P("sta", None), P("sta"))
    return jax.shard_map(
        local, mesh=mesh, in_specs=placed, out_specs=P("sta", None, None, "tm"), check_vma=False
    )
```

```python
import math

import jax
import jax.numpy as jnp
from jax import lax
from jax.sharding import PartitionSpec as P

SAMPLES = 65536
FACTOR_A = 256
BAND = 32
LAGS = 4
REACH = 3


highest = lax.Precision.HIGH
epsilon = 1e-06


def passed_along(block, axis, distance):
    devices = range(lax.axis_size(axis))
    route = [(i - distance, i) for i in devices if i - distance in devices]
    return lax.ppermute(block, axis, route)


def angles(row_ids, col_ids, modulus):
    product = row_ids[:, None] * col_ids[None, :] % modulus
    radians = product.astype(jnp.float32) * (2.0 * math.pi / modulus)
    return (jnp.cos(radians), jnp.sin(radians))


def matmul(left_mat, right_mat):
    return jnp.dot(left_mat, right_mat, precision=highest, preferred_element_type=jnp.float32)


def local(records, pair_blocks, pair_count):
    stations, hour_count, _ = records.shape
    time_devices = lax.axis_size("tm")
    time_rank = lax.axis_index("tm")
    owner_id = lax.axis_index("sta")
    factor_a = FACTOR_A
    factor_b = SAMPLES // FACTOR_A
    rows_local = factor_a // time_devices
    cols_local = factor_b // time_devices
    series = stations * hour_count
    arranged = records.reshape(series, rows_local, time_devices, cols_local).transpose(2, 1, 0, 3)
    spread = lax.all_to_all(
        arranged.reshape(time_devices, -1), "tm", split_axis=0, concat_axis=0, tiled=True
    ).reshape(factor_a, series, cols_local)
    index_a = jnp.arange(factor_a, dtype=jnp.int32)
    index_b = jnp.arange(factor_b, dtype=jnp.int32)
    paired = rows_local == 2 * BAND and factor_a == 2 * BAND * time_devices
    if paired:
        k1_ids = jnp.concatenate(
            [
                BAND * time_rank + jnp.arange(BAND, dtype=jnp.int32),
                factor_a - BAND * (time_rank + 1) + jnp.arange(BAND, dtype=jnp.int32),
            ]
        )
    else:
        k1_ids = time_rank * rows_local + jnp.arange(rows_local, dtype=jnp.int32)
    cosine_a, sine_a = angles(index_a, index_a, factor_a)
    flat_rows = spread.reshape(factor_a, series * cols_local)
    both_a = jnp.concatenate([cosine_a, -sine_a], axis=0)
    section = matmul(both_a, flat_rows).reshape(2, factor_a, series, cols_local)
    section_real, section_imag = section[0], section[1]
    col_global = time_rank * cols_local + jnp.arange(cols_local, dtype=jnp.int32)
    cosine_t, sine_t = angles(index_a, col_global, SAMPLES)
    twisted_real = section_real * cosine_t[:, None, :] + section_imag * sine_t[:, None, :]
    twisted_imag = section_imag * cosine_t[:, None, :] - section_real * sine_t[:, None, :]
    twisted = jnp.stack([twisted_real, twisted_imag], axis=2)
    if paired:
        bands = twisted.reshape(2, time_devices, BAND, series, 2, cols_local)
        grouped = jnp.stack([bands[0], bands[1][::-1]], axis=1)
        outgoing = grouped.reshape(time_devices, rows_local, series, 2, cols_local)[:, : BAND + 1]
        incoming = (
            lax.all_to_all(outgoing.reshape(time_devices, -1), "tm", split_axis=0, concat_axis=0, tiled=True)
            .reshape(time_devices, BAND + 1, series, 2, cols_local)
            .transpose(1, 2, 3, 0, 4)
            .reshape(BAND + 1, series, 2, factor_b)
        )
    else:
        moved = lax.all_to_all(twisted, "tm", split_axis=0, concat_axis=3, tiled=True)
    cosine_b, sine_b = angles(index_b, index_b, factor_b)
    forward_b = jnp.concatenate(
        [jnp.concatenate([cosine_b, -sine_b], axis=1), jnp.concatenate([sine_b, cosine_b], axis=1)],
        axis=0,
    )
    if paired:
        spec = matmul(incoming.reshape((BAND + 1) * series, 2 * factor_b), forward_b).reshape(
            BAND + 1, series, 2, factor_b
        )
        energy = spec[:, :, 0] * spec[:, :, 0] + spec[:, :, 1] * spec[:, :, 1]
        power_low = jnp.mean(energy[:BAND], axis=0)
        power_high = (energy[BAND] + jnp.sum(energy[1:BAND], axis=0)[:, ::-1]) / BAND
        scale_low = lax.rsqrt(power_low + epsilon)
        scale_high = lax.rsqrt(power_high + epsilon)
        scale_row = jnp.stack([scale_low, scale_high[:, ::-1]], axis=1)[None]
        sent = jnp.concatenate(
            [
                spec[:1] * scale_low[None, :, None, :],
                spec[1:BAND],
                spec[BAND:] * scale_high[None, :, None, :],
                scale_row,
            ]
        )
    else:
        spec = matmul(moved.reshape(rows_local * series, 2 * factor_b), forward_b)
        banded = spec.reshape(rows_local // BAND, BAND, series, 2, factor_b)
        band_power = jnp.mean(
            banded[:, :, :, 0] * banded[:, :, :, 0] + banded[:, :, :, 1] * banded[:, :, :, 1],
            axis=1,
            keepdims=True,
        )
        band_scale = lax.rsqrt(band_power + epsilon)
        sent = (banded * band_scale[:, :, :, None]).reshape(rows_local, series, 2, factor_b)
    k1_ids = lax.optimization_barrier((k1_ids, sent))[0]
    arrived = {}
    for distance in range(REACH, 0, -1):
        arrived[distance] = passed_along(sent.reshape(-1, factor_b), "sta", -distance).reshape(sent.shape)
    nearby = jnp.stack([sent] + [arrived[distance] for distance in range(1, REACH + 1)])
    slot_total = pair_blocks.shape[0]
    first_off = pair_blocks[:, 0] - owner_id
    second_off = pair_blocks[:, 1] - owner_id

    def chosen(offsets):
        pick = offsets.reshape((slot_total,) + (1,) * (nearby.ndim - 1))
        result = jnp.broadcast_to(nearby[REACH], (slot_total,) + nearby.shape[1:])
        for distance in range(REACH - 1, -1, -1):
            result = jnp.where(pick == distance, nearby[distance], result)
        return result

    def inverse_of(cosines, sines):
        return jnp.concatenate(
            [jnp.concatenate([cosines, sines], axis=1), jnp.concatenate([-sines, cosines], axis=1)],
            axis=0,
        )

    left_block = chosen(first_off)
    right_block = chosen(second_off)
    if paired:
        kept = BAND + 1
        spec_shape = (slot_total, kept, stations, hour_count, 2, factor_b)
        scale_shape = (slot_total, stations, hour_count, factor_b)
        left_spec = left_block[:, :kept].reshape(spec_shape)
        right_spec = right_block[:, :kept].reshape(spec_shape)

        def weight(left_scale, right_scale):
            return left_scale[:, None, :, None] * right_scale[:, None, None, :]

        left_low = left_block[:, kept, :, 0].reshape(scale_shape)
        left_turned = left_block[:, kept, :, 1].reshape(scale_shape)
        right_low = right_block[:, kept, :, 0].reshape(scale_shape)
        right_turned = right_block[:, kept, :, 1].reshape(scale_shape)
        weight_paired = weight(left_low, right_low) + weight(left_turned, right_turned)
        single = jnp.ones((slot_total, 1) + weight_paired.shape[2:], jnp.float32)
        row_weight = jnp.concatenate(
            [single, jnp.broadcast_to(weight_paired, (slot_total, BAND - 1) + weight_paired.shape[2:]), single],
            axis=1,
        )
    else:
        kept = rows_local
        spec_shape = (slot_total, kept, stations, hour_count, 2, factor_b)
        left_spec = left_block.reshape(spec_shape)
        right_spec = right_block.reshape(spec_shape)
        row_weight = jnp.ones((1, 1, 1, 1, 1, 1), jnp.float32)
    left_real = left_spec[:, :, :, None, :, 0]
    left_imag = left_spec[:, :, :, None, :, 1]
    right_real = right_spec[:, :, None, :, :, 0]
    right_imag = right_spec[:, :, None, :, :, 1]
    cross_real = jnp.sum((left_real * right_real + left_imag * right_imag) * row_weight, axis=4)
    cross_imag = jnp.sum((left_imag * right_real - left_real * right_imag) * row_weight, axis=4)
    cross = jnp.concatenate([cross_real, cross_imag], axis=-1)
    lag = matmul(cross.reshape(-1, 2 * factor_b), inverse_of(cosine_b, sine_b)).reshape(
        slot_total, kept, stations, stations, 2, factor_b
    )
    row_ids = k1_ids[:kept]
    lag_real, lag_imag = lag[:, :, :, :, 0], lag[:, :, :, :, 1]
    cosine_u, sine_u = angles(row_ids, index_b, SAMPLES)
    turn_real = lag_real * cosine_u[None, :, None, None, :] - lag_imag * sine_u[None, :, None, None, :]
    turn_imag = lag_real * sine_u[None, :, None, None, :] + lag_imag * cosine_u[None, :, None, None, :]
    lag_ids = jnp.concatenate(
        [jnp.arange(LAGS, dtype=jnp.int32), factor_a - LAGS + jnp.arange(LAGS, dtype=jnp.int32)]
    )
    cosine_l, sine_l = angles(lag_ids, row_ids, factor_a)
    lag_weights = jnp.concatenate([cosine_l, -sine_l], axis=1).reshape(
        time_devices, 2 * LAGS // time_devices, 2 * kept
    )
    turned = jnp.concatenate([turn_real, turn_imag], axis=1)
    scale_out = 1.0 / math.sqrt(SAMPLES * hour_count)
    live_mask = (jnp.arange(slot_total) < pair_count).astype(jnp.float32) * scale_out
    lag_block = jnp.einsum(
        "dwp,spijm->dsijwm",
        lag_weights,
        turned,
        precision=highest,
        preferred_element_type=jnp.float32,
    )
    lag_block = lag_block * live_mask[None, :, None, None, None, None]
    flat = lag_block.reshape(time_devices, -1)
    dest_ids = lax.broadcasted_iota(jnp.int32, flat.shape, 0)

    def chunk_for(shift):
        mine = dest_ids == (time_rank + shift) % time_devices
        return jnp.sum(jnp.where(mine, flat, 0.0), axis=0)

    total = chunk_for(0)
    for shift in range(1, time_devices):
        route = [(i, (i + shift) % time_devices) for i in range(time_devices)]
        total = total + lax.ppermute(chunk_for(shift), "tm", route)
    return total.reshape(slot_total, stations, stations, 2 * LAGS * factor_b // time_devices)


def solution(mesh):
    placed = (P("sta", None, "tm"), P("sta", None), P("sta"))
    return jax.shard_map(local, mesh=mesh, in_specs=placed, out_specs=P("sta", None, None, "tm"), check_vma=False)
```

```python
import math

import jax
import jax.numpy as jnp
from jax import lax
from jax.sharding import PartitionSpec as P

SAMPLES = 65536
FACTOR_A = 256
BAND = 32
LAGS = 4
REACH = 3


highest = lax.Precision.HIGH
epsilon = 1e-06


def passed_along(block, axis, distance):
    devices = range(lax.axis_size(axis))
    route = [(i - distance, i) for i in devices if i - distance in devices]
    return lax.ppermute(block, axis, route)


def angles(row_ids, col_ids, modulus):
    product = row_ids[:, None] * col_ids[None, :] % modulus
    radians = product.astype(jnp.float32) * (2.0 * math.pi / modulus)
    return (jnp.cos(radians), jnp.sin(radians))


def matmul(left_mat, right_mat):
    return jnp.dot(left_mat, right_mat, precision=highest, preferred_element_type=jnp.float32)


def local(records, pair_blocks, pair_count):
    stations, hour_count, _ = records.shape
    time_devices = lax.axis_size("tm")
    time_rank = lax.axis_index("tm")
    owner_id = lax.axis_index("sta")
    factor_a = FACTOR_A
    factor_b = SAMPLES // FACTOR_A
    rows_local = factor_a // time_devices
    cols_local = factor_b // time_devices
    series = stations * hour_count
    arranged = records.reshape(series, rows_local, time_devices, cols_local).transpose(2, 1, 0, 3)
    spread = lax.all_to_all(
        arranged.reshape(time_devices, -1), "tm", split_axis=0, concat_axis=0, tiled=True
    ).reshape(factor_a, series, cols_local)
    index_a = jnp.arange(factor_a, dtype=jnp.int32)
    index_b = jnp.arange(factor_b, dtype=jnp.int32)
    paired = rows_local == 2 * BAND and factor_a == 2 * BAND * time_devices
    if paired:
        k1_ids = jnp.concatenate(
            [
                BAND * time_rank + jnp.arange(BAND, dtype=jnp.int32),
                factor_a - BAND * (time_rank + 1) + jnp.arange(BAND, dtype=jnp.int32),
            ]
        )
    else:
        k1_ids = time_rank * rows_local + jnp.arange(rows_local, dtype=jnp.int32)
    cosine_a, sine_a = angles(index_a, index_a, factor_a)
    flat_rows = spread.reshape(factor_a, series * cols_local)
    both_a = jnp.concatenate([cosine_a, -sine_a], axis=0)
    section = matmul(both_a, flat_rows).reshape(2, factor_a, series, cols_local)
    section_real, section_imag = section[0], section[1]
    col_global = time_rank * cols_local + jnp.arange(cols_local, dtype=jnp.int32)
    cosine_t, sine_t = angles(index_a, col_global, SAMPLES)
    twisted_real = section_real * cosine_t[:, None, :] + section_imag * sine_t[:, None, :]
    twisted_imag = section_imag * cosine_t[:, None, :] - section_real * sine_t[:, None, :]
    twisted = jnp.stack([twisted_real, twisted_imag], axis=2)
    if paired:
        bands = twisted.reshape(2, time_devices, BAND, series, 2, cols_local)
        grouped = jnp.stack([bands[0], bands[1][::-1]], axis=1)
        outgoing = grouped.reshape(time_devices, rows_local, series, 2, cols_local)[:, : BAND + 1]
        incoming = (
            lax.all_to_all(outgoing.reshape(time_devices, -1), "tm", split_axis=0, concat_axis=0, tiled=True)
            .reshape(time_devices, BAND + 1, series, 2, cols_local)
            .transpose(1, 2, 3, 0, 4)
            .reshape(BAND + 1, series, 2, factor_b)
        )
    else:
        moved = lax.all_to_all(twisted, "tm", split_axis=0, concat_axis=3, tiled=True)
    cosine_b, sine_b = angles(index_b, index_b, factor_b)
    forward_b = jnp.concatenate(
        [jnp.concatenate([cosine_b, -sine_b], axis=1), jnp.concatenate([sine_b, cosine_b], axis=1)],
        axis=0,
    )
    if paired:
        spec = matmul(incoming.reshape((BAND + 1) * series, 2 * factor_b), forward_b).reshape(
            BAND + 1, series, 2, factor_b
        )
        energy = spec[:, :, 0] * spec[:, :, 0] + spec[:, :, 1] * spec[:, :, 1]
        power_low = jnp.mean(energy[:BAND], axis=0)
        power_high = (energy[BAND] + jnp.sum(energy[1:BAND], axis=0)[:, ::-1]) / BAND
        scale_low = lax.rsqrt(power_low + epsilon)
        scale_high = lax.rsqrt(power_high + epsilon)
        scale_row = jnp.stack([scale_low, scale_high[:, ::-1]], axis=1)[None]
        sent = jnp.concatenate(
            [
                spec[:1] * scale_low[None, :, None, :],
                spec[1:BAND],
                spec[BAND:] * scale_high[None, :, None, :],
                scale_row,
            ]
        )
    else:
        spec = matmul(moved.reshape(rows_local * series, 2 * factor_b), forward_b)
        banded = spec.reshape(rows_local // BAND, BAND, series, 2, factor_b)
        band_power = jnp.mean(
            banded[:, :, :, 0] * banded[:, :, :, 0] + banded[:, :, :, 1] * banded[:, :, :, 1],
            axis=1,
            keepdims=True,
        )
        band_scale = lax.rsqrt(band_power + epsilon)
        sent = (banded * band_scale[:, :, :, None]).reshape(rows_local, series, 2, factor_b)
    k1_ids = lax.optimization_barrier((k1_ids, sent))[0]
    arrived = {}
    for distance in range(REACH, 0, -1):
        arrived[distance] = passed_along(sent.reshape(-1, factor_b), "sta", -distance).reshape(sent.shape)
    nearby = jnp.stack([sent] + [arrived[distance] for distance in range(1, REACH + 1)])
    slot_total = pair_blocks.shape[0]
    first_off = pair_blocks[:, 0] - owner_id
    second_off = pair_blocks[:, 1] - owner_id

    def chosen(offsets):
        pick = offsets.reshape((slot_total,) + (1,) * (nearby.ndim - 1))
        result = jnp.broadcast_to(nearby[REACH], (slot_total,) + nearby.shape[1:])
        for distance in range(REACH - 1, -1, -1):
            result = jnp.where(pick == distance, nearby[distance], result)
        return result

    def inverse_of(cosines, sines):
        return jnp.concatenate(
            [jnp.concatenate([cosines, sines], axis=1), jnp.concatenate([-sines, cosines], axis=1)],
            axis=0,
        )

    left_block = chosen(first_off)
    right_block = chosen(second_off)
    if paired:
        kept = BAND + 1
        spec_shape = (slot_total, kept, stations, hour_count, 2, factor_b)
        scale_shape = (slot_total, stations, hour_count, factor_b)
        left_spec = left_block[:, :kept].reshape(spec_shape)
        right_spec = right_block[:, :kept].reshape(spec_shape)

        def weight(left_scale, right_scale):
            return left_scale[:, None, :, None] * right_scale[:, None, None, :]

        left_low = left_block[:, kept, :, 0].reshape(scale_shape)
        left_turned = left_block[:, kept, :, 1].reshape(scale_shape)
        right_low = right_block[:, kept, :, 0].reshape(scale_shape)
        right_turned = right_block[:, kept, :, 1].reshape(scale_shape)
        weight_paired = weight(left_low, right_low) + weight(left_turned, right_turned)
        single = jnp.ones((slot_total, 1) + weight_paired.shape[2:], jnp.float32)
        row_weight = jnp.concatenate(
            [single, jnp.broadcast_to(weight_paired, (slot_total, BAND - 1) + weight_paired.shape[2:]), single],
            axis=1,
        )
    else:
        kept = rows_local
        spec_shape = (slot_total, kept, stations, hour_count, 2, factor_b)
        left_spec = left_block.reshape(spec_shape)
        right_spec = right_block.reshape(spec_shape)
        row_weight = jnp.ones((1, 1, 1, 1, 1, 1), jnp.float32)
    left_real = left_spec[:, :, :, None, :, 0]
    left_imag = left_spec[:, :, :, None, :, 1]
    right_real = right_spec[:, :, None, :, :, 0]
    right_imag = right_spec[:, :, None, :, :, 1]
    cross_real = jnp.sum((left_real * right_real + left_imag * right_imag) * row_weight, axis=4)
    cross_imag = jnp.sum((left_imag * right_real - left_real * right_imag) * row_weight, axis=4)
    cross = jnp.concatenate([cross_real, cross_imag], axis=-1)
    lag = matmul(cross.reshape(-1, 2 * factor_b), inverse_of(cosine_b, sine_b)).reshape(
        slot_total, kept, stations, stations, 2, factor_b
    )
    row_ids = k1_ids[:kept]
    lag_real, lag_imag = lag[:, :, :, :, 0], lag[:, :, :, :, 1]
    cosine_u, sine_u = angles(row_ids, index_b, SAMPLES)
    turn_real = lag_real * cosine_u[None, :, None, None, :] - lag_imag * sine_u[None, :, None, None, :]
    turn_imag = lag_real * sine_u[None, :, None, None, :] + lag_imag * cosine_u[None, :, None, None, :]
    lag_ids = jnp.concatenate(
        [jnp.arange(LAGS, dtype=jnp.int32), factor_a - LAGS + jnp.arange(LAGS, dtype=jnp.int32)]
    )
    cosine_l, sine_l = angles(lag_ids, row_ids, factor_a)
    lag_weights = jnp.concatenate([cosine_l, -sine_l], axis=1).reshape(
        time_devices, 2 * LAGS // time_devices, 2 * kept
    )
    turned = jnp.concatenate([turn_real, turn_imag], axis=1)
    scale_out = 1.0 / math.sqrt(SAMPLES * hour_count)
    live_mask = (jnp.arange(slot_total) < pair_count).astype(jnp.float32) * scale_out
    table_ids = lax.broadcasted_iota(jnp.int32, lag_weights.shape, 0)
    lag_weights = jnp.stack(
        [
            jnp.sum(jnp.where(table_ids == (time_rank + shift) % time_devices, lag_weights, 0.0), axis=0)
            for shift in range(time_devices)
        ]
    )
    lag_block = jnp.einsum(
        "dwp,spijm->dsijwm",
        lag_weights,
        turned,
        precision=highest,
        preferred_element_type=jnp.float32,
    )
    lag_block = lag_block * live_mask[None, :, None, None, None, None]
    out_shape = (slot_total, stations, stations, 2 * LAGS * factor_b // time_devices)
    total = lag_block[0].reshape(out_shape)
    for shift in range(1, time_devices):
        route = [(i, (i + shift) % time_devices) for i in range(time_devices)]
        total = total + lax.ppermute(lag_block[shift].reshape(out_shape), "tm", route)
    return total


def solution(mesh):
    placed = (P("sta", None, "tm"), P("sta", None), P("sta"))
    return jax.shard_map(local, mesh=mesh, in_specs=placed, out_specs=P("sta", None, None, "tm"), check_vma=False)
```

```python
import math

import jax
import jax.numpy as jnp
from jax import lax
from jax.sharding import PartitionSpec as P

SAMPLES = 65536
FACTOR_A = 256
BAND = 32
LAGS = 4
REACH = 3


highest = lax.Precision.HIGH
epsilon = 1e-06


def passed_along(block, axis, distance):
    devices = range(lax.axis_size(axis))
    route = [(i - distance, i) for i in devices if i - distance in devices]
    return lax.ppermute(block, axis, route)


def angles(row_ids, col_ids, modulus):
    product = row_ids[:, None] * col_ids[None, :] % modulus
    radians = product.astype(jnp.float32) * (2.0 * math.pi / modulus)
    return (jnp.cos(radians), jnp.sin(radians))


def matmul(left_mat, right_mat):
    return jnp.dot(left_mat, right_mat, precision=highest, preferred_element_type=jnp.float32)


def local(records, pair_blocks, pair_count):
    stations, hour_count, _ = records.shape
    time_devices = lax.axis_size("tm")
    time_rank = lax.axis_index("tm")
    owner_id = lax.axis_index("sta")
    factor_a = FACTOR_A
    factor_b = SAMPLES // FACTOR_A
    rows_local = factor_a // time_devices
    cols_local = factor_b // time_devices
    series = stations * hour_count
    arranged = records.reshape(series, rows_local, time_devices, cols_local).transpose(2, 1, 0, 3)
    spread = lax.all_to_all(
        arranged.reshape(time_devices, -1), "tm", split_axis=0, concat_axis=0, tiled=True
    ).reshape(factor_a, series, cols_local)
    index_a = jnp.arange(factor_a, dtype=jnp.int32)
    index_b = jnp.arange(factor_b, dtype=jnp.int32)
    paired = rows_local == 2 * BAND and factor_a == 2 * BAND * time_devices
    if paired:
        k1_ids = jnp.concatenate(
            [
                BAND * time_rank + jnp.arange(BAND, dtype=jnp.int32),
                factor_a - BAND * (time_rank + 1) + jnp.arange(BAND, dtype=jnp.int32),
            ]
        )
    else:
        k1_ids = time_rank * rows_local + jnp.arange(rows_local, dtype=jnp.int32)
    flat_rows = spread.reshape(factor_a, series * cols_local)
    col_global = time_rank * cols_local + jnp.arange(cols_local, dtype=jnp.int32)
    cosine_b, sine_b = angles(index_b, index_b, factor_b)
    if paired:
        shift_ids = lax.broadcasted_iota(jnp.int32, (time_devices, BAND + 1), 0)
        place_ids = lax.broadcasted_iota(jnp.int32, (time_devices, BAND + 1), 1)
        target = (time_rank + shift_ids) % time_devices
        send_rows = jnp.where(
            place_ids < BAND, BAND * target + place_ids, factor_a - BAND * (target + 1)
        ).reshape(-1)
        cosine_a, sine_a = angles(send_rows, index_a, factor_a)
        section = matmul(jnp.concatenate([cosine_a, -sine_a], axis=0), flat_rows).reshape(
            2, -1, series, cols_local
        )
        cosine_t, sine_t = angles(send_rows, col_global, SAMPLES)
        section_real, section_imag = section[0], section[1]
        twisted_real = section_real * cosine_t[:, None, :] + section_imag * sine_t[:, None, :]
        twisted_imag = section_imag * cosine_t[:, None, :] - section_real * sine_t[:, None, :]
        outgoing = jnp.stack([twisted_real, twisted_imag], axis=2).reshape(time_devices, -1)
        pieces = [outgoing[0]]
        for shift in range(1, time_devices):
            route = [(i, (i + shift) % time_devices) for i in range(time_devices)]
            pieces.append(lax.ppermute(outgoing[shift], "tm", route))
        incoming = (
            jnp.stack(pieces)
            .reshape(time_devices, BAND + 1, series, 2, cols_local)
            .transpose(1, 2, 3, 0, 4)
            .reshape(BAND + 1, series, 2, factor_b)
        )
        column_of = (
            cols_local * ((time_rank - index_b // cols_local) % time_devices) + index_b % cols_local
        )
        cosine_p, sine_p = angles(column_of, index_b, factor_b)
        forward_b = jnp.concatenate(
            [jnp.concatenate([cosine_p, -sine_p], axis=1), jnp.concatenate([sine_p, cosine_p], axis=1)],
            axis=0,
        )
    else:
        cosine_a, sine_a = angles(index_a, index_a, factor_a)
        both_a = jnp.concatenate([cosine_a, -sine_a], axis=0)
        section = matmul(both_a, flat_rows).reshape(2, factor_a, series, cols_local)
        section_real, section_imag = section[0], section[1]
        cosine_t, sine_t = angles(index_a, col_global, SAMPLES)
        twisted_real = section_real * cosine_t[:, None, :] + section_imag * sine_t[:, None, :]
        twisted_imag = section_imag * cosine_t[:, None, :] - section_real * sine_t[:, None, :]
        twisted = jnp.stack([twisted_real, twisted_imag], axis=2)
        moved = lax.all_to_all(twisted, "tm", split_axis=0, concat_axis=3, tiled=True)
        forward_b = jnp.concatenate(
            [jnp.concatenate([cosine_b, -sine_b], axis=1), jnp.concatenate([sine_b, cosine_b], axis=1)],
            axis=0,
        )
    if paired:
        spec = matmul(incoming.reshape((BAND + 1) * series, 2 * factor_b), forward_b).reshape(
            BAND + 1, series, 2, factor_b
        )
        energy = spec[:, :, 0] * spec[:, :, 0] + spec[:, :, 1] * spec[:, :, 1]
        power_low = jnp.mean(energy[:BAND], axis=0)
        power_high = (energy[BAND] + jnp.sum(energy[1:BAND], axis=0)[:, ::-1]) / BAND
        scale_low = lax.rsqrt(power_low + epsilon)
        scale_high = lax.rsqrt(power_high + epsilon)
        scale_row = jnp.stack([scale_low, scale_high[:, ::-1]], axis=1)[None]
        sent = jnp.concatenate(
            [
                spec[:1] * scale_low[None, :, None, :],
                spec[1:BAND],
                spec[BAND:] * scale_high[None, :, None, :],
                scale_row,
            ]
        )
    else:
        spec = matmul(moved.reshape(rows_local * series, 2 * factor_b), forward_b)
        banded = spec.reshape(rows_local // BAND, BAND, series, 2, factor_b)
        band_power = jnp.mean(
            banded[:, :, :, 0] * banded[:, :, :, 0] + banded[:, :, :, 1] * banded[:, :, :, 1],
            axis=1,
            keepdims=True,
        )
        band_scale = lax.rsqrt(band_power + epsilon)
        sent = (banded * band_scale[:, :, :, None]).reshape(rows_local, series, 2, factor_b)
    k1_ids = lax.optimization_barrier((k1_ids, sent))[0]
    arrived = {}
    for distance in range(REACH, 0, -1):
        arrived[distance] = passed_along(sent.reshape(-1, factor_b), "sta", -distance).reshape(sent.shape)
    nearby = jnp.stack([sent] + [arrived[distance] for distance in range(1, REACH + 1)])
    slot_total = pair_blocks.shape[0]
    first_off = pair_blocks[:, 0] - owner_id
    second_off = pair_blocks[:, 1] - owner_id

    def chosen(offsets):
        pick = offsets.reshape((slot_total,) + (1,) * (nearby.ndim - 1))
        result = jnp.broadcast_to(nearby[REACH], (slot_total,) + nearby.shape[1:])
        for distance in range(REACH - 1, -1, -1):
            result = jnp.where(pick == distance, nearby[distance], result)
        return result

    def inverse_of(cosines, sines):
        return jnp.concatenate(
            [jnp.concatenate([cosines, sines], axis=1), jnp.concatenate([-sines, cosines], axis=1)],
            axis=0,
        )

    left_block = chosen(first_off)
    right_block = chosen(second_off)
    if paired:
        kept = BAND + 1
        spec_shape = (slot_total, kept, stations, hour_count, 2, factor_b)
        scale_shape = (slot_total, stations, hour_count, factor_b)
        left_spec = left_block[:, :kept].reshape(spec_shape)
        right_spec = right_block[:, :kept].reshape(spec_shape)

        def weight(left_scale, right_scale):
            return left_scale[:, None, :, None] * right_scale[:, None, None, :]

        left_low = left_block[:, kept, :, 0].reshape(scale_shape)
        left_turned = left_block[:, kept, :, 1].reshape(scale_shape)
        right_low = right_block[:, kept, :, 0].reshape(scale_shape)
        right_turned = right_block[:, kept, :, 1].reshape(scale_shape)
        weight_paired = weight(left_low, right_low) + weight(left_turned, right_turned)
        single = jnp.ones((slot_total, 1) + weight_paired.shape[2:], jnp.float32)
        row_weight = jnp.concatenate(
            [single, jnp.broadcast_to(weight_paired, (slot_total, BAND - 1) + weight_paired.shape[2:]), single],
            axis=1,
        )
    else:
        kept = rows_local
        spec_shape = (slot_total, kept, stations, hour_count, 2, factor_b)
        left_spec = left_block.reshape(spec_shape)
        right_spec = right_block.reshape(spec_shape)
        row_weight = jnp.ones((1, 1, 1, 1, 1, 1), jnp.float32)
    left_real = left_spec[:, :, :, None, :, 0]
    left_imag = left_spec[:, :, :, None, :, 1]
    right_real = right_spec[:, :, None, :, :, 0]
    right_imag = right_spec[:, :, None, :, :, 1]
    cross_real = jnp.sum((left_real * right_real + left_imag * right_imag) * row_weight, axis=4)
    cross_imag = jnp.sum((left_imag * right_real - left_real * right_imag) * row_weight, axis=4)
    cross = jnp.concatenate([cross_real, cross_imag], axis=-1)
    lag = matmul(cross.reshape(-1, 2 * factor_b), inverse_of(cosine_b, sine_b)).reshape(
        slot_total, kept, stations, stations, 2, factor_b
    )
    row_ids = k1_ids[:kept]
    lag_real, lag_imag = lag[:, :, :, :, 0], lag[:, :, :, :, 1]
    cosine_u, sine_u = angles(row_ids, index_b, SAMPLES)
    turn_real = lag_real * cosine_u[None, :, None, None, :] - lag_imag * sine_u[None, :, None, None, :]
    turn_imag = lag_real * sine_u[None, :, None, None, :] + lag_imag * cosine_u[None, :, None, None, :]
    lag_ids = jnp.concatenate(
        [jnp.arange(LAGS, dtype=jnp.int32), factor_a - LAGS + jnp.arange(LAGS, dtype=jnp.int32)]
    )
    cosine_l, sine_l = angles(lag_ids, row_ids, factor_a)
    lag_weights = jnp.concatenate([cosine_l, -sine_l], axis=1).reshape(
        time_devices, 2 * LAGS // time_devices, 2 * kept
    )
    turned = jnp.concatenate([turn_real, turn_imag], axis=1)
    scale_out = 1.0 / math.sqrt(SAMPLES * hour_count)
    live_mask = (jnp.arange(slot_total) < pair_count).astype(jnp.float32) * scale_out
    lag_block = jnp.einsum(
        "dwp,spijm->dsijwm",
        lag_weights,
        turned,
        precision=highest,
        preferred_element_type=jnp.float32,
    )
    lag_block = lag_block * live_mask[None, :, None, None, None, None]
    flat = lag_block.reshape(time_devices, -1)
    dest_ids = lax.broadcasted_iota(jnp.int32, flat.shape, 0)

    def chunk_for(shift):
        mine = dest_ids == (time_rank + shift) % time_devices
        return jnp.sum(jnp.where(mine, flat, 0.0), axis=0)

    total = chunk_for(0)
    for shift in range(1, time_devices):
        route = [(i, (i + shift) % time_devices) for i in range(time_devices)]
        total = total + lax.ppermute(chunk_for(shift), "tm", route)
    return total.reshape(slot_total, stations, stations, 2 * LAGS * factor_b // time_devices)


def solution(mesh):
    placed = (P("sta", None, "tm"), P("sta", None), P("sta"))
    return jax.shard_map(local, mesh=mesh, in_specs=placed, out_specs=P("sta", None, None, "tm"), check_vma=False)
```

```python
import math

import jax
import jax.numpy as jnp
from jax import lax
from jax.sharding import PartitionSpec as P

SAMPLES = 65536
FACTOR_A = 256
BAND = 32
LAGS = 4
REACH = 3


highest = lax.Precision.HIGH
epsilon = 1e-06


def passed_along(block, axis, distance):
    devices = range(lax.axis_size(axis))
    route = [(i - distance, i) for i in devices if i - distance in devices]
    return lax.ppermute(block, axis, route)


def angles(row_ids, col_ids, modulus):
    product = row_ids[:, None] * col_ids[None, :] % modulus
    radians = product.astype(jnp.float32) * (2.0 * math.pi / modulus)
    return (jnp.cos(radians), jnp.sin(radians))


def matmul(left_mat, right_mat):
    return jnp.dot(left_mat, right_mat, precision=highest, preferred_element_type=jnp.float32)


def local(records, pair_blocks, pair_count):
    stations, hour_count, _ = records.shape
    time_devices = lax.axis_size("tm")
    time_rank = lax.axis_index("tm")
    owner_id = lax.axis_index("sta")
    factor_a = FACTOR_A
    factor_b = SAMPLES // FACTOR_A
    rows_local = factor_a // time_devices
    cols_local = factor_b // time_devices
    series = stations * hour_count
    arranged = records.reshape(series, rows_local, time_devices, cols_local).transpose(2, 1, 0, 3)
    index_a = jnp.arange(factor_a, dtype=jnp.int32)
    paired = rows_local == 2 * BAND and factor_a == 2 * BAND * time_devices
    if paired:
        pieces = [lax.dynamic_index_in_dim(arranged, time_rank, 0, keepdims=False)]
        for shift in range(1, time_devices):
            route = [(i, (i + shift) % time_devices) for i in range(time_devices)]
            chunk = lax.dynamic_index_in_dim(arranged, (time_rank + shift) % time_devices, 0, keepdims=False)
            pieces.append(lax.ppermute(chunk, "tm", route))
        spread = jnp.stack(pieces).reshape(factor_a, series, cols_local)
        row_of = rows_local * ((time_rank - index_a // rows_local) % time_devices) + index_a % rows_local
    else:
        spread = lax.all_to_all(
            arranged.reshape(time_devices, -1), "tm", split_axis=0, concat_axis=0, tiled=True
        ).reshape(factor_a, series, cols_local)
    index_b = jnp.arange(factor_b, dtype=jnp.int32)
    if paired:
        k1_ids = jnp.concatenate(
            [
                BAND * time_rank + jnp.arange(BAND, dtype=jnp.int32),
                factor_a - BAND * (time_rank + 1) + jnp.arange(BAND, dtype=jnp.int32),
            ]
        )
    else:
        k1_ids = time_rank * rows_local + jnp.arange(rows_local, dtype=jnp.int32)
    flat_rows = spread.reshape(factor_a, series * cols_local)
    col_global = time_rank * cols_local + jnp.arange(cols_local, dtype=jnp.int32)
    cosine_b, sine_b = angles(index_b, index_b, factor_b)
    if paired:
        shift_ids = lax.broadcasted_iota(jnp.int32, (time_devices, BAND + 1), 0)
        place_ids = lax.broadcasted_iota(jnp.int32, (time_devices, BAND + 1), 1)
        target = (time_rank + shift_ids) % time_devices
        send_rows = jnp.where(
            place_ids < BAND, BAND * target + place_ids, factor_a - BAND * (target + 1)
        ).reshape(-1)
        cosine_a, sine_a = angles(send_rows, row_of, factor_a)
        section = matmul(jnp.concatenate([cosine_a, -sine_a], axis=0), flat_rows).reshape(
            2, -1, series, cols_local
        )
        cosine_t, sine_t = angles(send_rows, col_global, SAMPLES)
        section_real, section_imag = section[0], section[1]
        twisted_real = section_real * cosine_t[:, None, :] + section_imag * sine_t[:, None, :]
        twisted_imag = section_imag * cosine_t[:, None, :] - section_real * sine_t[:, None, :]
        outgoing = jnp.stack([twisted_real, twisted_imag], axis=2).reshape(time_devices, -1)
        pieces = [outgoing[0]]
        for shift in range(1, time_devices):
            route = [(i, (i + shift) % time_devices) for i in range(time_devices)]
            pieces.append(lax.ppermute(outgoing[shift], "tm", route))
        incoming = (
            jnp.stack(pieces)
            .reshape(time_devices, BAND + 1, series, 2, cols_local)
            .transpose(1, 2, 3, 0, 4)
            .reshape(BAND + 1, series, 2, factor_b)
        )
        column_of = (
            cols_local * ((time_rank - index_b // cols_local) % time_devices) + index_b % cols_local
        )
        cosine_p, sine_p = angles(column_of, index_b, factor_b)
        forward_b = jnp.concatenate(
            [jnp.concatenate([cosine_p, -sine_p], axis=1), jnp.concatenate([sine_p, cosine_p], axis=1)],
            axis=0,
        )
    else:
        cosine_a, sine_a = angles(index_a, index_a, factor_a)
        both_a = jnp.concatenate([cosine_a, -sine_a], axis=0)
        section = matmul(both_a, flat_rows).reshape(2, factor_a, series, cols_local)
        section_real, section_imag = section[0], section[1]
        cosine_t, sine_t = angles(index_a, col_global, SAMPLES)
        twisted_real = section_real * cosine_t[:, None, :] + section_imag * sine_t[:, None, :]
        twisted_imag = section_imag * cosine_t[:, None, :] - section_real * sine_t[:, None, :]
        twisted = jnp.stack([twisted_real, twisted_imag], axis=2)
        moved = lax.all_to_all(twisted, "tm", split_axis=0, concat_axis=3, tiled=True)
        forward_b = jnp.concatenate(
            [jnp.concatenate([cosine_b, -sine_b], axis=1), jnp.concatenate([sine_b, cosine_b], axis=1)],
            axis=0,
        )
    if paired:
        spec = matmul(incoming.reshape((BAND + 1) * series, 2 * factor_b), forward_b).reshape(
            BAND + 1, series, 2, factor_b
        )
        energy = spec[:, :, 0] * spec[:, :, 0] + spec[:, :, 1] * spec[:, :, 1]
        power_low = jnp.mean(energy[:BAND], axis=0)
        power_high = (energy[BAND] + jnp.sum(energy[1:BAND], axis=0)[:, ::-1]) / BAND
        scale_low = lax.rsqrt(power_low + epsilon)
        scale_high = lax.rsqrt(power_high + epsilon)
        scale_row = jnp.stack([scale_low, scale_high[:, ::-1]], axis=1)[None]
        sent = jnp.concatenate(
            [
                spec[:1] * scale_low[None, :, None, :],
                spec[1:BAND],
                spec[BAND:] * scale_high[None, :, None, :],
                scale_row,
            ]
        )
    else:
        spec = matmul(moved.reshape(rows_local * series, 2 * factor_b), forward_b)
        banded = spec.reshape(rows_local // BAND, BAND, series, 2, factor_b)
        band_power = jnp.mean(
            banded[:, :, :, 0] * banded[:, :, :, 0] + banded[:, :, :, 1] * banded[:, :, :, 1],
            axis=1,
            keepdims=True,
        )
        band_scale = lax.rsqrt(band_power + epsilon)
        sent = (banded * band_scale[:, :, :, None]).reshape(rows_local, series, 2, factor_b)
    k1_ids = lax.optimization_barrier((k1_ids, sent))[0]
    arrived = {}
    for distance in range(REACH, 0, -1):
        arrived[distance] = passed_along(sent.reshape(-1, factor_b), "sta", -distance).reshape(sent.shape)
    nearby = jnp.stack([sent] + [arrived[distance] for distance in range(1, REACH + 1)])
    slot_total = pair_blocks.shape[0]
    first_off = pair_blocks[:, 0] - owner_id
    second_off = pair_blocks[:, 1] - owner_id

    def chosen(offsets):
        pick = offsets.reshape((slot_total,) + (1,) * (nearby.ndim - 1))
        result = jnp.broadcast_to(nearby[REACH], (slot_total,) + nearby.shape[1:])
        for distance in range(REACH - 1, -1, -1):
            result = jnp.where(pick == distance, nearby[distance], result)
        return result

    def inverse_of(cosines, sines):
        return jnp.concatenate(
            [jnp.concatenate([cosines, sines], axis=1), jnp.concatenate([-sines, cosines], axis=1)],
            axis=0,
        )

    left_block = chosen(first_off)
    right_block = chosen(second_off)
    if paired:
        kept = BAND + 1
        spec_shape = (slot_total, kept, stations, hour_count, 2, factor_b)
        scale_shape = (slot_total, stations, hour_count, factor_b)
        left_spec = left_block[:, :kept].reshape(spec_shape)
        right_spec = right_block[:, :kept].reshape(spec_shape)

        def weight(left_scale, right_scale):
            return left_scale[:, None, :, None] * right_scale[:, None, None, :]

        left_low = left_block[:, kept, :, 0].reshape(scale_shape)
        left_turned = left_block[:, kept, :, 1].reshape(scale_shape)
        right_low = right_block[:, kept, :, 0].reshape(scale_shape)
        right_turned = right_block[:, kept, :, 1].reshape(scale_shape)
        weight_paired = weight(left_low, right_low) + weight(left_turned, right_turned)
        single = jnp.ones((slot_total, 1) + weight_paired.shape[2:], jnp.float32)
        row_weight = jnp.concatenate(
            [single, jnp.broadcast_to(weight_paired, (slot_total, BAND - 1) + weight_paired.shape[2:]), single],
            axis=1,
        )
    else:
        kept = rows_local
        spec_shape = (slot_total, kept, stations, hour_count, 2, factor_b)
        left_spec = left_block.reshape(spec_shape)
        right_spec = right_block.reshape(spec_shape)
        row_weight = jnp.ones((1, 1, 1, 1, 1, 1), jnp.float32)
    left_real = left_spec[:, :, :, None, :, 0]
    left_imag = left_spec[:, :, :, None, :, 1]
    right_real = right_spec[:, :, None, :, :, 0]
    right_imag = right_spec[:, :, None, :, :, 1]
    cross_real = jnp.sum((left_real * right_real + left_imag * right_imag) * row_weight, axis=4)
    cross_imag = jnp.sum((left_imag * right_real - left_real * right_imag) * row_weight, axis=4)
    cross = jnp.concatenate([cross_real, cross_imag], axis=-1)
    lag = matmul(cross.reshape(-1, 2 * factor_b), inverse_of(cosine_b, sine_b)).reshape(
        slot_total, kept, stations, stations, 2, factor_b
    )
    row_ids = k1_ids[:kept]
    lag_real, lag_imag = lag[:, :, :, :, 0], lag[:, :, :, :, 1]
    cosine_u, sine_u = angles(row_ids, index_b, SAMPLES)
    turn_real = lag_real * cosine_u[None, :, None, None, :] - lag_imag * sine_u[None, :, None, None, :]
    turn_imag = lag_real * sine_u[None, :, None, None, :] + lag_imag * cosine_u[None, :, None, None, :]
    lag_ids = jnp.concatenate(
        [jnp.arange(LAGS, dtype=jnp.int32), factor_a - LAGS + jnp.arange(LAGS, dtype=jnp.int32)]
    )
    cosine_l, sine_l = angles(lag_ids, row_ids, factor_a)
    lag_weights = jnp.concatenate([cosine_l, -sine_l], axis=1).reshape(
        time_devices, 2 * LAGS // time_devices, 2 * kept
    )
    turned = jnp.concatenate([turn_real, turn_imag], axis=1)
    scale_out = 1.0 / math.sqrt(SAMPLES * hour_count)
    live_mask = (jnp.arange(slot_total) < pair_count).astype(jnp.float32) * scale_out
    lag_block = jnp.einsum(
        "dwp,spijm->dsijwm",
        lag_weights,
        turned,
        precision=highest,
        preferred_element_type=jnp.float32,
    )
    lag_block = lag_block * live_mask[None, :, None, None, None, None]
    flat = lag_block.reshape(time_devices, -1)
    dest_ids = lax.broadcasted_iota(jnp.int32, flat.shape, 0)

    def chunk_for(shift):
        mine = dest_ids == (time_rank + shift) % time_devices
        return jnp.sum(jnp.where(mine, flat, 0.0), axis=0)

    total = chunk_for(0)
    for shift in range(1, time_devices):
        route = [(i, (i + shift) % time_devices) for i in range(time_devices)]
        total = total + lax.ppermute(chunk_for(shift), "tm", route)
    return total.reshape(slot_total, stations, stations, 2 * LAGS * factor_b // time_devices)


def solution(mesh):
    placed = (P("sta", None, "tm"), P("sta", None), P("sta"))
    return jax.shard_map(local, mesh=mesh, in_specs=placed, out_specs=P("sta", None, None, "tm"), check_vma=False)
```

```python
import math

import jax
import jax.numpy as jnp
from jax import lax
from jax.sharding import PartitionSpec as P

SAMPLES = 65536
FACTOR_A = 256
BAND = 32
LAGS = 4
REACH = 3


highest = lax.Precision.HIGH
epsilon = 1e-06


def passed_along(block, axis, distance):
    devices = range(lax.axis_size(axis))
    route = [(i - distance, i) for i in devices if i - distance in devices]
    return lax.ppermute(block, axis, route)


def angles(row_ids, col_ids, modulus):
    product = row_ids[:, None] * col_ids[None, :] % modulus
    radians = product.astype(jnp.float32) * (2.0 * math.pi / modulus)
    return (jnp.cos(radians), jnp.sin(radians))


def matmul(left_mat, right_mat):
    return jnp.dot(left_mat, right_mat, precision=highest, preferred_element_type=jnp.float32)


def natural_order(pieces, rank, count):
    blocks = []
    for place in range(count):
        wanted = (rank - place) % count
        block = pieces[count - 1]
        for shift in range(count - 2, -1, -1):
            block = jnp.where(wanted == shift, pieces[shift], block)
        blocks.append(block)
    return jnp.stack(blocks)


def local(records, pair_blocks, pair_count):
    stations, hour_count, _ = records.shape
    time_devices = lax.axis_size("tm")
    time_rank = lax.axis_index("tm")
    owner_id = lax.axis_index("sta")
    factor_a = FACTOR_A
    factor_b = SAMPLES // FACTOR_A
    rows_local = factor_a // time_devices
    cols_local = factor_b // time_devices
    series = stations * hour_count
    arranged = records.reshape(series, rows_local, time_devices, cols_local).transpose(2, 1, 0, 3)
    index_a = jnp.arange(factor_a, dtype=jnp.int32)
    paired = rows_local == 2 * BAND and factor_a == 2 * BAND * time_devices
    if paired:
        pieces = [lax.dynamic_index_in_dim(arranged, time_rank, 0, keepdims=False)]
        for shift in range(1, time_devices):
            route = [(i, (i + shift) % time_devices) for i in range(time_devices)]
            chunk = lax.dynamic_index_in_dim(arranged, (time_rank + shift) % time_devices, 0, keepdims=False)
            pieces.append(lax.ppermute(chunk, "tm", route))
        spread = natural_order(pieces, time_rank, time_devices).reshape(factor_a, series, cols_local)
    else:
        spread = lax.all_to_all(
            arranged.reshape(time_devices, -1), "tm", split_axis=0, concat_axis=0, tiled=True
        ).reshape(factor_a, series, cols_local)
    index_b = jnp.arange(factor_b, dtype=jnp.int32)
    if paired:
        k1_ids = jnp.concatenate(
            [
                BAND * time_rank + jnp.arange(BAND, dtype=jnp.int32),
                factor_a - BAND * (time_rank + 1) + jnp.arange(BAND, dtype=jnp.int32),
            ]
        )
    else:
        k1_ids = time_rank * rows_local + jnp.arange(rows_local, dtype=jnp.int32)
    flat_rows = spread.reshape(factor_a, series * cols_local)
    col_global = time_rank * cols_local + jnp.arange(cols_local, dtype=jnp.int32)
    cosine_b, sine_b = angles(index_b, index_b, factor_b)
    if paired:
        shift_ids = lax.broadcasted_iota(jnp.int32, (time_devices, BAND + 1), 0)
        place_ids = lax.broadcasted_iota(jnp.int32, (time_devices, BAND + 1), 1)
        target = (time_rank + shift_ids) % time_devices
        send_rows = jnp.where(
            place_ids < BAND, BAND * target + place_ids, factor_a - BAND * (target + 1)
        ).reshape(-1)
        section_all = matmul(jnp.concatenate([cosine_b, -sine_b], axis=0), flat_rows).reshape(
            2, factor_a, series, cols_local
        )
        picked = []
        for shift in range(time_devices):
            target_rank = (time_rank + shift) % time_devices
            picked.append(lax.dynamic_slice_in_dim(section_all, BAND * target_rank, BAND, axis=1))
            picked.append(
                lax.dynamic_slice_in_dim(section_all, factor_a - BAND * (target_rank + 1), 1, axis=1)
            )
        section = jnp.concatenate(picked, axis=1)
        cosine_t, sine_t = angles(send_rows, col_global, SAMPLES)
        section_real, section_imag = section[0], section[1]
        twisted_real = section_real * cosine_t[:, None, :] + section_imag * sine_t[:, None, :]
        twisted_imag = section_imag * cosine_t[:, None, :] - section_real * sine_t[:, None, :]
        outgoing = jnp.stack([twisted_real, twisted_imag], axis=2).reshape(time_devices, -1)
        pieces = [outgoing[0]]
        for shift in range(1, time_devices):
            route = [(i, (i + shift) % time_devices) for i in range(time_devices)]
            pieces.append(lax.ppermute(outgoing[shift], "tm", route))
        incoming = (
            natural_order(pieces, time_rank, time_devices)
            .reshape(time_devices, BAND + 1, series, 2, cols_local)
            .transpose(1, 2, 3, 0, 4)
            .reshape(BAND + 1, series, 2, factor_b)
        )
        forward_b = jnp.concatenate(
            [jnp.concatenate([cosine_b, -sine_b], axis=1), jnp.concatenate([sine_b, cosine_b], axis=1)],
            axis=0,
        )
    else:
        cosine_a, sine_a = angles(index_a, index_a, factor_a)
        both_a = jnp.concatenate([cosine_a, -sine_a], axis=0)
        section = matmul(both_a, flat_rows).reshape(2, factor_a, series, cols_local)
        section_real, section_imag = section[0], section[1]
        cosine_t, sine_t = angles(index_a, col_global, SAMPLES)
        twisted_real = section_real * cosine_t[:, None, :] + section_imag * sine_t[:, None, :]
        twisted_imag = section_imag * cosine_t[:, None, :] - section_real * sine_t[:, None, :]
        twisted = jnp.stack([twisted_real, twisted_imag], axis=2)
        moved = lax.all_to_all(twisted, "tm", split_axis=0, concat_axis=3, tiled=True)
        forward_b = jnp.concatenate(
            [jnp.concatenate([cosine_b, -sine_b], axis=1), jnp.concatenate([sine_b, cosine_b], axis=1)],
            axis=0,
        )
    if paired:
        spec = matmul(incoming.reshape((BAND + 1) * series, 2 * factor_b), forward_b).reshape(
            BAND + 1, series, 2, factor_b
        )
        energy = spec[:, :, 0] * spec[:, :, 0] + spec[:, :, 1] * spec[:, :, 1]
        power_low = jnp.mean(energy[:BAND], axis=0)
        power_high = (energy[BAND] + jnp.sum(energy[1:BAND], axis=0)[:, ::-1]) / BAND
        scale_low = lax.rsqrt(power_low + epsilon)
        scale_high = lax.rsqrt(power_high + epsilon)
        scale_row = jnp.stack([scale_low, scale_high[:, ::-1]], axis=1)[None]
        sent = jnp.concatenate(
            [
                spec[:1] * scale_low[None, :, None, :],
                spec[1:BAND],
                spec[BAND:] * scale_high[None, :, None, :],
                scale_row,
            ]
        )
    else:
        spec = matmul(moved.reshape(rows_local * series, 2 * factor_b), forward_b)
        banded = spec.reshape(rows_local // BAND, BAND, series, 2, factor_b)
        band_power = jnp.mean(
            banded[:, :, :, 0] * banded[:, :, :, 0] + banded[:, :, :, 1] * banded[:, :, :, 1],
            axis=1,
            keepdims=True,
        )
        band_scale = lax.rsqrt(band_power + epsilon)
        sent = (banded * band_scale[:, :, :, None]).reshape(rows_local, series, 2, factor_b)
    k1_ids = lax.optimization_barrier((k1_ids, sent))[0]
    arrived = {}
    for distance in range(REACH, 0, -1):
        arrived[distance] = passed_along(sent.reshape(-1, factor_b), "sta", -distance).reshape(sent.shape)
    nearby = jnp.stack([sent] + [arrived[distance] for distance in range(1, REACH + 1)])
    slot_total = pair_blocks.shape[0]
    first_off = pair_blocks[:, 0] - owner_id
    second_off = pair_blocks[:, 1] - owner_id

    def chosen(offsets):
        pick = offsets.reshape((slot_total,) + (1,) * (nearby.ndim - 1))
        result = jnp.broadcast_to(nearby[REACH], (slot_total,) + nearby.shape[1:])
        for distance in range(REACH - 1, -1, -1):
            result = jnp.where(pick == distance, nearby[distance], result)
        return result

    def inverse_of(cosines, sines):
        return jnp.concatenate(
            [jnp.concatenate([cosines, sines], axis=1), jnp.concatenate([-sines, cosines], axis=1)],
            axis=0,
        )

    left_block = chosen(first_off)
    right_block = chosen(second_off)
    if paired:
        kept = BAND + 1
        spec_shape = (slot_total, kept, stations, hour_count, 2, factor_b)
        scale_shape = (slot_total, stations, hour_count, factor_b)
        left_spec = left_block[:, :kept].reshape(spec_shape)
        right_spec = right_block[:, :kept].reshape(spec_shape)

        def weight(left_scale, right_scale):
            return left_scale[:, None, :, None] * right_scale[:, None, None, :]

        left_low = left_block[:, kept, :, 0].reshape(scale_shape)
        left_turned = left_block[:, kept, :, 1].reshape(scale_shape)
        right_low = right_block[:, kept, :, 0].reshape(scale_shape)
        right_turned = right_block[:, kept, :, 1].reshape(scale_shape)
        weight_paired = weight(left_low, right_low) + weight(left_turned, right_turned)
        single = jnp.ones((slot_total, 1) + weight_paired.shape[2:], jnp.float32)
        row_weight = jnp.concatenate(
            [single, jnp.broadcast_to(weight_paired, (slot_total, BAND - 1) + weight_paired.shape[2:]), single],
            axis=1,
        )
    else:
        kept = rows_local
        spec_shape = (slot_total, kept, stations, hour_count, 2, factor_b)
        left_spec = left_block.reshape(spec_shape)
        right_spec = right_block.reshape(spec_shape)
        row_weight = jnp.ones((1, 1, 1, 1, 1, 1), jnp.float32)
    left_real = left_spec[:, :, :, None, :, 0]
    left_imag = left_spec[:, :, :, None, :, 1]
    right_real = right_spec[:, :, None, :, :, 0]
    right_imag = right_spec[:, :, None, :, :, 1]
    cross_real = jnp.sum((left_real * right_real + left_imag * right_imag) * row_weight, axis=4)
    cross_imag = jnp.sum((left_imag * right_real - left_real * right_imag) * row_weight, axis=4)
    cross = jnp.concatenate([cross_real, cross_imag], axis=-1)
    lag = matmul(cross.reshape(-1, 2 * factor_b), inverse_of(cosine_b, sine_b)).reshape(
        slot_total, kept, stations, stations, 2, factor_b
    )
    row_ids = k1_ids[:kept]
    lag_real, lag_imag = lag[:, :, :, :, 0], lag[:, :, :, :, 1]
    cosine_u, sine_u = angles(row_ids, index_b, SAMPLES)
    turn_real = lag_real * cosine_u[None, :, None, None, :] - lag_imag * sine_u[None, :, None, None, :]
    turn_imag = lag_real * sine_u[None, :, None, None, :] + lag_imag * cosine_u[None, :, None, None, :]
    lag_ids = jnp.concatenate(
        [jnp.arange(LAGS, dtype=jnp.int32), factor_a - LAGS + jnp.arange(LAGS, dtype=jnp.int32)]
    )
    cosine_l, sine_l = angles(lag_ids, row_ids, factor_a)
    lag_weights = jnp.concatenate([cosine_l, -sine_l], axis=1).reshape(
        time_devices, 2 * LAGS // time_devices, 2 * kept
    )
    turned = jnp.concatenate([turn_real, turn_imag], axis=1)
    scale_out = 1.0 / math.sqrt(SAMPLES * hour_count)
    live_mask = (jnp.arange(slot_total) < pair_count).astype(jnp.float32) * scale_out
    lag_block = jnp.einsum(
        "dwp,spijm->dsijwm",
        lag_weights,
        turned,
        precision=highest,
        preferred_element_type=jnp.float32,
    )
    lag_block = lag_block * live_mask[None, :, None, None, None, None]
    flat = lag_block.reshape(time_devices, -1)
    dest_ids = lax.broadcasted_iota(jnp.int32, flat.shape, 0)

    def chunk_for(shift):
        mine = dest_ids == (time_rank + shift) % time_devices
        return jnp.sum(jnp.where(mine, flat, 0.0), axis=0)

    total = chunk_for(0)
    for shift in range(1, time_devices):
        route = [(i, (i + shift) % time_devices) for i in range(time_devices)]
        total = total + lax.ppermute(chunk_for(shift), "tm", route)
    return total.reshape(slot_total, stations, stations, 2 * LAGS * factor_b // time_devices)


def solution(mesh):
    placed = (P("sta", None, "tm"), P("sta", None), P("sta"))
    return jax.shard_map(local, mesh=mesh, in_specs=placed, out_specs=P("sta", None, None, "tm"), check_vma=False)
```

```python
import math

import jax
import jax.numpy as jnp
from jax import lax
from jax.sharding import PartitionSpec as P

SAMPLES = 65536
FACTOR_A = 256
BAND = 32
LAGS = 4
REACH = 3


highest = lax.Precision.HIGH
epsilon = 1e-06


def passed_along(block, axis, distance):
    devices = range(lax.axis_size(axis))
    route = [(i - distance, i) for i in devices if i - distance in devices]
    return lax.ppermute(block, axis, route)


def angles(row_ids, col_ids, modulus):
    product = row_ids[:, None] * col_ids[None, :] % modulus
    radians = product.astype(jnp.float32) * (2.0 * math.pi / modulus)
    return (jnp.cos(radians), jnp.sin(radians))


def matmul(left_mat, right_mat):
    return jnp.dot(left_mat, right_mat, precision=highest, preferred_element_type=jnp.float32)


def local(records, pair_blocks, pair_count):
    stations, hour_count, _ = records.shape
    time_devices = lax.axis_size("tm")
    time_rank = lax.axis_index("tm")
    owner_id = lax.axis_index("sta")
    factor_a = FACTOR_A
    factor_b = SAMPLES // FACTOR_A
    rows_local = factor_a // time_devices
    cols_local = factor_b // time_devices
    series = stations * hour_count
    arranged = records.reshape(series, rows_local, time_devices, cols_local).transpose(2, 1, 0, 3)
    index_a = jnp.arange(factor_a, dtype=jnp.int32)
    paired = rows_local == 2 * BAND and factor_a == 2 * BAND * time_devices
    if paired:
        rows_view = records.reshape(series, rows_local, factor_b)

        def column_block(owner):
            return lax.dynamic_slice_in_dim(rows_view, cols_local * owner, cols_local, axis=2)

        pieces = [column_block(time_rank)]
        for shift in range(1, time_devices):
            route = [(i, (i + shift) % time_devices) for i in range(time_devices)]
            pieces.append(lax.ppermute(column_block((time_rank + shift) % time_devices), "tm", route))
        spread = jnp.stack(pieces).transpose(0, 2, 1, 3).reshape(factor_a, series, cols_local)
        row_of = rows_local * ((time_rank - index_a // rows_local) % time_devices) + index_a % rows_local
    else:
        spread = lax.all_to_all(
            arranged.reshape(time_devices, -1), "tm", split_axis=0, concat_axis=0, tiled=True
        ).reshape(factor_a, series, cols_local)
    index_b = jnp.arange(factor_b, dtype=jnp.int32)
    if paired:
        k1_ids = jnp.concatenate(
            [
                BAND * time_rank + jnp.arange(BAND, dtype=jnp.int32),
                factor_a - BAND * (time_rank + 1) + jnp.arange(BAND, dtype=jnp.int32),
            ]
        )
    else:
        k1_ids = time_rank * rows_local + jnp.arange(rows_local, dtype=jnp.int32)
    flat_rows = spread.reshape(factor_a, series * cols_local)
    col_global = time_rank * cols_local + jnp.arange(cols_local, dtype=jnp.int32)
    cosine_b, sine_b = angles(index_b, index_b, factor_b)
    if paired:
        shift_ids = lax.broadcasted_iota(jnp.int32, (time_devices, BAND + 1), 0)
        place_ids = lax.broadcasted_iota(jnp.int32, (time_devices, BAND + 1), 1)
        target = (time_rank + shift_ids) % time_devices
        send_rows = jnp.where(
            place_ids < BAND, BAND * target + place_ids, factor_a - BAND * (target + 1)
        ).reshape(-1)
        cosine_a, sine_a = angles(send_rows, row_of, factor_a)
        section = matmul(jnp.concatenate([cosine_a, -sine_a], axis=0), flat_rows).reshape(
            2, -1, series, cols_local
        )
        cosine_t, sine_t = angles(send_rows, col_global, SAMPLES)
        section_real, section_imag = section[0], section[1]
        twisted_real = section_real * cosine_t[:, None, :] + section_imag * sine_t[:, None, :]
        twisted_imag = section_imag * cosine_t[:, None, :] - section_real * sine_t[:, None, :]
        outgoing = jnp.stack([twisted_real, twisted_imag], axis=2).reshape(time_devices, -1)
        pieces = [outgoing[0]]
        for shift in range(1, time_devices):
            route = [(i, (i + shift) % time_devices) for i in range(time_devices)]
            pieces.append(lax.ppermute(outgoing[shift], "tm", route))
        incoming = (
            jnp.stack(pieces)
            .reshape(time_devices, BAND + 1, series, 2, cols_local)
            .transpose(1, 2, 3, 0, 4)
            .reshape(BAND + 1, series, 2, factor_b)
        )
        column_of = (
            cols_local * ((time_rank - index_b // cols_local) % time_devices) + index_b % cols_local
        )
        cosine_p, sine_p = angles(column_of, index_b, factor_b)
        forward_b = jnp.concatenate(
            [jnp.concatenate([cosine_p, -sine_p], axis=1), jnp.concatenate([sine_p, cosine_p], axis=1)],
            axis=0,
        )
    else:
        cosine_a, sine_a = angles(index_a, index_a, factor_a)
        both_a = jnp.concatenate([cosine_a, -sine_a], axis=0)
        section = matmul(both_a, flat_rows).reshape(2, factor_a, series, cols_local)
        section_real, section_imag = section[0], section[1]
        cosine_t, sine_t = angles(index_a, col_global, SAMPLES)
        twisted_real = section_real * cosine_t[:, None, :] + section_imag * sine_t[:, None, :]
        twisted_imag = section_imag * cosine_t[:, None, :] - section_real * sine_t[:, None, :]
        twisted = jnp.stack([twisted_real, twisted_imag], axis=2)
        moved = lax.all_to_all(twisted, "tm", split_axis=0, concat_axis=3, tiled=True)
        forward_b = jnp.concatenate(
            [jnp.concatenate([cosine_b, -sine_b], axis=1), jnp.concatenate([sine_b, cosine_b], axis=1)],
            axis=0,
        )
    if paired:
        spec = matmul(incoming.reshape((BAND + 1) * series, 2 * factor_b), forward_b).reshape(
            BAND + 1, series, 2, factor_b
        )
        energy = spec[:, :, 0] * spec[:, :, 0] + spec[:, :, 1] * spec[:, :, 1]
        power_low = jnp.mean(energy[:BAND], axis=0)
        power_high = (energy[BAND] + jnp.sum(energy[1:BAND], axis=0)[:, ::-1]) / BAND
        scale_low = lax.rsqrt(power_low + epsilon)
        scale_high = lax.rsqrt(power_high + epsilon)
        scale_row = jnp.stack([scale_low, scale_high[:, ::-1]], axis=1)[None]
        sent = jnp.concatenate(
            [
                spec[:1] * scale_low[None, :, None, :],
                spec[1:BAND],
                spec[BAND:] * scale_high[None, :, None, :],
                scale_row,
            ]
        )
    else:
        spec = matmul(moved.reshape(rows_local * series, 2 * factor_b), forward_b)
        banded = spec.reshape(rows_local // BAND, BAND, series, 2, factor_b)
        band_power = jnp.mean(
            banded[:, :, :, 0] * banded[:, :, :, 0] + banded[:, :, :, 1] * banded[:, :, :, 1],
            axis=1,
            keepdims=True,
        )
        band_scale = lax.rsqrt(band_power + epsilon)
        sent = (banded * band_scale[:, :, :, None]).reshape(rows_local, series, 2, factor_b)
    k1_ids = lax.optimization_barrier((k1_ids, sent))[0]
    arrived = {}
    for distance in range(REACH, 0, -1):
        arrived[distance] = passed_along(sent.reshape(-1, factor_b), "sta", -distance).reshape(sent.shape)
    nearby = jnp.stack([sent] + [arrived[distance] for distance in range(1, REACH + 1)])
    slot_total = pair_blocks.shape[0]
    first_off = pair_blocks[:, 0] - owner_id
    second_off = pair_blocks[:, 1] - owner_id

    def chosen(offsets):
        pick = offsets.reshape((slot_total,) + (1,) * (nearby.ndim - 1))
        result = jnp.broadcast_to(nearby[REACH], (slot_total,) + nearby.shape[1:])
        for distance in range(REACH - 1, -1, -1):
            result = jnp.where(pick == distance, nearby[distance], result)
        return result

    def inverse_of(cosines, sines):
        return jnp.concatenate(
            [jnp.concatenate([cosines, sines], axis=1), jnp.concatenate([-sines, cosines], axis=1)],
            axis=0,
        )

    left_block = chosen(first_off)
    right_block = chosen(second_off)
    if paired:
        kept = BAND + 1
        spec_shape = (slot_total, kept, stations, hour_count, 2, factor_b)
        scale_shape = (slot_total, stations, hour_count, factor_b)
        left_spec = left_block[:, :kept].reshape(spec_shape)
        right_spec = right_block[:, :kept].reshape(spec_shape)

        def weight(left_scale, right_scale):
            return left_scale[:, None, :, None] * right_scale[:, None, None, :]

        left_low = left_block[:, kept, :, 0].reshape(scale_shape)
        left_turned = left_block[:, kept, :, 1].reshape(scale_shape)
        right_low = right_block[:, kept, :, 0].reshape(scale_shape)
        right_turned = right_block[:, kept, :, 1].reshape(scale_shape)
        weight_paired = weight(left_low, right_low) + weight(left_turned, right_turned)
        single = jnp.ones((slot_total, 1) + weight_paired.shape[2:], jnp.float32)
        row_weight = jnp.concatenate(
            [single, jnp.broadcast_to(weight_paired, (slot_total, BAND - 1) + weight_paired.shape[2:]), single],
            axis=1,
        )
    else:
        kept = rows_local
        spec_shape = (slot_total, kept, stations, hour_count, 2, factor_b)
        left_spec = left_block.reshape(spec_shape)
        right_spec = right_block.reshape(spec_shape)
        row_weight = jnp.ones((1, 1, 1, 1, 1, 1), jnp.float32)
    left_real = left_spec[:, :, :, None, :, 0]
    left_imag = left_spec[:, :, :, None, :, 1]
    right_real = right_spec[:, :, None, :, :, 0]
    right_imag = right_spec[:, :, None, :, :, 1]
    cross_real = jnp.sum((left_real * right_real + left_imag * right_imag) * row_weight, axis=4)
    cross_imag = jnp.sum((left_imag * right_real - left_real * right_imag) * row_weight, axis=4)
    cross = jnp.concatenate([cross_real, cross_imag], axis=-1)
    lag = matmul(cross.reshape(-1, 2 * factor_b), inverse_of(cosine_b, sine_b)).reshape(
        slot_total, kept, stations, stations, 2, factor_b
    )
    row_ids = k1_ids[:kept]
    lag_real, lag_imag = lag[:, :, :, :, 0], lag[:, :, :, :, 1]
    cosine_u, sine_u = angles(row_ids, index_b, SAMPLES)
    turn_real = lag_real * cosine_u[None, :, None, None, :] - lag_imag * sine_u[None, :, None, None, :]
    turn_imag = lag_real * sine_u[None, :, None, None, :] + lag_imag * cosine_u[None, :, None, None, :]
    lag_ids = jnp.concatenate(
        [jnp.arange(LAGS, dtype=jnp.int32), factor_a - LAGS + jnp.arange(LAGS, dtype=jnp.int32)]
    )
    cosine_l, sine_l = angles(lag_ids, row_ids, factor_a)
    lag_weights = jnp.concatenate([cosine_l, -sine_l], axis=1).reshape(
        time_devices, 2 * LAGS // time_devices, 2 * kept
    )
    turned = jnp.concatenate([turn_real, turn_imag], axis=1)
    scale_out = 1.0 / math.sqrt(SAMPLES * hour_count)
    live_mask = (jnp.arange(slot_total) < pair_count).astype(jnp.float32) * scale_out
    lag_block = jnp.einsum(
        "dwp,spijm->dsijwm",
        lag_weights,
        turned,
        precision=highest,
        preferred_element_type=jnp.float32,
    )
    lag_block = lag_block * live_mask[None, :, None, None, None, None]
    flat = lag_block.reshape(time_devices, -1)
    dest_ids = lax.broadcasted_iota(jnp.int32, flat.shape, 0)

    def chunk_for(shift):
        mine = dest_ids == (time_rank + shift) % time_devices
        return jnp.sum(jnp.where(mine, flat, 0.0), axis=0)

    total = chunk_for(0)
    for shift in range(1, time_devices):
        route = [(i, (i + shift) % time_devices) for i in range(time_devices)]
        total = total + lax.ppermute(chunk_for(shift), "tm", route)
    return total.reshape(slot_total, stations, stations, 2 * LAGS * factor_b // time_devices)


def solution(mesh):
    placed = (P("sta", None, "tm"), P("sta", None), P("sta"))
    return jax.shard_map(local, mesh=mesh, in_specs=placed, out_specs=P("sta", None, None, "tm"), check_vma=False)
```

```python
import math

import jax
import jax.numpy as jnp
from jax import lax
from jax.sharding import PartitionSpec as P

SAMPLES = 65536
FACTOR_A = 256
BAND = 32
LAGS = 4
REACH = 3


highest = lax.Precision.HIGH
epsilon = 1e-06


def passed_along(block, axis, distance):
    devices = range(lax.axis_size(axis))
    route = [(i - distance, i) for i in devices if i - distance in devices]
    return lax.ppermute(block, axis, route)


def angles(row_ids, col_ids, modulus):
    product = row_ids[:, None] * col_ids[None, :] % modulus
    radians = product.astype(jnp.float32) * (2.0 * math.pi / modulus)
    return (jnp.cos(radians), jnp.sin(radians))


def matmul(left_mat, right_mat):
    return jnp.dot(left_mat, right_mat, precision=highest, preferred_element_type=jnp.float32)


def local(records, pair_blocks, pair_count):
    stations, hour_count, _ = records.shape
    time_devices = lax.axis_size("tm")
    time_rank = lax.axis_index("tm")
    owner_id = lax.axis_index("sta")
    factor_a = FACTOR_A
    factor_b = SAMPLES // FACTOR_A
    rows_local = factor_a // time_devices
    cols_local = factor_b // time_devices
    series = stations * hour_count
    arranged = records.reshape(series, rows_local, time_devices, cols_local).transpose(2, 1, 0, 3)
    index_a = jnp.arange(factor_a, dtype=jnp.int32)
    paired = rows_local == 2 * BAND and factor_a == 2 * BAND * time_devices
    if paired:
        pieces = [lax.dynamic_index_in_dim(arranged, time_rank, 0, keepdims=False)]
        for shift in range(1, time_devices):
            route = [(i, (i + shift) % time_devices) for i in range(time_devices)]
            chunk = lax.dynamic_index_in_dim(arranged, (time_rank + shift) % time_devices, 0, keepdims=False)
            pieces.append(lax.ppermute(chunk, "tm", route))
        spread = jnp.stack(pieces).reshape(factor_a, series, cols_local)
        row_of = rows_local * ((time_rank - index_a // rows_local) % time_devices) + index_a % rows_local
    else:
        spread = lax.all_to_all(
            arranged.reshape(time_devices, -1), "tm", split_axis=0, concat_axis=0, tiled=True
        ).reshape(factor_a, series, cols_local)
    index_b = jnp.arange(factor_b, dtype=jnp.int32)
    if paired:
        k1_ids = jnp.concatenate(
            [
                BAND * time_rank + jnp.arange(BAND, dtype=jnp.int32),
                factor_a - BAND * (time_rank + 1) + jnp.arange(BAND, dtype=jnp.int32),
            ]
        )
    else:
        k1_ids = time_rank * rows_local + jnp.arange(rows_local, dtype=jnp.int32)
    flat_rows = spread.reshape(factor_a, series * cols_local)
    col_global = time_rank * cols_local + jnp.arange(cols_local, dtype=jnp.int32)
    cosine_b, sine_b = angles(index_b, index_b, factor_b)
    if paired:
        shift_ids = lax.broadcasted_iota(jnp.int32, (time_devices, BAND + 1), 0)
        place_ids = lax.broadcasted_iota(jnp.int32, (time_devices, BAND + 1), 1)
        target = (time_rank + shift_ids) % time_devices
        send_rows = jnp.where(
            place_ids < BAND, BAND * target + place_ids, factor_a - BAND * (target + 1)
        ).reshape(-1)
        cosine_a, sine_a = angles(send_rows, row_of, factor_a)
        section = matmul(jnp.concatenate([cosine_a, -sine_a], axis=0), flat_rows).reshape(
            2, -1, series, cols_local
        )
        cosine_t, sine_t = angles(send_rows, col_global, SAMPLES)
        section_real, section_imag = section[0], section[1]
        twisted_real = section_real * cosine_t[:, None, :] + section_imag * sine_t[:, None, :]
        twisted_imag = section_imag * cosine_t[:, None, :] - section_real * sine_t[:, None, :]
        outgoing = jnp.stack([twisted_real, twisted_imag], axis=2).reshape(time_devices, -1)
        pieces = [outgoing[0]]
        for shift in range(1, time_devices):
            route = [(i, (i + shift) % time_devices) for i in range(time_devices)]
            pieces.append(lax.ppermute(outgoing[shift], "tm", route))
        incoming = (
            jnp.stack(pieces)
            .reshape(time_devices, BAND + 1, series, 2, cols_local)
            .transpose(1, 2, 3, 0, 4)
            .reshape(BAND + 1, series, 2, factor_b)
        )
        column_of = (
            cols_local * ((time_rank - index_b // cols_local) % time_devices) + index_b % cols_local
        )
        cosine_p, sine_p = angles(column_of, index_b, factor_b)
        forward_b = jnp.concatenate(
            [jnp.concatenate([cosine_p, -sine_p], axis=1), jnp.concatenate([sine_p, cosine_p], axis=1)],
            axis=0,
        )
    else:
        cosine_a, sine_a = angles(index_a, index_a, factor_a)
        both_a = jnp.concatenate([cosine_a, -sine_a], axis=0)
        section = matmul(both_a, flat_rows).reshape(2, factor_a, series, cols_local)
        section_real, section_imag = section[0], section[1]
        cosine_t, sine_t = angles(index_a, col_global, SAMPLES)
        twisted_real = section_real * cosine_t[:, None, :] + section_imag * sine_t[:, None, :]
        twisted_imag = section_imag * cosine_t[:, None, :] - section_real * sine_t[:, None, :]
        twisted = jnp.stack([twisted_real, twisted_imag], axis=2)
        moved = lax.all_to_all(twisted, "tm", split_axis=0, concat_axis=3, tiled=True)
        forward_b = jnp.concatenate(
            [jnp.concatenate([cosine_b, -sine_b], axis=1), jnp.concatenate([sine_b, cosine_b], axis=1)],
            axis=0,
        )
    if paired:
        spec = matmul(incoming.reshape((BAND + 1) * series, 2 * factor_b), forward_b).reshape(
            BAND + 1, series, 2, factor_b
        )
        energy = spec[:, :, 0] * spec[:, :, 0] + spec[:, :, 1] * spec[:, :, 1]
        power_low = jnp.mean(energy[:BAND], axis=0)
        power_high = (energy[BAND] + jnp.sum(energy[1:BAND], axis=0)[:, ::-1]) / BAND
        scale_low = lax.rsqrt(power_low + epsilon)
        scale_high = lax.rsqrt(power_high + epsilon)
        scale_row = jnp.stack([scale_low, scale_high[:, ::-1]], axis=1)[None]
        sent = jnp.concatenate(
            [
                spec[:1] * scale_low[None, :, None, :],
                spec[1:BAND],
                spec[BAND:] * scale_high[None, :, None, :],
                scale_row,
            ]
        )
    else:
        spec = matmul(moved.reshape(rows_local * series, 2 * factor_b), forward_b)
        banded = spec.reshape(rows_local // BAND, BAND, series, 2, factor_b)
        band_power = jnp.mean(
            banded[:, :, :, 0] * banded[:, :, :, 0] + banded[:, :, :, 1] * banded[:, :, :, 1],
            axis=1,
            keepdims=True,
        )
        band_scale = lax.rsqrt(band_power + epsilon)
        sent = (banded * band_scale[:, :, :, None]).reshape(rows_local, series, 2, factor_b)
    k1_ids = lax.optimization_barrier((k1_ids, sent))[0]
    arrived = {}
    for distance in range(REACH, 0, -1):
        arrived[distance] = passed_along(sent.reshape(-1, factor_b), "sta", -distance).reshape(sent.shape)
    nearby = jnp.stack([sent] + [arrived[distance] for distance in range(1, REACH + 1)])
    slot_total = pair_blocks.shape[0]
    first_off = pair_blocks[:, 0] - owner_id
    second_off = pair_blocks[:, 1] - owner_id

    def chosen(offsets):
        pick = offsets.reshape((slot_total,) + (1,) * (nearby.ndim - 1))
        result = jnp.broadcast_to(nearby[REACH], (slot_total,) + nearby.shape[1:])
        for distance in range(REACH - 1, -1, -1):
            result = jnp.where(pick == distance, nearby[distance], result)
        return result

    def inverse_of(cosines, sines):
        return jnp.concatenate(
            [jnp.concatenate([cosines, sines], axis=1), jnp.concatenate([-sines, cosines], axis=1)],
            axis=0,
        )

    left_block = chosen(first_off)
    right_block = chosen(second_off)
    if paired:
        kept = BAND + 1
        spec_shape = (slot_total, kept, stations, hour_count, 2, factor_b)
        scale_shape = (slot_total, stations, hour_count, factor_b)
        left_spec = left_block[:, :kept].reshape(spec_shape)
        right_spec = right_block[:, :kept].reshape(spec_shape)

        def weight(left_scale, right_scale):
            return left_scale[:, None, :, None] * right_scale[:, None, None, :]

        left_low = left_block[:, kept, :, 0].reshape(scale_shape)
        left_turned = left_block[:, kept, :, 1].reshape(scale_shape)
        right_low = right_block[:, kept, :, 0].reshape(scale_shape)
        right_turned = right_block[:, kept, :, 1].reshape(scale_shape)
        weight_paired = weight(left_low, right_low) + weight(left_turned, right_turned)
        single = jnp.ones((slot_total, 1) + weight_paired.shape[2:], jnp.float32)
        row_weight = jnp.concatenate(
            [single, jnp.broadcast_to(weight_paired, (slot_total, BAND - 1) + weight_paired.shape[2:]), single],
            axis=1,
        )
    else:
        kept = rows_local
        spec_shape = (slot_total, kept, stations, hour_count, 2, factor_b)
        left_spec = left_block.reshape(spec_shape)
        right_spec = right_block.reshape(spec_shape)
        row_weight = jnp.ones((1, 1, 1, 1, 1, 1), jnp.float32)
    left_real = left_spec[:, :, :, None, :, 0]
    left_imag = left_spec[:, :, :, None, :, 1]
    right_real = right_spec[:, :, None, :, :, 0]
    right_imag = right_spec[:, :, None, :, :, 1]
    cross_real = jnp.sum((left_real * right_real + left_imag * right_imag) * row_weight, axis=4)
    cross_imag = jnp.sum((left_imag * right_real - left_real * right_imag) * row_weight, axis=4)
    cross = jnp.concatenate([cross_real, cross_imag], axis=-1)
    lag = matmul(cross.reshape(-1, 2 * factor_b), inverse_of(cosine_b, sine_b)).reshape(
        slot_total, kept, stations, stations, 2, factor_b
    )
    row_ids = k1_ids[:kept]
    lag_real, lag_imag = lag[:, :, :, :, 0], lag[:, :, :, :, 1]
    cosine_u, sine_u = angles(row_ids, index_b, SAMPLES)
    turn_real = lag_real * cosine_u[None, :, None, None, :] - lag_imag * sine_u[None, :, None, None, :]
    turn_imag = lag_real * sine_u[None, :, None, None, :] + lag_imag * cosine_u[None, :, None, None, :]
    lag_ids = jnp.concatenate(
        [jnp.arange(LAGS, dtype=jnp.int32), factor_a - LAGS + jnp.arange(LAGS, dtype=jnp.int32)]
    )
    cosine_l, sine_l = angles(lag_ids, row_ids, factor_a)
    lag_weights = jnp.concatenate([cosine_l, -sine_l], axis=1).reshape(
        time_devices, 2 * LAGS // time_devices, 2 * kept
    )
    turned = jnp.concatenate([turn_real, turn_imag], axis=1)
    scale_out = 1.0 / math.sqrt(SAMPLES * hour_count)
    live_mask = (jnp.arange(slot_total) < pair_count).astype(jnp.float32) * scale_out
    lag_block = jnp.einsum(
        "dwp,spijm->dsijwm",
        lag_weights,
        turned,
        precision=highest,
        preferred_element_type=jnp.float32,
    )
    lag_block = lag_block * live_mask[None, :, None, None, None, None]
    flat = lag_block.reshape(time_devices, -1)
    dest_ids = lax.broadcasted_iota(jnp.int32, flat.shape, 0)

    def chunk_for(shift):
        mine = dest_ids == (time_rank + shift) % time_devices
        return jnp.sum(jnp.where(mine, flat, 0.0), axis=0)

    out_shape = (slot_total, stations, stations, 2 * LAGS * factor_b // time_devices)
    total = chunk_for(0).reshape(out_shape)
    for shift in range(1, time_devices):
        route = [(i, (i + shift) % time_devices) for i in range(time_devices)]
        total = total + lax.ppermute(chunk_for(shift).reshape(out_shape), "tm", route)
    return total


def solution(mesh):
    placed = (P("sta", None, "tm"), P("sta", None), P("sta"))
    return jax.shard_map(local, mesh=mesh, in_specs=placed, out_specs=P("sta", None, None, "tm"), check_vma=False)
```

```python
import math

import jax
import jax.numpy as jnp
from jax import lax
from jax.sharding import PartitionSpec as P

SAMPLES = 65536
FACTOR_A = 256
BAND = 32
LAGS = 4
REACH = 3


highest = lax.Precision.HIGH
epsilon = 1e-06


def passed_along(block, axis, distance):
    devices = range(lax.axis_size(axis))
    route = [(i - distance, i) for i in devices if i - distance in devices]
    return lax.ppermute(block, axis, route)


def angles(row_ids, col_ids, modulus):
    product = row_ids[:, None] * col_ids[None, :] % modulus
    radians = product.astype(jnp.float32) * (2.0 * math.pi / modulus)
    return (jnp.cos(radians), jnp.sin(radians))


def matmul(left_mat, right_mat):
    return jnp.dot(left_mat, right_mat, precision=highest, preferred_element_type=jnp.float32)


def local(records, pair_blocks, pair_count):
    stations, hour_count, _ = records.shape
    time_devices = lax.axis_size("tm")
    time_rank = lax.axis_index("tm")
    owner_id = lax.axis_index("sta")
    factor_a = FACTOR_A
    factor_b = SAMPLES // FACTOR_A
    rows_local = factor_a // time_devices
    cols_local = factor_b // time_devices
    series = stations * hour_count
    arranged = records.reshape(series, rows_local, time_devices, cols_local).transpose(2, 1, 0, 3)
    index_a = jnp.arange(factor_a, dtype=jnp.int32)
    paired = rows_local == 2 * BAND and factor_a == 2 * BAND * time_devices
    if paired:
        pieces = [lax.dynamic_index_in_dim(arranged, time_rank, 0, keepdims=False)]
        for shift in range(1, time_devices):
            route = [(i, (i + shift) % time_devices) for i in range(time_devices)]
            chunk = lax.dynamic_index_in_dim(arranged, (time_rank + shift) % time_devices, 0, keepdims=False)
            pieces.append(lax.ppermute(chunk, "tm", route))
        spread = jnp.stack(pieces).reshape(factor_a, series, cols_local)
        row_of = rows_local * ((time_rank - index_a // rows_local) % time_devices) + index_a % rows_local
    else:
        spread = lax.all_to_all(
            arranged.reshape(time_devices, -1), "tm", split_axis=0, concat_axis=0, tiled=True
        ).reshape(factor_a, series, cols_local)
    index_b = jnp.arange(factor_b, dtype=jnp.int32)
    if paired:
        k1_ids = jnp.concatenate(
            [
                BAND * time_rank + jnp.arange(BAND, dtype=jnp.int32),
                factor_a - BAND * (time_rank + 1) + jnp.arange(BAND, dtype=jnp.int32),
            ]
        )
    else:
        k1_ids = time_rank * rows_local + jnp.arange(rows_local, dtype=jnp.int32)
    flat_rows = spread.reshape(factor_a, series * cols_local)
    col_global = time_rank * cols_local + jnp.arange(cols_local, dtype=jnp.int32)
    if paired:
        shift_ids = lax.broadcasted_iota(jnp.int32, (time_devices, BAND + 1), 0)
        place_ids = lax.broadcasted_iota(jnp.int32, (time_devices, BAND + 1), 1)
        target = (time_rank + shift_ids) % time_devices
        send_rows = jnp.where(
            place_ids < BAND, BAND * target + place_ids, factor_a - BAND * (target + 1)
        ).reshape(-1)
        cosine_a, sine_a = angles(send_rows, row_of, factor_a)
        section = matmul(jnp.concatenate([cosine_a, -sine_a], axis=0), flat_rows).reshape(
            2, -1, series, cols_local
        )
        cosine_t, sine_t = angles(send_rows, col_global, SAMPLES)
        section_real, section_imag = section[0], section[1]
        twisted_real = section_real * cosine_t[:, None, :] + section_imag * sine_t[:, None, :]
        twisted_imag = section_imag * cosine_t[:, None, :] - section_real * sine_t[:, None, :]
        outgoing = jnp.stack([twisted_real, twisted_imag], axis=2).reshape(time_devices, -1)
        pieces = [outgoing[0]]
        for shift in range(1, time_devices):
            route = [(i, (i + shift) % time_devices) for i in range(time_devices)]
            pieces.append(lax.ppermute(outgoing[shift], "tm", route))
        incoming = (
            jnp.stack(pieces)
            .reshape(time_devices, BAND + 1, series, 2, cols_local)
            .transpose(1, 2, 3, 0, 4)
            .reshape(BAND + 1, series, 2, factor_b)
        )
        column_of = (
            cols_local * ((time_rank - index_b // cols_local) % time_devices) + index_b % cols_local
        )
        column_of = lax.optimization_barrier((column_of, outgoing))[0]
        cosine_p, sine_p = angles(column_of, index_b, factor_b)
        forward_b = jnp.concatenate(
            [jnp.concatenate([cosine_p, -sine_p], axis=1), jnp.concatenate([sine_p, cosine_p], axis=1)],
            axis=0,
        )
    else:
        cosine_b, sine_b = angles(index_b, index_b, factor_b)
        cosine_a, sine_a = angles(index_a, index_a, factor_a)
        both_a = jnp.concatenate([cosine_a, -sine_a], axis=0)
        section = matmul(both_a, flat_rows).reshape(2, factor_a, series, cols_local)
        section_real, section_imag = section[0], section[1]
        cosine_t, sine_t = angles(index_a, col_global, SAMPLES)
        twisted_real = section_real * cosine_t[:, None, :] + section_imag * sine_t[:, None, :]
        twisted_imag = section_imag * cosine_t[:, None, :] - section_real * sine_t[:, None, :]
        twisted = jnp.stack([twisted_real, twisted_imag], axis=2)
        moved = lax.all_to_all(twisted, "tm", split_axis=0, concat_axis=3, tiled=True)
        forward_b = jnp.concatenate(
            [jnp.concatenate([cosine_b, -sine_b], axis=1), jnp.concatenate([sine_b, cosine_b], axis=1)],
            axis=0,
        )
    if paired:
        spec = matmul(incoming.reshape((BAND + 1) * series, 2 * factor_b), forward_b).reshape(
            BAND + 1, series, 2, factor_b
        )
        energy = spec[:, :, 0] * spec[:, :, 0] + spec[:, :, 1] * spec[:, :, 1]
        power_low = jnp.mean(energy[:BAND], axis=0)
        power_high = (energy[BAND] + jnp.sum(energy[1:BAND], axis=0)[:, ::-1]) / BAND
        scale_low = lax.rsqrt(power_low + epsilon)
        scale_high = lax.rsqrt(power_high + epsilon)
        scale_row = jnp.stack([scale_low, scale_high[:, ::-1]], axis=1)[None]
        sent = jnp.concatenate(
            [
                spec[:1] * scale_low[None, :, None, :],
                spec[1:BAND],
                spec[BAND:] * scale_high[None, :, None, :],
                scale_row,
            ]
        )
    else:
        spec = matmul(moved.reshape(rows_local * series, 2 * factor_b), forward_b)
        banded = spec.reshape(rows_local // BAND, BAND, series, 2, factor_b)
        band_power = jnp.mean(
            banded[:, :, :, 0] * banded[:, :, :, 0] + banded[:, :, :, 1] * banded[:, :, :, 1],
            axis=1,
            keepdims=True,
        )
        band_scale = lax.rsqrt(band_power + epsilon)
        sent = (banded * band_scale[:, :, :, None]).reshape(rows_local, series, 2, factor_b)
    k1_ids, late_index = lax.optimization_barrier((k1_ids, index_b, sent))[:2]
    if paired:
        cosine_b, sine_b = angles(late_index, late_index, factor_b)
    arrived = {}
    for distance in range(REACH, 0, -1):
        arrived[distance] = passed_along(sent.reshape(-1, factor_b), "sta", -distance).reshape(sent.shape)
    nearby = jnp.stack([sent] + [arrived[distance] for distance in range(1, REACH + 1)])
    slot_total = pair_blocks.shape[0]
    first_off = pair_blocks[:, 0] - owner_id
    second_off = pair_blocks[:, 1] - owner_id

    def chosen(offsets):
        pick = offsets.reshape((slot_total,) + (1,) * (nearby.ndim - 1))
        result = jnp.broadcast_to(nearby[REACH], (slot_total,) + nearby.shape[1:])
        for distance in range(REACH - 1, -1, -1):
            result = jnp.where(pick == distance, nearby[distance], result)
        return result

    def inverse_of(cosines, sines):
        return jnp.concatenate(
            [jnp.concatenate([cosines, sines], axis=1), jnp.concatenate([-sines, cosines], axis=1)],
            axis=0,
        )

    left_block = chosen(first_off)
    right_block = chosen(second_off)
    if paired:
        kept = BAND + 1
        spec_shape = (slot_total, kept, stations, hour_count, 2, factor_b)
        scale_shape = (slot_total, stations, hour_count, factor_b)
        left_spec = left_block[:, :kept].reshape(spec_shape)
        right_spec = right_block[:, :kept].reshape(spec_shape)

        def weight(left_scale, right_scale):
            return left_scale[:, None, :, None] * right_scale[:, None, None, :]

        left_low = left_block[:, kept, :, 0].reshape(scale_shape)
        left_turned = left_block[:, kept, :, 1].reshape(scale_shape)
        right_low = right_block[:, kept, :, 0].reshape(scale_shape)
        right_turned = right_block[:, kept, :, 1].reshape(scale_shape)
        weight_paired = weight(left_low, right_low) + weight(left_turned, right_turned)
        single = jnp.ones((slot_total, 1) + weight_paired.shape[2:], jnp.float32)
        row_weight = jnp.concatenate(
            [single, jnp.broadcast_to(weight_paired, (slot_total, BAND - 1) + weight_paired.shape[2:]), single],
            axis=1,
        )
    else:
        kept = rows_local
        spec_shape = (slot_total, kept, stations, hour_count, 2, factor_b)
        left_spec = left_block.reshape(spec_shape)
        right_spec = right_block.reshape(spec_shape)
        row_weight = jnp.ones((1, 1, 1, 1, 1, 1), jnp.float32)
    left_real = left_spec[:, :, :, None, :, 0]
    left_imag = left_spec[:, :, :, None, :, 1]
    right_real = right_spec[:, :, None, :, :, 0]
    right_imag = right_spec[:, :, None, :, :, 1]
    cross_real = jnp.sum((left_real * right_real + left_imag * right_imag) * row_weight, axis=4)
    cross_imag = jnp.sum((left_imag * right_real - left_real * right_imag) * row_weight, axis=4)
    cross = jnp.concatenate([cross_real, cross_imag], axis=-1)
    lag = matmul(cross.reshape(-1, 2 * factor_b), inverse_of(cosine_b, sine_b)).reshape(
        slot_total, kept, stations, stations, 2, factor_b
    )
    row_ids = k1_ids[:kept]
    lag_real, lag_imag = lag[:, :, :, :, 0], lag[:, :, :, :, 1]
    cosine_u, sine_u = angles(row_ids, index_b, SAMPLES)
    turn_real = lag_real * cosine_u[None, :, None, None, :] - lag_imag * sine_u[None, :, None, None, :]
    turn_imag = lag_real * sine_u[None, :, None, None, :] + lag_imag * cosine_u[None, :, None, None, :]
    lag_ids = jnp.concatenate(
        [jnp.arange(LAGS, dtype=jnp.int32), factor_a - LAGS + jnp.arange(LAGS, dtype=jnp.int32)]
    )
    cosine_l, sine_l = angles(lag_ids, row_ids, factor_a)
    lag_weights = jnp.concatenate([cosine_l, -sine_l], axis=1).reshape(
        time_devices, 2 * LAGS // time_devices, 2 * kept
    )
    turned = jnp.concatenate([turn_real, turn_imag], axis=1)
    scale_out = 1.0 / math.sqrt(SAMPLES * hour_count)
    live_mask = (jnp.arange(slot_total) < pair_count).astype(jnp.float32) * scale_out
    lag_block = jnp.einsum(
        "dwp,spijm->dsijwm",
        lag_weights,
        turned,
        precision=highest,
        preferred_element_type=jnp.float32,
    )
    lag_block = lag_block * live_mask[None, :, None, None, None, None]
    flat = lag_block.reshape(time_devices, -1)
    dest_ids = lax.broadcasted_iota(jnp.int32, flat.shape, 0)

    def chunk_for(shift):
        mine = dest_ids == (time_rank + shift) % time_devices
        return jnp.sum(jnp.where(mine, flat, 0.0), axis=0)

    total = chunk_for(0)
    for shift in range(1, time_devices):
        route = [(i, (i + shift) % time_devices) for i in range(time_devices)]
        total = total + lax.ppermute(chunk_for(shift), "tm", route)
    return total.reshape(slot_total, stations, stations, 2 * LAGS * factor_b // time_devices)


def solution(mesh):
    placed = (P("sta", None, "tm"), P("sta", None), P("sta"))
    return jax.shard_map(local, mesh=mesh, in_specs=placed, out_specs=P("sta", None, None, "tm"), check_vma=False)
```

```python
import math

import jax
import jax.numpy as jnp
from jax import lax
from jax.sharding import PartitionSpec as P

SAMPLES = 65536
FACTOR_A = 256
BAND = 32
LAGS = 4
REACH = 3


highest = lax.Precision.HIGH
epsilon = 1e-06


def passed_along(block, axis, distance):
    devices = range(lax.axis_size(axis))
    route = [(i - distance, i) for i in devices if i - distance in devices]
    return lax.ppermute(block, axis, route)


def angles(row_ids, col_ids, modulus):
    product = row_ids[:, None] * col_ids[None, :] % modulus
    radians = product.astype(jnp.float32) * (2.0 * math.pi / modulus)
    return (jnp.cos(radians), jnp.sin(radians))


def matmul(left_mat, right_mat):
    return jnp.dot(left_mat, right_mat, precision=highest, preferred_element_type=jnp.float32)


def local(records, pair_blocks, pair_count):
    stations, hour_count, _ = records.shape
    time_devices = lax.axis_size("tm")
    time_rank = lax.axis_index("tm")
    owner_id = lax.axis_index("sta")
    factor_a = FACTOR_A
    factor_b = SAMPLES // FACTOR_A
    rows_local = factor_a // time_devices
    cols_local = factor_b // time_devices
    series = stations * hour_count
    arranged = records.reshape(series, rows_local, time_devices, cols_local).transpose(2, 1, 0, 3)
    index_a = jnp.arange(factor_a, dtype=jnp.int32)
    paired = rows_local == 2 * BAND and factor_a == 2 * BAND * time_devices
    if paired:
        pieces = [lax.dynamic_index_in_dim(arranged, time_rank, 0, keepdims=False)]
        for shift in range(1, time_devices):
            route = [(i, (i + shift) % time_devices) for i in range(time_devices)]
            chunk = lax.dynamic_index_in_dim(arranged, (time_rank + shift) % time_devices, 0, keepdims=False)
            pieces.append(lax.ppermute(chunk, "tm", route))
        spread = jnp.stack(pieces).reshape(factor_a, series, cols_local)
        row_of = rows_local * ((time_rank - index_a // rows_local) % time_devices) + index_a % rows_local
    else:
        spread = lax.all_to_all(
            arranged.reshape(time_devices, -1), "tm", split_axis=0, concat_axis=0, tiled=True
        ).reshape(factor_a, series, cols_local)
    index_b = jnp.arange(factor_b, dtype=jnp.int32)
    if paired:
        k1_ids = jnp.concatenate(
            [
                BAND * time_rank + jnp.arange(BAND, dtype=jnp.int32),
                factor_a - BAND * (time_rank + 1) + jnp.arange(BAND, dtype=jnp.int32),
            ]
        )
    else:
        k1_ids = time_rank * rows_local + jnp.arange(rows_local, dtype=jnp.int32)
    flat_rows = spread.reshape(factor_a, series * cols_local)
    col_global = time_rank * cols_local + jnp.arange(cols_local, dtype=jnp.int32)
    if paired:
        shift_ids = lax.broadcasted_iota(jnp.int32, (time_devices, BAND + 1), 0)
        place_ids = lax.broadcasted_iota(jnp.int32, (time_devices, BAND + 1), 1)
        target = (time_rank + shift_ids) % time_devices
        send_rows = jnp.where(
            place_ids < BAND, BAND * target + place_ids, factor_a - BAND * (target + 1)
        ).reshape(-1)
        cosine_a, sine_a = angles(send_rows, row_of, factor_a)
        section = matmul(jnp.concatenate([cosine_a, -sine_a], axis=0), flat_rows).reshape(
            2, -1, series, cols_local
        )
        cosine_t, sine_t = angles(send_rows, col_global, SAMPLES)
        section_real, section_imag = section[0], section[1]
        twisted_real = section_real * cosine_t[:, None, :] + section_imag * sine_t[:, None, :]
        twisted_imag = section_imag * cosine_t[:, None, :] - section_real * sine_t[:, None, :]
        outgoing = jnp.stack([twisted_real, twisted_imag], axis=2).reshape(time_devices, -1)
        pieces = [outgoing[0]]
        for shift in range(1, time_devices):
            route = [(i, (i + shift) % time_devices) for i in range(time_devices)]
            pieces.append(lax.ppermute(outgoing[shift], "tm", route))
        incoming = (
            jnp.stack(pieces)
            .reshape(time_devices, BAND + 1, series, 2, cols_local)
            .transpose(1, 2, 3, 0, 4)
            .reshape(BAND + 1, series, 2, factor_b)
        )
        column_of = (
            cols_local * ((time_rank - index_b // cols_local) % time_devices) + index_b % cols_local
        )
        column_of = lax.optimization_barrier((column_of, outgoing))[0]
        cosine_p, sine_p = angles(column_of, index_b, factor_b)
        forward_b = jnp.concatenate(
            [jnp.concatenate([cosine_p, -sine_p], axis=1), jnp.concatenate([sine_p, cosine_p], axis=1)],
            axis=0,
        )
    else:
        cosine_b, sine_b = angles(index_b, index_b, factor_b)
        cosine_a, sine_a = angles(index_a, index_a, factor_a)
        both_a = jnp.concatenate([cosine_a, -sine_a], axis=0)
        section = matmul(both_a, flat_rows).reshape(2, factor_a, series, cols_local)
        section_real, section_imag = section[0], section[1]
        cosine_t, sine_t = angles(index_a, col_global, SAMPLES)
        twisted_real = section_real * cosine_t[:, None, :] + section_imag * sine_t[:, None, :]
        twisted_imag = section_imag * cosine_t[:, None, :] - section_real * sine_t[:, None, :]
        twisted = jnp.stack([twisted_real, twisted_imag], axis=2)
        moved = lax.all_to_all(twisted, "tm", split_axis=0, concat_axis=3, tiled=True)
        forward_b = jnp.concatenate(
            [jnp.concatenate([cosine_b, -sine_b], axis=1), jnp.concatenate([sine_b, cosine_b], axis=1)],
            axis=0,
        )
    if paired:
        spec = matmul(incoming.reshape((BAND + 1) * series, 2 * factor_b), forward_b).reshape(
            BAND + 1, series, 2, factor_b
        )
        energy = spec[:, :, 0] * spec[:, :, 0] + spec[:, :, 1] * spec[:, :, 1]
        power_low = jnp.mean(energy[:BAND], axis=0)
        power_high = (energy[BAND] + jnp.sum(energy[1:BAND], axis=0)[:, ::-1]) / BAND
        scale_low = lax.rsqrt(power_low + epsilon)
        scale_high = lax.rsqrt(power_high + epsilon)
        scale_row = jnp.stack([scale_low, scale_high[:, ::-1]], axis=1)[None]
        sent = jnp.concatenate(
            [
                spec[:1] * scale_low[None, :, None, :],
                spec[1:BAND],
                spec[BAND:] * scale_high[None, :, None, :],
                scale_row,
            ]
        )
    else:
        spec = matmul(moved.reshape(rows_local * series, 2 * factor_b), forward_b)
        banded = spec.reshape(rows_local // BAND, BAND, series, 2, factor_b)
        band_power = jnp.mean(
            banded[:, :, :, 0] * banded[:, :, :, 0] + banded[:, :, :, 1] * banded[:, :, :, 1],
            axis=1,
            keepdims=True,
        )
        band_scale = lax.rsqrt(band_power + epsilon)
        sent = (banded * band_scale[:, :, :, None]).reshape(rows_local, series, 2, factor_b)
    k1_ids, late_index = lax.optimization_barrier((k1_ids, index_b, sent))[:2]
    if paired:
        cosine_b, sine_b = angles(late_index, late_index, factor_b)
    arrived = {}
    for distance in range(REACH, 0, -1):
        arrived[distance] = passed_along(sent.reshape(-1, factor_b), "sta", -distance).reshape(sent.shape)
    nearby = jnp.stack([sent] + [arrived[distance] for distance in range(1, REACH + 1)])
    slot_total = pair_blocks.shape[0]
    first_off = pair_blocks[:, 0] - owner_id
    second_off = pair_blocks[:, 1] - owner_id

    def chosen(offsets):
        pick = offsets.reshape((slot_total,) + (1,) * (nearby.ndim - 1))
        result = jnp.broadcast_to(nearby[REACH], (slot_total,) + nearby.shape[1:])
        for distance in range(REACH - 1, -1, -1):
            result = jnp.where(pick == distance, nearby[distance], result)
        return result

    def inverse_of(cosines, sines):
        return jnp.concatenate(
            [jnp.concatenate([cosines, sines], axis=1), jnp.concatenate([-sines, cosines], axis=1)],
            axis=0,
        )

    left_block = chosen(first_off)
    right_block = chosen(second_off)
    if paired:
        kept = BAND + 1
        spec_shape = (slot_total, kept, stations, hour_count, 2, factor_b)
        scale_shape = (slot_total, stations, hour_count, factor_b)
        left_spec = left_block[:, :kept].reshape(spec_shape)
        right_spec = right_block[:, :kept].reshape(spec_shape)

        def weight(left_scale, right_scale):
            return left_scale[:, None, :, None] * right_scale[:, None, None, :]

        left_low = left_block[:, kept, :, 0].reshape(scale_shape)
        left_turned = left_block[:, kept, :, 1].reshape(scale_shape)
        right_low = right_block[:, kept, :, 0].reshape(scale_shape)
        right_turned = right_block[:, kept, :, 1].reshape(scale_shape)
        weight_paired = weight(left_low, right_low) + weight(left_turned, right_turned)
        single = jnp.ones((slot_total, 1) + weight_paired.shape[2:], jnp.float32)
        row_weight = jnp.concatenate(
            [single, jnp.broadcast_to(weight_paired, (slot_total, BAND - 1) + weight_paired.shape[2:]), single],
            axis=1,
        )
    else:
        kept = rows_local
        spec_shape = (slot_total, kept, stations, hour_count, 2, factor_b)
        left_spec = left_block.reshape(spec_shape)
        right_spec = right_block.reshape(spec_shape)
        row_weight = jnp.ones((1, 1, 1, 1, 1, 1), jnp.float32)
    left_real = left_spec[:, :, :, None, :, 0]
    left_imag = left_spec[:, :, :, None, :, 1]
    right_real = right_spec[:, :, None, :, :, 0]
    right_imag = right_spec[:, :, None, :, :, 1]
    cross_real = jnp.sum((left_real * right_real + left_imag * right_imag) * row_weight, axis=4)
    cross_imag = jnp.sum((left_imag * right_real - left_real * right_imag) * row_weight, axis=4)
    cross = jnp.concatenate([cross_real, cross_imag], axis=-1)
    lag = matmul(cross.reshape(-1, 2 * factor_b), inverse_of(cosine_b, sine_b)).reshape(
        slot_total, kept, stations, stations, 2, factor_b
    )
    row_ids = k1_ids[:kept]
    lag_real, lag_imag = lag[:, :, :, :, 0], lag[:, :, :, :, 1]
    cosine_u, sine_u = angles(row_ids, index_b, SAMPLES)
    turn_real = lag_real * cosine_u[None, :, None, None, :] - lag_imag * sine_u[None, :, None, None, :]
    turn_imag = lag_real * sine_u[None, :, None, None, :] + lag_imag * cosine_u[None, :, None, None, :]
    lag_ids = jnp.concatenate(
        [jnp.arange(LAGS, dtype=jnp.int32), factor_a - LAGS + jnp.arange(LAGS, dtype=jnp.int32)]
    )
    cosine_l, sine_l = angles(lag_ids, row_ids, factor_a)
    lag_weights = jnp.concatenate([cosine_l, -sine_l], axis=1).reshape(
        time_devices, 2 * LAGS // time_devices, 2 * kept
    )
    turned = jnp.concatenate([turn_real, turn_imag], axis=1)
    scale_out = 1.0 / math.sqrt(SAMPLES * hour_count)
    live_mask = (jnp.arange(slot_total) < pair_count).astype(jnp.float32) * scale_out
    table_ids = lax.broadcasted_iota(jnp.int32, lag_weights.shape, 0)
    lag_weights = jnp.stack(
        [
            jnp.sum(jnp.where(table_ids == (time_rank + shift) % time_devices, lag_weights, 0.0), axis=0)
            for shift in range(time_devices)
        ]
    )
    lag_block = jnp.einsum(
        "dwp,spijm->dsijwm",
        lag_weights,
        turned,
        precision=highest,
        preferred_element_type=jnp.float32,
    )
    lag_block = lag_block * live_mask[None, :, None, None, None, None]
    flat = lag_block.reshape(time_devices, -1)
    total = flat[0]
    for shift in range(1, time_devices):
        route = [(i, (i + shift) % time_devices) for i in range(time_devices)]
        total = total + lax.ppermute(flat[shift], "tm", route)
    return total.reshape(slot_total, stations, stations, 2 * LAGS * factor_b // time_devices)


def solution(mesh):
    placed = (P("sta", None, "tm"), P("sta", None), P("sta"))
    return jax.shard_map(local, mesh=mesh, in_specs=placed, out_specs=P("sta", None, None, "tm"), check_vma=False)
```

```python
import math

import jax
import jax.numpy as jnp
from jax import lax
from jax.sharding import PartitionSpec as P

SAMPLES = 65536
FACTOR_A = 256
BAND = 32
LAGS = 4
REACH = 3


highest = lax.Precision.HIGH
epsilon = 1e-06


def passed_along(block, axis, distance):
    devices = range(lax.axis_size(axis))
    route = [(i - distance, i) for i in devices if i - distance in devices]
    return lax.ppermute(block, axis, route)


def angles(row_ids, col_ids, modulus):
    product = row_ids[:, None] * col_ids[None, :] % modulus
    radians = product.astype(jnp.float32) * (2.0 * math.pi / modulus)
    return (jnp.cos(radians), jnp.sin(radians))


def matmul(left_mat, right_mat):
    return jnp.dot(left_mat, right_mat, precision=highest, preferred_element_type=jnp.float32)


def local(records, pair_blocks, pair_count):
    stations, hour_count, _ = records.shape
    time_devices = lax.axis_size("tm")
    time_rank = lax.axis_index("tm")
    owner_id = lax.axis_index("sta")
    factor_a = FACTOR_A
    factor_b = SAMPLES // FACTOR_A
    rows_local = factor_a // time_devices
    cols_local = factor_b // time_devices
    series = stations * hour_count
    arranged = records.reshape(series, rows_local, time_devices, cols_local).transpose(2, 1, 0, 3)
    index_a = jnp.arange(factor_a, dtype=jnp.int32)
    paired = rows_local == 2 * BAND and factor_a == 2 * BAND * time_devices
    if paired:
        pieces = [lax.dynamic_index_in_dim(arranged, time_rank, 0, keepdims=False)]
        for shift in range(1, time_devices):
            route = [(i, (i + shift) % time_devices) for i in range(time_devices)]
            chunk = lax.dynamic_index_in_dim(arranged, (time_rank + shift) % time_devices, 0, keepdims=False)
            pieces.append(lax.ppermute(chunk, "tm", route))
        spread = jnp.stack(pieces).reshape(factor_a, series, cols_local)
        row_of = rows_local * ((time_rank - index_a // rows_local) % time_devices) + index_a % rows_local
    else:
        spread = lax.all_to_all(
            arranged.reshape(time_devices, -1), "tm", split_axis=0, concat_axis=0, tiled=True
        ).reshape(factor_a, series, cols_local)
    index_b = jnp.arange(factor_b, dtype=jnp.int32)
    if paired:
        k1_ids = jnp.concatenate(
            [
                BAND * time_rank + jnp.arange(BAND, dtype=jnp.int32),
                factor_a - BAND * (time_rank + 1) + jnp.arange(BAND, dtype=jnp.int32),
            ]
        )
    else:
        k1_ids = time_rank * rows_local + jnp.arange(rows_local, dtype=jnp.int32)
    flat_rows = spread.reshape(factor_a, series * cols_local)
    col_global = time_rank * cols_local + jnp.arange(cols_local, dtype=jnp.int32)
    if paired:
        shift_ids = lax.broadcasted_iota(jnp.int32, (time_devices, BAND + 1), 0)
        place_ids = lax.broadcasted_iota(jnp.int32, (time_devices, BAND + 1), 1)
        target = (time_rank + shift_ids) % time_devices
        send_rows = jnp.where(
            place_ids < BAND, BAND * target + place_ids, factor_a - BAND * (target + 1)
        ).reshape(-1)
        cosine_a, sine_a = angles(send_rows, row_of, factor_a)
        section = matmul(jnp.concatenate([cosine_a, -sine_a], axis=0), flat_rows).reshape(
            2, -1, series, cols_local
        )
        cosine_t, sine_t = angles(send_rows, col_global, SAMPLES)
        section_real, section_imag = section[0], section[1]
        twisted_real = section_real * cosine_t[:, None, :] + section_imag * sine_t[:, None, :]
        twisted_imag = section_imag * cosine_t[:, None, :] - section_real * sine_t[:, None, :]
        outgoing = jnp.stack([twisted_real, twisted_imag], axis=2).reshape(time_devices, -1)
        pieces = [outgoing[0]]
        for shift in range(1, time_devices):
            route = [(i, (i + shift) % time_devices) for i in range(time_devices)]
            pieces.append(lax.ppermute(outgoing[shift], "tm", route))
        incoming = (
            jnp.stack(pieces)
            .reshape(time_devices, BAND + 1, series, 2, cols_local)
            .transpose(1, 2, 3, 0, 4)
            .reshape(BAND + 1, series, 2, factor_b)
        )
        column_of = (
            cols_local * ((time_rank - index_b // cols_local) % time_devices) + index_b % cols_local
        )
        column_of = lax.optimization_barrier((column_of, outgoing))[0]
        cosine_p, sine_p = angles(column_of, index_b, factor_b)
        forward_b = jnp.concatenate(
            [jnp.concatenate([cosine_p, -sine_p], axis=1), jnp.concatenate([sine_p, cosine_p], axis=1)],
            axis=0,
        )
    else:
        cosine_b, sine_b = angles(index_b, index_b, factor_b)
        cosine_a, sine_a = angles(index_a, index_a, factor_a)
        both_a = jnp.concatenate([cosine_a, -sine_a], axis=0)
        section = matmul(both_a, flat_rows).reshape(2, factor_a, series, cols_local)
        section_real, section_imag = section[0], section[1]
        cosine_t, sine_t = angles(index_a, col_global, SAMPLES)
        twisted_real = section_real * cosine_t[:, None, :] + section_imag * sine_t[:, None, :]
        twisted_imag = section_imag * cosine_t[:, None, :] - section_real * sine_t[:, None, :]
        twisted = jnp.stack([twisted_real, twisted_imag], axis=2)
        moved = lax.all_to_all(twisted, "tm", split_axis=0, concat_axis=3, tiled=True)
        forward_b = jnp.concatenate(
            [jnp.concatenate([cosine_b, -sine_b], axis=1), jnp.concatenate([sine_b, cosine_b], axis=1)],
            axis=0,
        )
    if paired:
        spec = matmul(incoming.reshape((BAND + 1) * series, 2 * factor_b), forward_b).reshape(
            BAND + 1, series, 2, factor_b
        )
        energy = spec[:, :, 0] * spec[:, :, 0] + spec[:, :, 1] * spec[:, :, 1]
        power_low = jnp.mean(energy[:BAND], axis=0)
        power_high = (energy[BAND] + jnp.sum(energy[1:BAND], axis=0)[:, ::-1]) / BAND
        scale_low = lax.rsqrt(power_low + epsilon)
        scale_high = lax.rsqrt(power_high + epsilon)
        scale_row = jnp.stack([scale_low, scale_high[:, ::-1]], axis=1)[None]
        sent = jnp.concatenate(
            [
                spec[:1] * scale_low[None, :, None, :],
                spec[1:BAND],
                spec[BAND:] * scale_high[None, :, None, :],
                scale_row,
            ]
        )
    else:
        spec = matmul(moved.reshape(rows_local * series, 2 * factor_b), forward_b)
        banded = spec.reshape(rows_local // BAND, BAND, series, 2, factor_b)
        band_power = jnp.mean(
            banded[:, :, :, 0] * banded[:, :, :, 0] + banded[:, :, :, 1] * banded[:, :, :, 1],
            axis=1,
            keepdims=True,
        )
        band_scale = lax.rsqrt(band_power + epsilon)
        sent = (banded * band_scale[:, :, :, None]).reshape(rows_local, series, 2, factor_b)
    k1_ids, late_index = lax.optimization_barrier((k1_ids, index_b, sent))[:2]
    if paired:
        cosine_b, sine_b = angles(late_index, late_index, factor_b)
    arrived = {}
    for distance in range(REACH, 0, -1):
        arrived[distance] = passed_along(sent.reshape(-1, factor_b), "sta", -distance).reshape(sent.shape)
    nearby = jnp.stack([sent] + [arrived[distance] for distance in range(1, REACH + 1)])
    slot_total = pair_blocks.shape[0]
    first_off = pair_blocks[:, 0] - owner_id
    second_off = pair_blocks[:, 1] - owner_id

    def chosen(offsets):
        pick = offsets.reshape((slot_total,) + (1,) * (nearby.ndim - 1))
        result = jnp.broadcast_to(nearby[REACH], (slot_total,) + nearby.shape[1:])
        for distance in range(REACH - 1, -1, -1):
            result = jnp.where(pick == distance, nearby[distance], result)
        return result

    def inverse_of(cosines, sines):
        return jnp.concatenate(
            [jnp.concatenate([cosines, sines], axis=1), jnp.concatenate([-sines, cosines], axis=1)],
            axis=0,
        )

    left_block = chosen(first_off)
    right_block = chosen(second_off)
    if paired:
        kept = BAND + 1
        spec_shape = (slot_total, kept, stations, hour_count, 2, factor_b)
        scale_shape = (slot_total, stations, hour_count, factor_b)
        left_spec = left_block[:, :kept].reshape(spec_shape)
        right_spec = right_block[:, :kept].reshape(spec_shape)

        def weight(left_scale, right_scale):
            return left_scale[:, None, :, None] * right_scale[:, None, None, :]

        left_low = left_block[:, kept, :, 0].reshape(scale_shape)
        left_turned = left_block[:, kept, :, 1].reshape(scale_shape)
        right_low = right_block[:, kept, :, 0].reshape(scale_shape)
        right_turned = right_block[:, kept, :, 1].reshape(scale_shape)
        weight_paired = weight(left_low, right_low) + weight(left_turned, right_turned)
        single = jnp.ones((slot_total, 1) + weight_paired.shape[2:], jnp.float32)
        row_weight = jnp.concatenate(
            [single, jnp.broadcast_to(weight_paired, (slot_total, BAND - 1) + weight_paired.shape[2:]), single],
            axis=1,
        )
    else:
        kept = rows_local
        spec_shape = (slot_total, kept, stations, hour_count, 2, factor_b)
        left_spec = left_block.reshape(spec_shape)
        right_spec = right_block.reshape(spec_shape)
        row_weight = jnp.ones((1, 1, 1, 1, 1, 1), jnp.float32)
    left_real = left_spec[:, :, :, None, :, 0]
    left_imag = left_spec[:, :, :, None, :, 1]
    right_real = right_spec[:, :, None, :, :, 0]
    right_imag = right_spec[:, :, None, :, :, 1]
    cross_real = jnp.sum((left_real * right_real + left_imag * right_imag) * row_weight, axis=4)
    cross_imag = jnp.sum((left_imag * right_real - left_real * right_imag) * row_weight, axis=4)
    cross = jnp.concatenate([cross_real, cross_imag], axis=-1)
    lag = matmul(cross.reshape(-1, 2 * factor_b), inverse_of(cosine_b, sine_b)).reshape(
        slot_total, kept, stations, stations, 2, factor_b
    )
    row_ids = k1_ids[:kept]
    lag_real, lag_imag = lag[:, :, :, :, 0], lag[:, :, :, :, 1]
    cosine_u, sine_u = angles(row_ids, index_b, SAMPLES)
    turn_real = lag_real * cosine_u[None, :, None, None, :] - lag_imag * sine_u[None, :, None, None, :]
    turn_imag = lag_real * sine_u[None, :, None, None, :] + lag_imag * cosine_u[None, :, None, None, :]
    lag_ids = jnp.concatenate(
        [jnp.arange(LAGS, dtype=jnp.int32), factor_a - LAGS + jnp.arange(LAGS, dtype=jnp.int32)]
    )
    cosine_l, sine_l = angles(lag_ids, row_ids, factor_a)
    lag_weights = jnp.concatenate([cosine_l, -sine_l], axis=1).reshape(
        time_devices, 2 * LAGS // time_devices, 2 * kept
    )
    turned = jnp.concatenate([turn_real, turn_imag], axis=1)
    scale_out = 1.0 / math.sqrt(SAMPLES * hour_count)
    live_mask = (jnp.arange(slot_total) < pair_count).astype(jnp.float32) * scale_out
    table_ids = lax.broadcasted_iota(jnp.int32, lag_weights.shape, 0)
    lag_weights = jnp.stack(
        [
            jnp.sum(jnp.where(table_ids == (time_rank + shift) % time_devices, lag_weights, 0.0), axis=0)
            for shift in range(time_devices)
        ]
    )
    lag_block = jnp.einsum(
        "dwp,spijm->dsijwm",
        lag_weights,
        turned,
        precision=highest,
        preferred_element_type=jnp.float32,
    )
    lag_block = lag_block * live_mask[None, :, None, None, None, None]
    out_shape = (slot_total, stations, stations, 2 * LAGS * factor_b // time_devices)
    total = lag_block[0].reshape(out_shape)
    for shift in range(1, time_devices):
        route = [(i, (i + shift) % time_devices) for i in range(time_devices)]
        total = total + lax.ppermute(lag_block[shift].reshape(out_shape), "tm", route)
    return total


def solution(mesh):
    placed = (P("sta", None, "tm"), P("sta", None), P("sta"))
    return jax.shard_map(local, mesh=mesh, in_specs=placed, out_specs=P("sta", None, None, "tm"), check_vma=False)
```
